32 devices in a mesh: ctx: 8 (over z, y), head: 4 (over x, core).
Axes of the slice: x: 2, y: 2, z: 4, core: 2. Of those that a mesh axis runs over, the one named last changes fastest.
Arguments:
- soft_q: bfloat16 [2048, 2048], P('ctx', 'head'), may hold values from -8 to 8
- soft_k: bfloat16 [2048, 2048], P('ctx', 'head'), may hold values from -8 to 8
- soft_v: bfloat16 [2048, 2048], P('ctx', 'head'), may hold values from -16 to 16
- soft_dout: bfloat16 [2048, 2048], P('ctx', 'head'), may hold values from -12 to 12
- lin_q: bfloat16 [2048, 2048], P('ctx', 'head'), may hold values from -12 to 12
- lin_k: bfloat16 [2048, 2048], P('ctx', 'head'), may hold values from -6 to 6
- lin_v: bfloat16 [2048, 2048], P('ctx', 'head'), may hold values from -24 to 24
- lin_gate: float32 [16, 2048], P('head', 'ctx'), may hold values from -1.2 to 0
- lin_dy: bfloat16 [2048, 2048], P('ctx', 'head'), may hold values from -6 to 6
Outputs:
- soft_dq: bfloat16 [2048, 2048], P('ctx', 'head')
- soft_dk: bfloat16 [2048, 2048], P('ctx', 'head')
- soft_dv: bfloat16 [2048, 2048], P('ctx', 'head')
- lin_dq: bfloat16 [2048, 2048], P('ctx', 'head')
- lin_dk: bfloat16 [2048, 2048], P('ctx', 'head')
- lin_dv: bfloat16 [2048, 2048], P('ctx', 'head')
The draws below stay inside these ranges and needn't reach their ends.
All inputs are finite; a program needn't handle non-finite values.
Results may differ from the reference program's by a relative error of at most 0.0073.
Values may be sent and summed in bfloat16 or wider, within the bound.
No kernel may reach another device: no remote copies, remote signals or barrier semaphores. Data moves between devices by JAX's collectives and lax.ppermute only.
A program may use at most 64 MiB of HBM per device.

```python
import math
import jax
import jax.numpy as jnp
from jax import lax

TOK_DEV = 256
LOCAL_HEADS = 16
HEAD_DIM = 128
WIDTH = 2048
SEQUENCE_TOKENS = 2048


def drawn_pair(key):
    base_key = jax.random.fold_in(key, 11)
    first_key, second_key = jax.random.split(base_key, 2)
    full_shape = (SEQUENCE_TOKENS, LOCAL_HEADS, HEAD_DIM)
    queries = jnp.clip(jax.random.normal(first_key, full_shape, jnp.float32), -4.0, 4.0)
    key_rows = jnp.clip(jax.random.normal(second_key, full_shape, jnp.float32), -4.0, 4.0)
    return (queries.reshape(SEQUENCE_TOKENS, WIDTH), key_rows.reshape(SEQUENCE_TOKENS, WIDTH))


def draw_soft_q(key, part):
    return drawn_pair(key)[0].astype(jnp.bfloat16)


def draw_soft_k(key, part):
    return drawn_pair(key)[1].astype(jnp.bfloat16)


def draw_lin_q(key, part):
    base_key = jax.random.fold_in(key, 21)
    value_key, scale_key = jax.random.split(base_key, 2)
    values = jnp.clip(jax.random.normal(value_key, (SEQUENCE_TOKENS, WIDTH), jnp.float32), -4.0, 4.0)
    row_scale = jnp.exp(jax.random.uniform(scale_key, (SEQUENCE_TOKENS, 1), jnp.float32, math.log(0.3), math.log(3.0)))
    return (values * row_scale).astype(jnp.bfloat16)


def draw_lin_v(key, part):
    base_key = jax.random.fold_in(key, 41)
    value_key, scale_key = jax.random.split(base_key, 2)
    values = jnp.clip(jax.random.normal(value_key, (SEQUENCE_TOKENS, WIDTH), jnp.float32), -4.0, 4.0)
    col_scale = jnp.exp(jax.random.uniform(scale_key, (1, WIDTH), jnp.float32, math.log(0.3), math.log(3.0)))
    head_rank = (jnp.arange(WIDTH) // HEAD_DIM).astype(jnp.float32)
    rising = jnp.power(3.0, 0.5 * head_rank / (LOCAL_HEADS - 1))[None, :]
    return (values * col_scale * rising).astype(jnp.bfloat16)


def draw_lin_gate(key, part):
    base_key = jax.random.fold_in(key, 31)
    order_key, device_key, token_key, location_random_key, depth_random_key = jax.random.split(base_key, 5)
    ranks = jax.random.permutation(order_key, LOCAL_HEADS)
    keep_count = LOCAL_HEADS // 2
    slow_heads = ranks < keep_count
    decay_rates = jnp.where(slow_heads, 0.2 * math.log(10.0) / SEQUENCE_TOKENS, math.log(10.0) / 40.0)[:, None]
    device_multiplier = jax.random.uniform(device_key, (LOCAL_HEADS, SEQUENCE_TOKENS // TOK_DEV), jnp.float32, 0.5, 1.5)
    device_multiplier = jnp.repeat(device_multiplier, TOK_DEV, axis=1)
    token_multiplier = jax.random.uniform(token_key, (LOCAL_HEADS, SEQUENCE_TOKENS), jnp.float32, 0.5, 1.5)
    spike_location = jax.random.randint(location_random_key, (LOCAL_HEADS, 2, 1), 0, SEQUENCE_TOKENS)
    spike_depth = jnp.log(jax.random.uniform(depth_random_key, (LOCAL_HEADS, 2, 1), jnp.float32, 0.6, 0.8))
    spike_events = jnp.sum(jnp.where(jnp.arange(SEQUENCE_TOKENS)[None, None, :] == spike_location, spike_depth, 0.0), axis=1)
    return -decay_rates * device_multiplier * token_multiplier + spike_events


def shard_levels(key, shape, shards, low, top_value):
    loudness = 1.0
    for dim, parts in shards:
        draws = jax.random.uniform(jax.random.fold_in(jax.random.fold_in(key, 6), dim), (parts,), jnp.float32, low / len(shards), top_value / len(shards))
        loudness = loudness * jnp.repeat(jnp.exp(draws), shape[dim] // parts).reshape((-1,) + (1,) * (len(shape) - 1 - dim))
    return loudness


def centred(rng, dims, width, reach, cuts=(), held_as=jnp.bfloat16):
    values = width * jax.random.normal(rng, dims, jnp.float32)
    if cuts:
        values = values * shard_levels(rng, dims, cuts, -0.22, 0.18)
    return jnp.clip(values, -reach, reach).astype(held_as)


def setup_inputs(seed: int = 0) -> dict:
    streams_of = jax.random.split(jax.random.key(seed), 10)
    return {
        "soft_q": draw_soft_q(jax.random.fold_in(streams_of[9], 71), 0),
        "soft_k": draw_soft_k(jax.random.fold_in(streams_of[9], 71), 0),
        "soft_v": centred(streams_of[2], (SEQUENCE_TOKENS, WIDTH), 4.0, 16.0, ((0, 8), (1, 4))),
        "soft_dout": centred(streams_of[3], (SEQUENCE_TOKENS, WIDTH), 2.0, 12.0, ((0, 8), (1, 4))),
        "lin_q": draw_lin_q(jax.random.fold_in(streams_of[9], 71), 0),
        "lin_k": centred(streams_of[5], (SEQUENCE_TOKENS, WIDTH), 1.0, 6.0, ((0, 8), (1, 4))),
        "lin_v": draw_lin_v(jax.random.fold_in(streams_of[9], 71), 0),
        "lin_gate": draw_lin_gate(jax.random.fold_in(streams_of[9], 71), 0),
        "lin_dy": centred(streams_of[8], (SEQUENCE_TOKENS, WIDTH), 1.0, 6.0, ((0, 8), (1, 4))),
    }


masked_fill = -1e+30
exact_mode = lax.Precision.HIGHEST

def round_half(array):
    return lax.optimization_barrier(array.astype(jnp.bfloat16)).astype(jnp.float32)

def linear_parts(gates):
    running = jnp.cumsum(gates, axis=1)
    block_total = running[:, -1]
    length = gates.shape[1]
    row_ids = lax.broadcasted_iota(jnp.int32, (length, length), 0)
    col_ids = lax.broadcasted_iota(jnp.int32, (length, length), 1)
    lower = (col_ids <= row_ids)[None]
    spread = jnp.where(lower, running[:, :, None] - running[:, None, :], 0.0)
    window_weight = jnp.where(lower, jnp.exp(spread), 0.0)
    tail_weight = jnp.exp(block_total[:, None] - running)
    return (jnp.exp(running), jnp.exp(block_total), tail_weight, window_weight)

def reference(soft_q, soft_k, soft_v, soft_dout, lin_q, lin_k, lin_v, lin_gate, lin_dy):
    blocks = SEQUENCE_TOKENS // TOK_DEV
    factor = HEAD_DIM ** (-0.5)

    def split_blocks(array):
        return array.reshape(blocks, TOK_DEV, LOCAL_HEADS, HEAD_DIM)

    def softmax_block(carry, inputs):
        queries, keys_own, values_own, grad_out, keys_prev, values_prev, prev_flag = inputs
        query_f = queries.astype(jnp.float32)
        key_own_f = keys_own.astype(jnp.float32)
        value_own_f = values_own.astype(jnp.float32)
        grad_f = grad_out.astype(jnp.float32)
        key_prev_f = keys_prev.astype(jnp.float32)
        value_prev_f = values_prev.astype(jnp.float32)
        row_ids = lax.broadcasted_iota(jnp.int32, (TOK_DEV, TOK_DEV), 0)
        col_ids = lax.broadcasted_iota(jnp.int32, (TOK_DEV, TOK_DEV), 1)
        own_mask = (col_ids <= row_ids)[None]
        prev_mask = ((col_ids > row_ids) & prev_flag)[None]
        scores_own = jnp.einsum('thd,shd->hts', query_f, key_own_f) * factor
        scores_prev = jnp.einsum('thd,shd->hts', query_f, key_prev_f) * factor
        row_max = jnp.maximum(lax.optimization_barrier(jnp.max(jnp.where(own_mask, scores_own, masked_fill), axis=2)), lax.optimization_barrier(jnp.max(jnp.where(prev_mask, scores_prev, masked_fill), axis=2)))
        total = lax.optimization_barrier(jnp.sum(jnp.where(own_mask, jnp.exp(scores_own - row_max[..., None]), 0.0), axis=2))
        total = total + lax.optimization_barrier(jnp.sum(jnp.where(prev_mask, jnp.exp(scores_prev - row_max[..., None]), 0.0), axis=2))
        log_total = row_max + jnp.log(total)
        probs_own = jnp.where(own_mask, jnp.exp(scores_own - log_total[..., None]), 0.0)
        probs_prev = jnp.where(prev_mask, jnp.exp(scores_prev - log_total[..., None]), 0.0)
        dprob_own = jnp.einsum('thd,shd->hts', grad_f, value_own_f)
        dprob_prev = jnp.einsum('thd,shd->hts', grad_f, value_prev_f)
        row_delta = lax.optimization_barrier(jnp.sum(probs_own * dprob_own, axis=2)) + lax.optimization_barrier(jnp.sum(probs_prev * dprob_prev, axis=2))
        dscore_own = round_half(probs_own * (dprob_own - row_delta[..., None]))
        dscore_prev = round_half(probs_prev * (dprob_prev - row_delta[..., None]))
        grad_q = (jnp.einsum('hts,shd->thd', dscore_own, key_own_f) + jnp.einsum('hts,shd->thd', dscore_prev, key_prev_f)) * factor
        grad_k_own = jnp.einsum('hts,thd->shd', dscore_own, query_f) * factor
        grad_v_own = jnp.einsum('hts,thd->shd', round_half(probs_own), grad_f)
        grad_k_cross = jnp.einsum('hts,thd->shd', dscore_prev, query_f) * factor
        grad_v_cross = jnp.einsum('hts,thd->shd', round_half(probs_prev), grad_f)
        outputs = (grad_q.astype(jnp.bfloat16), (grad_k_own + carry[0]).astype(jnp.bfloat16), (grad_v_own + carry[1]).astype(jnp.bfloat16))
        return ((grad_k_cross, grad_v_cross), outputs)
    key_blocks = split_blocks(soft_k)
    value_blocks = split_blocks(soft_v)
    zero_block = jnp.zeros((1, TOK_DEV, LOCAL_HEADS, HEAD_DIM), soft_k.dtype)
    keys_prev = jnp.concatenate([zero_block, key_blocks[:-1]], axis=0)
    values_prev = jnp.concatenate([zero_block, value_blocks[:-1]], axis=0)
    prev_flags = jnp.arange(blocks) > 0
    start = (jnp.zeros((TOK_DEV, LOCAL_HEADS, HEAD_DIM), jnp.float32), jnp.zeros((TOK_DEV, LOCAL_HEADS, HEAD_DIM), jnp.float32))
    unused, soft_grads = lax.scan(softmax_block, start, (split_blocks(soft_q), key_blocks, value_blocks, split_blocks(soft_dout), keys_prev, values_prev, prev_flags), reverse=True)

    def linear_forward(state, inputs):
        queries, keys, values, gates = inputs
        query_f = queries.astype(jnp.float32)
        key_f = keys.astype(jnp.float32)
        value_f = values.astype(jnp.float32)
        lead_weight, block_decay, tail_weight, window_weight = linear_parts(gates)
        attended = round_half(jnp.einsum('thd,shd->hts', query_f, key_f, precision=exact_mode) * factor * window_weight)
        output = jnp.einsum('hts,she->the', attended, value_f, precision=exact_mode)
        output = output + factor * lead_weight.T[:, :, None] * jnp.einsum('thd,hde->the', query_f, state, precision=exact_mode)
        summary = jnp.einsum('hs,shd,she->hde', tail_weight, key_f, value_f, precision=exact_mode)
        return (block_decay[:, None, None] * state + summary, (output, state))

    def linear_backward(carry, inputs):
        queries, keys, values, gates, grads, state_in = inputs
        query_f = queries.astype(jnp.float32)
        key_f = keys.astype(jnp.float32)
        value_f = values.astype(jnp.float32)
        lead_weight, block_decay, tail_weight, window_weight = linear_parts(gates)
        attended = round_half(jnp.einsum('thd,shd->hts', query_f, key_f, precision=exact_mode) * factor * window_weight)
        grad_scores = round_half(jnp.einsum('the,she->hts', grads, value_f, precision=exact_mode) * factor * window_weight)
        grad_q = jnp.einsum('hts,shd->thd', grad_scores, key_f, precision=exact_mode)
        grad_q = grad_q + factor * lead_weight.T[:, :, None] * jnp.einsum('hde,the->thd', state_in, grads, precision=exact_mode)
        grad_k = jnp.einsum('hts,thd->shd', grad_scores, query_f, precision=exact_mode)
        grad_k = grad_k + tail_weight.T[:, :, None] * jnp.einsum('hde,she->shd', carry, value_f, precision=exact_mode)
        grad_v = jnp.einsum('hts,the->she', attended, grads, precision=exact_mode)
        grad_v = grad_v + tail_weight.T[:, :, None] * jnp.einsum('hde,shd->she', carry, key_f, precision=exact_mode)
        grad_summary = factor * jnp.einsum('ht,thd,the->hde', lead_weight, query_f, grads, precision=exact_mode)
        outputs = (grad_q.astype(jnp.bfloat16), grad_k.astype(jnp.bfloat16), grad_v.astype(jnp.bfloat16))
        return (grad_summary + block_decay[:, None, None] * carry, outputs)
    gate_blocks = lin_gate.reshape(LOCAL_HEADS, blocks, TOK_DEV).transpose(1, 0, 2)
    lin_blocks = (split_blocks(lin_q), split_blocks(lin_k), split_blocks(lin_v))
    state_zero = jnp.zeros((LOCAL_HEADS, HEAD_DIM, HEAD_DIM), jnp.float32)
    unused, (lin_out, states_in) = lax.scan(linear_forward, state_zero, lin_blocks + (gate_blocks,))
    dy_f = split_blocks(lin_dy).astype(jnp.float32)
    sum_sq = lax.optimization_barrier(jnp.sum(lin_out * lin_out, axis=(2, 3)))
    sum_dot = lax.optimization_barrier(jnp.sum(lin_out * dy_f, axis=(2, 3)))
    rms = jnp.sqrt(sum_sq / (LOCAL_HEADS * HEAD_DIM) + 1e-06)
    lin_do = dy_f / rms[..., None, None] - lin_out * (sum_dot / (rms ** 3 * (LOCAL_HEADS * HEAD_DIM)))[..., None, None]
    lin_do = round_half(lin_do)
    unused, lin_grads = lax.scan(linear_backward, state_zero, lin_blocks + (gate_blocks, lin_do, states_in), reverse=True)
    shape_out = (SEQUENCE_TOKENS, LOCAL_HEADS * HEAD_DIM)
    return (soft_grads[0].reshape(shape_out), soft_grads[1].reshape(shape_out), soft_grads[2].reshape(shape_out), lin_grads[0].reshape(shape_out), lin_grads[1].reshape(shape_out), lin_grads[2].reshape(shape_out))
```

```python
import jax
import jax.numpy as jnp
from jax import lax
from jax.sharding import PartitionSpec as P

LOCAL_HEADS = 16
HEAD_DIM = 128


masked_fill = -1e30
exact_mode = lax.Precision.HIGHEST


def shifted(x, axis, by):
    peers = lax.axis_size(axis)
    pairs = [(i, i + by) for i in range(peers) if 0 <= i + by < peers]
    return lax.ppermute(x, axis, pairs)


def exclusive_scan(decay, value, axis, reverse):
    count = lax.axis_size(axis)
    place = lax.axis_index(axis)
    win_decay, win_value = decay, value
    res_decay = jnp.ones_like(decay)
    res_value = jnp.zeros_like(value)
    step = 1
    while step < count:
        got_decay, got_value = shifted((win_decay, win_value), axis, -step if reverse else step)
        valid = (place + step < count) if reverse else (place >= step)
        got_decay = jnp.where(valid, got_decay, 1.0)
        res_value = res_value + res_decay[:, None, None] * got_value
        win_value = win_value + win_decay[:, None, None] * got_value
        res_decay = res_decay * got_decay
        win_decay = win_decay * got_decay
        step *= 2
    return res_value


def linear_parts(gates):
    running = jnp.cumsum(gates, axis=1)
    block_total = running[:, -1]
    length = gates.shape[1]
    row_ids = lax.broadcasted_iota(jnp.int32, (length, length), 0)
    col_ids = lax.broadcasted_iota(jnp.int32, (length, length), 1)
    lower = (col_ids <= row_ids)[None]
    spread = jnp.where(lower, running[:, :, None] - running[:, None, :], 0.0)
    window_weight = jnp.where(lower, jnp.exp(spread), 0.0)
    tail_weight = jnp.exp(block_total[:, None] - running)
    return (jnp.exp(running), jnp.exp(block_total), tail_weight, window_weight)


def body(soft_q, soft_k, soft_v, soft_dout, lin_q, lin_k, lin_v, lin_gate, lin_dy):
    heads_here = lin_gate.shape[0]
    length = soft_q.shape[0]
    head_size = soft_q.shape[1] // heads_here
    factor = head_size ** (-0.5)
    position = lax.axis_index("ctx")
    has_prev = position > 0
    has_next = position < lax.axis_size("ctx") - 1
    shape_heads = (length, heads_here, head_size)
    shape_flat = (length, heads_here * head_size)

    lin_queries = lin_q.reshape(shape_heads)
    lin_keys = lin_k.reshape(shape_heads)
    lin_values = lin_v.reshape(shape_heads)
    query_f = lin_queries.astype(jnp.float32)
    key_f = lin_keys.astype(jnp.float32)
    value_f = lin_values.astype(jnp.float32)
    lead_weight, block_decay, tail_weight, window_weight = linear_parts(lin_gate)
    summary = jnp.einsum("hs,shd,she->hde", tail_weight, key_f, value_f, precision=exact_mode)
    state_in = exclusive_scan(block_decay, summary, "ctx", False)

    queries = soft_q.reshape(shape_heads)
    keys_own = soft_k.reshape(shape_heads)
    values_own = soft_v.reshape(shape_heads)
    grad_out = soft_dout.reshape(shape_heads)
    pair_prev = shifted(jnp.stack((soft_k, soft_v)), "ctx", 1)
    pair_next = shifted(jnp.stack((soft_q, soft_dout)), "ctx", -1)
    keys_prev = pair_prev[0].reshape(shape_heads)
    values_prev = pair_prev[1].reshape(shape_heads)
    queries_next = pair_next[0].reshape(shape_heads)
    grad_out_next = pair_next[1].reshape(shape_heads)
    row_ids = lax.broadcasted_iota(jnp.int32, (length, length), 0)
    col_ids = lax.broadcasted_iota(jnp.int32, (length, length), 1)
    own_mask = (col_ids <= row_ids)[None]
    prev_mask = ((col_ids > row_ids) & has_prev)[None]
    next_mask = ((col_ids > row_ids) & has_next)[None]
    scores_own = (
        jnp.einsum("thd,shd->hts", queries, keys_own, preferred_element_type=jnp.float32) * factor
    )
    scores_prev = (
        jnp.einsum("thd,shd->hts", queries, keys_prev, preferred_element_type=jnp.float32) * factor
    )
    row_max = jnp.maximum(
        jnp.max(jnp.where(own_mask, scores_own, masked_fill), axis=2),
        jnp.max(jnp.where(prev_mask, scores_prev, masked_fill), axis=2),
    )
    total = jnp.sum(jnp.where(own_mask, jnp.exp(scores_own - row_max[..., None]), 0.0), axis=2)
    total = total + jnp.sum(
        jnp.where(prev_mask, jnp.exp(scores_prev - row_max[..., None]), 0.0), axis=2
    )
    log_total = row_max + jnp.log(total)
    probs_own = jnp.where(own_mask, jnp.exp(scores_own - log_total[..., None]), 0.0)
    probs_prev = jnp.where(prev_mask, jnp.exp(scores_prev - log_total[..., None]), 0.0)
    dprob_own = jnp.einsum("thd,shd->hts", grad_out, values_own, preferred_element_type=jnp.float32)
    dprob_prev = jnp.einsum(
        "thd,shd->hts", grad_out, values_prev, preferred_element_type=jnp.float32
    )
    row_delta = jnp.sum(probs_own * dprob_own, axis=2) + jnp.sum(probs_prev * dprob_prev, axis=2)
    stats_next = shifted(jnp.stack((log_total, row_delta)), "ctx", -1)
    dscore_own = (probs_own * (dprob_own - row_delta[..., None])).astype(jnp.bfloat16)
    dscore_prev = (probs_prev * (dprob_prev - row_delta[..., None])).astype(jnp.bfloat16)
    grad_q = (
        jnp.einsum("hts,shd->thd", dscore_own, keys_own, preferred_element_type=jnp.float32)
        + jnp.einsum("hts,shd->thd", dscore_prev, keys_prev, preferred_element_type=jnp.float32)
    ) * factor
    grad_k = (
        jnp.einsum("hts,thd->shd", dscore_own, queries, preferred_element_type=jnp.float32) * factor
    )
    grad_v = jnp.einsum(
        "hts,thd->shd", probs_own.astype(jnp.bfloat16), grad_out, preferred_element_type=jnp.float32
    )
    scores_next = (
        jnp.einsum("thd,shd->hts", queries_next, keys_own, preferred_element_type=jnp.float32)
        * factor
    )
    probs_next = jnp.where(next_mask, jnp.exp(scores_next - stats_next[0][..., None]), 0.0)
    dprob_next = jnp.einsum(
        "thd,shd->hts", grad_out_next, values_own, preferred_element_type=jnp.float32
    )
    dscore_next = (probs_next * (dprob_next - stats_next[1][..., None])).astype(jnp.bfloat16)
    grad_k = grad_k + (
        jnp.einsum("hts,thd->shd", dscore_next, queries_next, preferred_element_type=jnp.float32)
        * factor
    )
    grad_v = grad_v + jnp.einsum(
        "hts,thd->shd",
        probs_next.astype(jnp.bfloat16),
        grad_out_next,
        preferred_element_type=jnp.float32,
    )

    lin_scores = jnp.einsum(
        "thd,shd->hts", lin_queries, lin_keys, preferred_element_type=jnp.float32
    )
    attended = (lin_scores * factor * window_weight).astype(jnp.bfloat16)
    lin_output = jnp.einsum(
        "hts,she->the", attended, lin_values, preferred_element_type=jnp.float32
    )
    lin_output = lin_output + factor * lead_weight.T[:, :, None] * jnp.einsum(
        "thd,hde->the", query_f, state_in, precision=exact_mode
    )
    dy_f = lin_dy.reshape(shape_heads).astype(jnp.float32)
    norm_sums = lax.psum(
        (jnp.sum(lin_output * lin_output, axis=(1, 2)), jnp.sum(lin_output * dy_f, axis=(1, 2))),
        "head",
    )
    width_all = LOCAL_HEADS * HEAD_DIM
    rms_value = jnp.sqrt(norm_sums[0] / width_all + 1e-06)
    lin_grad = (
        dy_f / rms_value[:, None, None]
        - lin_output * (norm_sums[1] / (rms_value**3 * width_all))[:, None, None]
    )
    lin_grad_b = lin_grad.astype(jnp.bfloat16)
    lin_grad_f = lin_grad_b.astype(jnp.float32)
    grad_summary = factor * jnp.einsum(
        "ht,thd,the->hde", lead_weight, query_f, lin_grad_f, precision=exact_mode
    )
    grad_in = exclusive_scan(block_decay, grad_summary, "ctx", True)
    grad_raw = jnp.einsum(
        "the,she->hts", lin_grad_b, lin_values, preferred_element_type=jnp.float32
    )
    grad_scores = (grad_raw * factor * window_weight).astype(jnp.bfloat16)
    lin_grad_q = jnp.einsum(
        "hts,shd->thd", grad_scores, lin_keys, preferred_element_type=jnp.float32
    )
    lin_grad_q = lin_grad_q + factor * lead_weight.T[:, :, None] * jnp.einsum(
        "hde,the->thd", state_in, lin_grad_f, precision=exact_mode
    )
    lin_grad_k = jnp.einsum(
        "hts,thd->shd", grad_scores, lin_queries, preferred_element_type=jnp.float32
    )
    lin_grad_k = lin_grad_k + tail_weight.T[:, :, None] * jnp.einsum(
        "hde,she->shd", grad_in, value_f, precision=exact_mode
    )
    lin_grad_v = jnp.einsum(
        "hts,the->she", attended, lin_grad_b, preferred_element_type=jnp.float32
    )
    lin_grad_v = lin_grad_v + tail_weight.T[:, :, None] * jnp.einsum(
        "hde,shd->she", grad_in, key_f, precision=exact_mode
    )
    return (
        grad_q.astype(jnp.bfloat16).reshape(shape_flat),
        grad_k.astype(jnp.bfloat16).reshape(shape_flat),
        grad_v.astype(jnp.bfloat16).reshape(shape_flat),
        lin_grad_q.astype(jnp.bfloat16).reshape(shape_flat),
        lin_grad_k.astype(jnp.bfloat16).reshape(shape_flat),
        lin_grad_v.astype(jnp.bfloat16).reshape(shape_flat),
    )


def solution(mesh):
    in_specs = (
        P("ctx", "head"),
        P("ctx", "head"),
        P("ctx", "head"),
        P("ctx", "head"),
        P("ctx", "head"),
        P("ctx", "head"),
        P("ctx", "head"),
        P("head", "ctx"),
        P("ctx", "head"),
    )
    out_specs = (
        P("ctx", "head"),
        P("ctx", "head"),
        P("ctx", "head"),
        P("ctx", "head"),
        P("ctx", "head"),
        P("ctx", "head"),
    )
    return jax.shard_map(body, mesh=mesh, in_specs=in_specs, out_specs=out_specs, check_vma=False)
```

```python
import jax
import jax.numpy as jnp
from jax import lax
from jax.sharding import PartitionSpec as P

LOCAL_HEADS = 16
HEAD_DIM = 128


masked_fill = -1e30
exact_mode = lax.Precision.HIGHEST


def shifted(x, axis, by):
    peers = lax.axis_size(axis)
    pairs = [(i, i + by) for i in range(peers) if 0 <= i + by < peers]
    return lax.ppermute(x, axis, pairs)


def exclusive_scan(decay, value, axis, reverse):
    count = lax.axis_size(axis)
    heads, size = value.shape[0], value.shape[1]
    rows = lax.broadcasted_iota(jnp.int32, (heads, size + 8, value.shape[2]), 1)
    top = rows < size
    window = jnp.concatenate(
        [value, jnp.broadcast_to(decay[:, None, None], (heads, 8, value.shape[2]))], axis=1
    )
    result = jnp.where(top, 0.0, 1.0)
    step = 1
    while step < count:
        got = shifted(window, axis, -step if reverse else step)
        result = jnp.where(top, result + result[:, size:size + 1, :1] * got, result * got)
        window = jnp.where(top, window + window[:, size:size + 1, :1] * got, window * got)
        step *= 2
    return result[:, :size]


def linear_parts(gates):
    running = jnp.cumsum(gates, axis=1)
    block_total = running[:, -1]
    length = gates.shape[1]
    row_ids = lax.broadcasted_iota(jnp.int32, (length, length), 0)
    col_ids = lax.broadcasted_iota(jnp.int32, (length, length), 1)
    lower = (col_ids <= row_ids)[None]
    spread = jnp.where(lower, running[:, :, None] - running[:, None, :], 0.0)
    window_weight = jnp.where(lower, jnp.exp(spread), 0.0)
    tail_weight = jnp.exp(block_total[:, None] - running)
    return (jnp.exp(running), jnp.exp(block_total), tail_weight, window_weight)


def body(soft_q, soft_k, soft_v, soft_dout, lin_q, lin_k, lin_v, lin_gate, lin_dy):
    heads_here = lin_gate.shape[0]
    length = soft_q.shape[0]
    head_size = soft_q.shape[1] // heads_here
    factor = head_size ** (-0.5)
    position = lax.axis_index("ctx")
    has_prev = position > 0
    has_next = position < lax.axis_size("ctx") - 1
    shape_heads = (length, heads_here, head_size)
    shape_flat = (length, heads_here * head_size)

    lin_queries = lin_q.reshape(shape_heads)
    lin_keys = lin_k.reshape(shape_heads)
    lin_values = lin_v.reshape(shape_heads)
    query_f = lin_queries.astype(jnp.float32)
    key_f = lin_keys.astype(jnp.float32)
    value_f = lin_values.astype(jnp.float32)
    lead_weight, block_decay, tail_weight, window_weight = linear_parts(lin_gate)
    summary = jnp.einsum("hs,shd,she->hde", tail_weight, key_f, value_f, precision=exact_mode)
    state_in = exclusive_scan(block_decay, summary, "ctx", False)

    queries = soft_q.reshape(shape_heads)
    keys_own = soft_k.reshape(shape_heads)
    values_own = soft_v.reshape(shape_heads)
    grad_out = soft_dout.reshape(shape_heads)
    pair_prev = shifted(jnp.stack((soft_k, soft_v)), "ctx", 1)
    pair_next = shifted(jnp.stack((soft_q, soft_dout)), "ctx", -1)
    keys_prev = pair_prev[0].reshape(shape_heads)
    values_prev = pair_prev[1].reshape(shape_heads)
    queries_next = pair_next[0].reshape(shape_heads)
    grad_out_next = pair_next[1].reshape(shape_heads)
    row_ids = lax.broadcasted_iota(jnp.int32, (length, length), 0)
    col_ids = lax.broadcasted_iota(jnp.int32, (length, length), 1)
    own_mask = (col_ids <= row_ids)[None]
    prev_mask = ((col_ids > row_ids) & has_prev)[None]
    next_mask = ((col_ids > row_ids) & has_next)[None]
    scores_own = (
        jnp.einsum("thd,shd->hts", queries, keys_own, preferred_element_type=jnp.float32) * factor
    )
    scores_prev = (
        jnp.einsum("thd,shd->hts", queries, keys_prev, preferred_element_type=jnp.float32) * factor
    )
    row_max = jnp.maximum(
        jnp.max(jnp.where(own_mask, scores_own, masked_fill), axis=2),
        jnp.max(jnp.where(prev_mask, scores_prev, masked_fill), axis=2),
    )
    total = jnp.sum(jnp.where(own_mask, jnp.exp(scores_own - row_max[..., None]), 0.0), axis=2)
    total = total + jnp.sum(
        jnp.where(prev_mask, jnp.exp(scores_prev - row_max[..., None]), 0.0), axis=2
    )
    log_total = row_max + jnp.log(total)
    probs_own = jnp.where(own_mask, jnp.exp(scores_own - log_total[..., None]), 0.0)
    probs_prev = jnp.where(prev_mask, jnp.exp(scores_prev - log_total[..., None]), 0.0)
    dprob_own = jnp.einsum("thd,shd->hts", grad_out, values_own, preferred_element_type=jnp.float32)
    dprob_prev = jnp.einsum(
        "thd,shd->hts", grad_out, values_prev, preferred_element_type=jnp.float32
    )
    row_delta = jnp.sum(probs_own * dprob_own, axis=2) + jnp.sum(probs_prev * dprob_prev, axis=2)
    stats_next = shifted(jnp.stack((log_total, row_delta)), "ctx", -1)
    dscore_own = (probs_own * (dprob_own - row_delta[..., None])).astype(jnp.bfloat16)
    dscore_prev = (probs_prev * (dprob_prev - row_delta[..., None])).astype(jnp.bfloat16)
    grad_q = (
        jnp.einsum("hts,shd->thd", dscore_own, keys_own, preferred_element_type=jnp.float32)
        + jnp.einsum("hts,shd->thd", dscore_prev, keys_prev, preferred_element_type=jnp.float32)
    ) * factor
    grad_k = (
        jnp.einsum("hts,thd->shd", dscore_own, queries, preferred_element_type=jnp.float32) * factor
    )
    grad_v = jnp.einsum(
        "hts,thd->shd", probs_own.astype(jnp.bfloat16), grad_out, preferred_element_type=jnp.float32
    )
    late = (grad_k, grad_v, queries_next, grad_out_next, stats_next, keys_own, values_own)

    def next_block_terms(grad_k, grad_v, queries_next, grad_out_next, stats_next, keys_own,
                         values_own):
        scores_next = (
            jnp.einsum("thd,shd->hts", queries_next, keys_own, preferred_element_type=jnp.float32)
            * factor
        )
        probs_next = jnp.where(next_mask, jnp.exp(scores_next - stats_next[0][..., None]), 0.0)
        dprob_next = jnp.einsum(
            "thd,shd->hts", grad_out_next, values_own, preferred_element_type=jnp.float32
        )
        dscore_next = (probs_next * (dprob_next - stats_next[1][..., None])).astype(jnp.bfloat16)
        grad_k = grad_k + (
            jnp.einsum("hts,thd->shd", dscore_next, queries_next, preferred_element_type=jnp.float32)
            * factor
        )
        grad_v = grad_v + jnp.einsum(
            "hts,thd->shd",
            probs_next.astype(jnp.bfloat16),
            grad_out_next,
            preferred_element_type=jnp.float32,
        )

        return grad_k, grad_v

    lin_scores = jnp.einsum(
        "thd,shd->hts", lin_queries, lin_keys, preferred_element_type=jnp.float32
    )
    attended = (lin_scores * factor * window_weight).astype(jnp.bfloat16)
    lin_output = jnp.einsum(
        "hts,she->the", attended, lin_values, preferred_element_type=jnp.float32
    )
    lin_output = lin_output + factor * lead_weight.T[:, :, None] * jnp.einsum(
        "thd,hde->the", query_f, state_in, precision=exact_mode
    )
    dy_f = lin_dy.reshape(shape_heads).astype(jnp.float32)
    norm_sums = lax.psum(
        (jnp.sum(lin_output * lin_output, axis=(1, 2)), jnp.sum(lin_output * dy_f, axis=(1, 2))),
        "head",
    )
    late = lax.optimization_barrier((norm_sums, late))[1]
    grad_k, grad_v = next_block_terms(*late)
    width_all = LOCAL_HEADS * HEAD_DIM
    rms_value = jnp.sqrt(norm_sums[0] / width_all + 1e-06)
    lin_grad = (
        dy_f / rms_value[:, None, None]
        - lin_output * (norm_sums[1] / (rms_value**3 * width_all))[:, None, None]
    )
    lin_grad_b = lin_grad.astype(jnp.bfloat16)
    lin_grad_f = lin_grad_b.astype(jnp.float32)
    grad_summary = factor * jnp.einsum(
        "ht,thd,the->hde", lead_weight, query_f, lin_grad_f, precision=exact_mode
    )
    grad_in = exclusive_scan(block_decay, grad_summary, "ctx", True)
    grad_raw = jnp.einsum(
        "the,she->hts", lin_grad_b, lin_values, preferred_element_type=jnp.float32
    )
    grad_scores = (grad_raw * factor * window_weight).astype(jnp.bfloat16)
    lin_grad_q = jnp.einsum(
        "hts,shd->thd", grad_scores, lin_keys, preferred_element_type=jnp.float32
    )
    lin_grad_q = lin_grad_q + factor * lead_weight.T[:, :, None] * jnp.einsum(
        "hde,the->thd", state_in, lin_grad_f, precision=exact_mode
    )
    lin_grad_k = jnp.einsum(
        "hts,thd->shd", grad_scores, lin_queries, preferred_element_type=jnp.float32
    )
    lin_grad_k = lin_grad_k + tail_weight.T[:, :, None] * jnp.einsum(
        "hde,she->shd", grad_in, value_f, precision=exact_mode
    )
    lin_grad_v = jnp.einsum(
        "hts,the->she", attended, lin_grad_b, preferred_element_type=jnp.float32
    )
    lin_grad_v = lin_grad_v + tail_weight.T[:, :, None] * jnp.einsum(
        "hde,shd->she", grad_in, key_f, precision=exact_mode
    )
    return (
        grad_q.astype(jnp.bfloat16).reshape(shape_flat),
        grad_k.astype(jnp.bfloat16).reshape(shape_flat),
        grad_v.astype(jnp.bfloat16).reshape(shape_flat),
        lin_grad_q.astype(jnp.bfloat16).reshape(shape_flat),
        lin_grad_k.astype(jnp.bfloat16).reshape(shape_flat),
        lin_grad_v.astype(jnp.bfloat16).reshape(shape_flat),
    )


def solution(mesh):
    in_specs = (
        P("ctx", "head"),
        P("ctx", "head"),
        P("ctx", "head"),
        P("ctx", "head"),
        P("ctx", "head"),
        P("ctx", "head"),
        P("ctx", "head"),
        P("head", "ctx"),
        P("ctx", "head"),
    )
    out_specs = (
        P("ctx", "head"),
        P("ctx", "head"),
        P("ctx", "head"),
        P("ctx", "head"),
        P("ctx", "head"),
        P("ctx", "head"),
    )
    return jax.shard_map(body, mesh=mesh, in_specs=in_specs, out_specs=out_specs, check_vma=False)
```

```python
import jax
import jax.numpy as jnp
from jax import lax
from jax.sharding import PartitionSpec as P

LOCAL_HEADS = 16
HEAD_DIM = 128


masked_fill = -1e30
exact_mode = lax.Precision.HIGHEST


def shifted(x, axis, by):
    peers = lax.axis_size(axis)
    pairs = [(i, i + by) for i in range(peers) if 0 <= i + by < peers]
    return lax.ppermute(x, axis, pairs)


def exclusive_scan(decay, value, axis, reverse):
    count = lax.axis_size(axis)
    heads, size = value.shape[0], value.shape[1]
    rows = lax.broadcasted_iota(jnp.int32, (heads, size + 8, value.shape[2]), 1)
    top = rows < size
    window = jnp.concatenate(
        [value, jnp.broadcast_to(decay[:, None, None], (heads, 8, value.shape[2]))], axis=1
    )
    result = jnp.where(top, 0.0, 1.0)
    step = 1
    while step < count:
        got = shifted(window.astype(jnp.bfloat16), axis, -step if reverse else step)
        got = got.astype(jnp.float32)
        result = jnp.where(top, result + result[:, size:size + 1, :1] * got, result * got)
        window = jnp.where(top, window + window[:, size:size + 1, :1] * got, window * got)
        step *= 2
    return result[:, :size]


def linear_parts(gates):
    running = jnp.cumsum(gates, axis=1)
    block_total = running[:, -1]
    length = gates.shape[1]
    row_ids = lax.broadcasted_iota(jnp.int32, (length, length), 0)
    col_ids = lax.broadcasted_iota(jnp.int32, (length, length), 1)
    lower = (col_ids <= row_ids)[None]
    spread = jnp.where(lower, running[:, :, None] - running[:, None, :], 0.0)
    window_weight = jnp.where(lower, jnp.exp(spread), 0.0)
    tail_weight = jnp.exp(block_total[:, None] - running)
    return (jnp.exp(running), jnp.exp(block_total), tail_weight, window_weight)


def body(soft_q, soft_k, soft_v, soft_dout, lin_q, lin_k, lin_v, lin_gate, lin_dy):
    heads_here = lin_gate.shape[0]
    length = soft_q.shape[0]
    head_size = soft_q.shape[1] // heads_here
    factor = head_size ** (-0.5)
    position = lax.axis_index("ctx")
    has_prev = position > 0
    has_next = position < lax.axis_size("ctx") - 1
    shape_heads = (length, heads_here, head_size)
    shape_flat = (length, heads_here * head_size)

    lin_queries = lin_q.reshape(shape_heads)
    lin_keys = lin_k.reshape(shape_heads)
    lin_values = lin_v.reshape(shape_heads)
    query_f = lin_queries.astype(jnp.float32)
    key_f = lin_keys.astype(jnp.float32)
    value_f = lin_values.astype(jnp.float32)
    lead_weight, block_decay, tail_weight, window_weight = linear_parts(lin_gate)
    summary = jnp.einsum("hs,shd,she->hde", tail_weight, key_f, value_f, precision=exact_mode)
    state_in = exclusive_scan(block_decay, summary, "ctx", False)

    queries = soft_q.reshape(shape_heads)
    keys_own = soft_k.reshape(shape_heads)
    values_own = soft_v.reshape(shape_heads)
    grad_out = soft_dout.reshape(shape_heads)
    pair_prev = shifted(jnp.stack((soft_k, soft_v)), "ctx", 1)
    pair_next = shifted(jnp.stack((soft_q, soft_dout)), "ctx", -1)
    keys_prev = pair_prev[0].reshape(shape_heads)
    values_prev = pair_prev[1].reshape(shape_heads)
    queries_next = pair_next[0].reshape(shape_heads)
    grad_out_next = pair_next[1].reshape(shape_heads)
    row_ids = lax.broadcasted_iota(jnp.int32, (length, length), 0)
    col_ids = lax.broadcasted_iota(jnp.int32, (length, length), 1)
    own_mask = (col_ids <= row_ids)[None]
    prev_mask = ((col_ids > row_ids) & has_prev)[None]
    next_mask = ((col_ids > row_ids) & has_next)[None]
    scores_own = (
        jnp.einsum("thd,shd->hts", queries, keys_own, preferred_element_type=jnp.float32) * factor
    )
    scores_prev = (
        jnp.einsum("thd,shd->hts", queries, keys_prev, preferred_element_type=jnp.float32) * factor
    )
    row_max = jnp.maximum(
        jnp.max(jnp.where(own_mask, scores_own, masked_fill), axis=2),
        jnp.max(jnp.where(prev_mask, scores_prev, masked_fill), axis=2),
    )
    total = jnp.sum(jnp.where(own_mask, jnp.exp(scores_own - row_max[..., None]), 0.0), axis=2)
    total = total + jnp.sum(
        jnp.where(prev_mask, jnp.exp(scores_prev - row_max[..., None]), 0.0), axis=2
    )
    log_total = row_max + jnp.log(total)
    probs_own = jnp.where(own_mask, jnp.exp(scores_own - log_total[..., None]), 0.0)
    probs_prev = jnp.where(prev_mask, jnp.exp(scores_prev - log_total[..., None]), 0.0)
    dprob_own = jnp.einsum("thd,shd->hts", grad_out, values_own, preferred_element_type=jnp.float32)
    dprob_prev = jnp.einsum(
        "thd,shd->hts", grad_out, values_prev, preferred_element_type=jnp.float32
    )
    row_delta = jnp.sum(probs_own * dprob_own, axis=2) + jnp.sum(probs_prev * dprob_prev, axis=2)
    stats_next = shifted(jnp.stack((log_total, row_delta)), "ctx", -1)
    dscore_own = (probs_own * (dprob_own - row_delta[..., None])).astype(jnp.bfloat16)
    dscore_prev = (probs_prev * (dprob_prev - row_delta[..., None])).astype(jnp.bfloat16)
    grad_q = (
        jnp.einsum("hts,shd->thd", dscore_own, keys_own, preferred_element_type=jnp.float32)
        + jnp.einsum("hts,shd->thd", dscore_prev, keys_prev, preferred_element_type=jnp.float32)
    ) * factor
    grad_k = (
        jnp.einsum("hts,thd->shd", dscore_own, queries, preferred_element_type=jnp.float32) * factor
    )
    grad_v = jnp.einsum(
        "hts,thd->shd", probs_own.astype(jnp.bfloat16), grad_out, preferred_element_type=jnp.float32
    )
    late = (grad_k, grad_v, queries_next, grad_out_next, stats_next, keys_own, values_own)

    def next_block_terms(grad_k, grad_v, queries_next, grad_out_next, stats_next, keys_own,
                         values_own):
        scores_next = (
            jnp.einsum("thd,shd->hts", queries_next, keys_own, preferred_element_type=jnp.float32)
            * factor
        )
        probs_next = jnp.where(next_mask, jnp.exp(scores_next - stats_next[0][..., None]), 0.0)
        dprob_next = jnp.einsum(
            "thd,shd->hts", grad_out_next, values_own, preferred_element_type=jnp.float32
        )
        dscore_next = (probs_next * (dprob_next - stats_next[1][..., None])).astype(jnp.bfloat16)
        grad_k = grad_k + (
            jnp.einsum("hts,thd->shd", dscore_next, queries_next, preferred_element_type=jnp.float32)
            * factor
        )
        grad_v = grad_v + jnp.einsum(
            "hts,thd->shd",
            probs_next.astype(jnp.bfloat16),
            grad_out_next,
            preferred_element_type=jnp.float32,
        )

        return grad_k, grad_v

    lin_scores = jnp.einsum(
        "thd,shd->hts", lin_queries, lin_keys, preferred_element_type=jnp.float32
    )
    attended = (lin_scores * factor * window_weight).astype(jnp.bfloat16)
    lin_output = jnp.einsum(
        "hts,she->the", attended, lin_values, preferred_element_type=jnp.float32
    )
    lin_output = lin_output + factor * lead_weight.T[:, :, None] * jnp.einsum(
        "thd,hde->the", query_f, state_in, precision=exact_mode
    )
    dy_f = lin_dy.reshape(shape_heads).astype(jnp.float32)
    norm_sums = lax.psum(
        (jnp.sum(lin_output * lin_output, axis=(1, 2)), jnp.sum(lin_output * dy_f, axis=(1, 2))),
        "head",
    )
    late = lax.optimization_barrier((norm_sums, late))[1]
    grad_k, grad_v = next_block_terms(*late)
    width_all = LOCAL_HEADS * HEAD_DIM
    rms_value = jnp.sqrt(norm_sums[0] / width_all + 1e-06)
    lin_grad = (
        dy_f / rms_value[:, None, None]
        - lin_output * (norm_sums[1] / (rms_value**3 * width_all))[:, None, None]
    )
    lin_grad_b = lin_grad.astype(jnp.bfloat16)
    lin_grad_f = lin_grad_b.astype(jnp.float32)
    grad_summary = factor * jnp.einsum(
        "ht,thd,the->hde", lead_weight, query_f, lin_grad_f, precision=exact_mode
    )
    grad_in = exclusive_scan(block_decay, grad_summary, "ctx", True)
    lin_grad_b, lin_grad_f = lax.optimization_barrier((grad_summary, lin_grad_b, lin_grad_f))[1:]
    grad_raw = jnp.einsum(
        "the,she->hts", lin_grad_b, lin_values, preferred_element_type=jnp.float32
    )
    grad_scores = (grad_raw * factor * window_weight).astype(jnp.bfloat16)
    lin_grad_q = jnp.einsum(
        "hts,shd->thd", grad_scores, lin_keys, preferred_element_type=jnp.float32
    )
    lin_grad_q = lin_grad_q + factor * lead_weight.T[:, :, None] * jnp.einsum(
        "hde,the->thd", state_in, lin_grad_f, precision=exact_mode
    )
    lin_grad_k = jnp.einsum(
        "hts,thd->shd", grad_scores, lin_queries, preferred_element_type=jnp.float32
    )
    lin_grad_k = lin_grad_k + tail_weight.T[:, :, None] * jnp.einsum(
        "hde,she->shd", grad_in, value_f, precision=exact_mode
    )
    lin_grad_v = jnp.einsum(
        "hts,the->she", attended, lin_grad_b, preferred_element_type=jnp.float32
    )
    lin_grad_v = lin_grad_v + tail_weight.T[:, :, None] * jnp.einsum(
        "hde,shd->she", grad_in, key_f, precision=exact_mode
    )
    return (
        grad_q.astype(jnp.bfloat16).reshape(shape_flat),
        grad_k.astype(jnp.bfloat16).reshape(shape_flat),
        grad_v.astype(jnp.bfloat16).reshape(shape_flat),
        lin_grad_q.astype(jnp.bfloat16).reshape(shape_flat),
        lin_grad_k.astype(jnp.bfloat16).reshape(shape_flat),
        lin_grad_v.astype(jnp.bfloat16).reshape(shape_flat),
    )


def solution(mesh):
    in_specs = (
        P("ctx", "head"),
        P("ctx", "head"),
        P("ctx", "head"),
        P("ctx", "head"),
        P("ctx", "head"),
        P("ctx", "head"),
        P("ctx", "head"),
        P("head", "ctx"),
        P("ctx", "head"),
    )
    out_specs = (
        P("ctx", "head"),
        P("ctx", "head"),
        P("ctx", "head"),
        P("ctx", "head"),
        P("ctx", "head"),
        P("ctx", "head"),
    )
    return jax.shard_map(body, mesh=mesh, in_specs=in_specs, out_specs=out_specs, check_vma=False)
```

```python
import jax
import jax.numpy as jnp
from jax import lax
from jax.sharding import PartitionSpec as P

LOCAL_HEADS = 16
HEAD_DIM = 128


masked_fill = -1e30
exact_mode = lax.Precision.HIGHEST


def shifted(x, axis, by):
    peers = lax.axis_size(axis)
    pairs = [(i, i + by) for i in range(peers) if 0 <= i + by < peers]
    return lax.ppermute(x, axis, pairs)


def exclusive_scan(decay, value, axis, reverse, stages=(), carry=()):
    count = lax.axis_size(axis)
    heads, size = value.shape[0], value.shape[1]
    rows = lax.broadcasted_iota(jnp.int32, (heads, size + 8, value.shape[2]), 1)
    top = rows < size
    window = jnp.concatenate(
        [value, jnp.broadcast_to(decay[:, None, None], (heads, 8, value.shape[2]))], axis=1
    )
    result = jnp.where(top, 0.0, 1.0)
    step = 1
    turn = 0
    while step < count:
        send = window.astype(jnp.bfloat16)
        if turn < len(stages):
            send, carry = lax.optimization_barrier((send, carry))
        got = shifted(send, axis, -step if reverse else step)
        if turn < len(stages):
            carry = stages[turn](carry)
        got = got.astype(jnp.float32)
        window = jnp.where(top, window + window[:, size:size + 1, :1] * got, window * got)
        result = jnp.where(top, result + result[:, size:size + 1, :1] * got, result * got)
        step *= 2
        turn += 1
    for stage in stages[turn:]:
        carry = stage(carry)
    return result[:, :size], carry


def linear_parts(gates):
    running = jnp.cumsum(gates, axis=1)
    block_total = running[:, -1]
    length = gates.shape[1]
    row_ids = lax.broadcasted_iota(jnp.int32, (length, length), 0)
    col_ids = lax.broadcasted_iota(jnp.int32, (length, length), 1)
    lower = (col_ids <= row_ids)[None]
    spread = jnp.where(lower, running[:, :, None] - running[:, None, :], 0.0)
    window_weight = jnp.where(lower, jnp.exp(spread), 0.0)
    tail_weight = jnp.exp(block_total[:, None] - running)
    return (jnp.exp(running), jnp.exp(block_total), tail_weight, window_weight)


def body(soft_q, soft_k, soft_v, soft_dout, lin_q, lin_k, lin_v, lin_gate, lin_dy):
    heads_here = lin_gate.shape[0]
    length = soft_q.shape[0]
    head_size = soft_q.shape[1] // heads_here
    factor = head_size ** (-0.5)
    position = lax.axis_index("ctx")
    has_prev = position > 0
    has_next = position < lax.axis_size("ctx") - 1
    shape_heads = (length, heads_here, head_size)
    shape_flat = (length, heads_here * head_size)
    row_ids = lax.broadcasted_iota(jnp.int32, (length, length), 0)
    col_ids = lax.broadcasted_iota(jnp.int32, (length, length), 1)
    own_mask = (col_ids <= row_ids)[None]
    prev_mask = ((col_ids > row_ids) & has_prev)[None]
    next_mask = ((col_ids > row_ids) & has_next)[None]

    lin_queries = lin_q.reshape(shape_heads)
    lin_keys = lin_k.reshape(shape_heads)
    lin_values = lin_v.reshape(shape_heads)
    query_f = lin_queries.astype(jnp.float32)
    key_f = lin_keys.astype(jnp.float32)
    value_f = lin_values.astype(jnp.float32)
    lead_weight, block_decay, tail_weight, window_weight = linear_parts(lin_gate)
    summary = jnp.einsum("hs,shd,she->hde", tail_weight, key_f, value_f, precision=exact_mode)

    def soft_sends(c):
        c = dict(c)
        pair_prev = shifted(jnp.stack((c["soft_k"], c["soft_v"])), "ctx", 1)
        pair_next = shifted(jnp.stack((c["soft_q"], c["soft_dout"])), "ctx", -1)
        c["keys_prev"] = pair_prev[0].reshape(shape_heads)
        c["values_prev"] = pair_prev[1].reshape(shape_heads)
        c["queries_next"] = pair_next[0].reshape(shape_heads)
        c["grad_out_next"] = pair_next[1].reshape(shape_heads)
        queries = c["soft_q"].reshape(shape_heads)
        keys_own = c["soft_k"].reshape(shape_heads)
        values_own = c["soft_v"].reshape(shape_heads)
        grad_out = c["soft_dout"].reshape(shape_heads)
        c["scores_own"] = (
            jnp.einsum("thd,shd->hts", queries, keys_own, preferred_element_type=jnp.float32)
            * factor
        )
        c["dprob_own"] = jnp.einsum(
            "thd,shd->hts", grad_out, values_own, preferred_element_type=jnp.float32
        )
        lin_scores = jnp.einsum(
            "thd,shd->hts", c["lin_q"].reshape(shape_heads), c["lin_k"].reshape(shape_heads),
            preferred_element_type=jnp.float32,
        )
        c["attended"] = (lin_scores * factor * c["window_weight"]).astype(jnp.bfloat16)
        c["lin_intra"] = jnp.einsum(
            "hts,she->the", c["attended"], c["lin_v"].reshape(shape_heads),
            preferred_element_type=jnp.float32,
        )
        return c

    def soft_stats(c):
        c = dict(c)
        queries = c["soft_q"].reshape(shape_heads)
        grad_out = c["soft_dout"].reshape(shape_heads)
        scores_own = c["scores_own"]
        dprob_own = c["dprob_own"]
        scores_prev = (
            jnp.einsum("thd,shd->hts", queries, c["keys_prev"], preferred_element_type=jnp.float32)
            * factor
        )
        row_max = jnp.maximum(
            jnp.max(jnp.where(own_mask, scores_own, masked_fill), axis=2),
            jnp.max(jnp.where(prev_mask, scores_prev, masked_fill), axis=2),
        )
        total = jnp.sum(jnp.where(own_mask, jnp.exp(scores_own - row_max[..., None]), 0.0), axis=2)
        total = total + jnp.sum(
            jnp.where(prev_mask, jnp.exp(scores_prev - row_max[..., None]), 0.0), axis=2
        )
        log_total = row_max + jnp.log(total)
        probs_own = jnp.where(own_mask, jnp.exp(scores_own - log_total[..., None]), 0.0)
        probs_prev = jnp.where(prev_mask, jnp.exp(scores_prev - log_total[..., None]), 0.0)
        dprob_prev = jnp.einsum(
            "thd,shd->hts", grad_out, c["values_prev"], preferred_element_type=jnp.float32
        )
        row_delta = jnp.sum(probs_own * dprob_own, axis=2) + jnp.sum(
            probs_prev * dprob_prev, axis=2
        )
        c["stats_next"] = shifted(jnp.stack((log_total, row_delta)), "ctx", -1)
        c["dscore_own"] = (probs_own * (dprob_own - row_delta[..., None])).astype(jnp.bfloat16)
        c["dscore_prev"] = (probs_prev * (dprob_prev - row_delta[..., None])).astype(jnp.bfloat16)
        c["probs_own_b"] = probs_own.astype(jnp.bfloat16)
        for name in ("scores_own", "dprob_own"):
            del c[name]
        return c

    def soft_grads(c):
        c = dict(c)
        queries = c["soft_q"].reshape(shape_heads)
        keys_own = c["soft_k"].reshape(shape_heads)
        grad_out = c["soft_dout"].reshape(shape_heads)
        c["grad_q"] = (
            jnp.einsum("hts,shd->thd", c["dscore_own"], keys_own, preferred_element_type=jnp.float32)
            + jnp.einsum(
                "hts,shd->thd", c["dscore_prev"], c["keys_prev"], preferred_element_type=jnp.float32
            )
        ) * factor
        c["grad_k"] = (
            jnp.einsum("hts,thd->shd", c["dscore_own"], queries, preferred_element_type=jnp.float32)
            * factor
        )
        c["grad_v"] = jnp.einsum(
            "hts,thd->shd", c["probs_own_b"], grad_out, preferred_element_type=jnp.float32
        )
        for name in ("dscore_own", "dscore_prev", "probs_own_b", "keys_prev", "values_prev"):
            del c[name]
        return c

    carry = dict(
        soft_q=soft_q, soft_k=soft_k, soft_v=soft_v, soft_dout=soft_dout,
        lin_q=lin_q, lin_k=lin_k, lin_v=lin_v, window_weight=window_weight,
    )
    state_in, carry = exclusive_scan(
        block_decay, summary, "ctx", False, (soft_sends, soft_stats, soft_grads), carry
    )

    lin_output = carry["lin_intra"] + factor * lead_weight.T[:, :, None] * jnp.einsum(
        "thd,hde->the", query_f, state_in, precision=exact_mode
    )
    dy_f = lin_dy.reshape(shape_heads).astype(jnp.float32)
    norm_sums = lax.psum(
        (jnp.sum(lin_output * lin_output, axis=(1, 2)), jnp.sum(lin_output * dy_f, axis=(1, 2))),
        "head",
    )
    width_all = LOCAL_HEADS * HEAD_DIM
    rms_value = jnp.sqrt(norm_sums[0] / width_all + 1e-06)
    lin_grad = (
        dy_f / rms_value[:, None, None]
        - lin_output * (norm_sums[1] / (rms_value**3 * width_all))[:, None, None]
    )
    lin_grad_b = lin_grad.astype(jnp.bfloat16)
    lin_grad_f = lin_grad_b.astype(jnp.float32)
    grad_summary = factor * jnp.einsum(
        "ht,thd,the->hde", lead_weight, query_f, lin_grad_f, precision=exact_mode
    )

    def linear_own(c):
        c = dict(c)
        grad_b = c["lin_grad_b"]
        grad_raw = jnp.einsum(
            "the,she->hts", grad_b, c["lin_v"].reshape(shape_heads),
            preferred_element_type=jnp.float32,
        )
        grad_scores = (grad_raw * factor * c["window_weight"]).astype(jnp.bfloat16)
        lin_grad_q = jnp.einsum(
            "hts,shd->thd", grad_scores, c["lin_k"].reshape(shape_heads),
            preferred_element_type=jnp.float32,
        )
        lin_grad_q = lin_grad_q + factor * c["lead_weight"].T[:, :, None] * jnp.einsum(
            "hde,the->thd", c["state_in"], grad_b.astype(jnp.float32), precision=exact_mode
        )
        c["lin_dq"] = lin_grad_q.astype(jnp.bfloat16).reshape(shape_flat)
        c["lin_dk"] = jnp.einsum(
            "hts,thd->shd", grad_scores, c["lin_q"].reshape(shape_heads),
            preferred_element_type=jnp.float32,
        )
        c["lin_dv"] = jnp.einsum(
            "hts,the->she", c["attended"], grad_b, preferred_element_type=jnp.float32
        )
        for name in ("lin_grad_b", "state_in", "lead_weight", "attended", "window_weight"):
            del c[name]
        return c

    def soft_next_scores(c):
        c = dict(c)
        keys_own = c["soft_k"].reshape(shape_heads)
        values_own = c["soft_v"].reshape(shape_heads)
        stats_next = c["stats_next"]
        scores_next = (
            jnp.einsum(
                "thd,shd->hts", c["queries_next"], keys_own, preferred_element_type=jnp.float32
            )
            * factor
        )
        probs_next = jnp.where(next_mask, jnp.exp(scores_next - stats_next[0][..., None]), 0.0)
        dprob_next = jnp.einsum(
            "thd,shd->hts", c["grad_out_next"], values_own, preferred_element_type=jnp.float32
        )
        c["dscore_next"] = (probs_next * (dprob_next - stats_next[1][..., None])).astype(
            jnp.bfloat16
        )
        c["probs_next_b"] = probs_next.astype(jnp.bfloat16)
        return c

    def soft_next_grads(c):
        c = dict(c)
        grad_k = c["grad_k"] + (
            jnp.einsum(
                "hts,thd->shd", c["dscore_next"], c["queries_next"],
                preferred_element_type=jnp.float32,
            )
            * factor
        )
        grad_v = c["grad_v"] + jnp.einsum(
            "hts,thd->shd", c["probs_next_b"], c["grad_out_next"],
            preferred_element_type=jnp.float32,
        )
        c["soft_dk"] = grad_k.astype(jnp.bfloat16).reshape(shape_flat)
        c["soft_dv"] = grad_v.astype(jnp.bfloat16).reshape(shape_flat)
        return c

    late = dict(
        lin_grad_b=lin_grad_b, state_in=state_in, lead_weight=lead_weight,
        attended=carry["attended"], window_weight=window_weight,
        lin_q=lin_q, lin_k=lin_k, lin_v=lin_v,
        soft_k=soft_k, soft_v=soft_v, stats_next=carry["stats_next"],
        queries_next=carry["queries_next"], grad_out_next=carry["grad_out_next"],
        grad_k=carry["grad_k"], grad_v=carry["grad_v"],
    )
    grad_in, late = exclusive_scan(
        block_decay, grad_summary, "ctx", True, (linear_own, soft_next_scores, soft_next_grads),
        late,
    )
    lin_grad_k = late["lin_dk"] + tail_weight.T[:, :, None] * jnp.einsum(
        "hde,she->shd", grad_in, value_f, precision=exact_mode
    )
    lin_grad_v = late["lin_dv"] + tail_weight.T[:, :, None] * jnp.einsum(
        "hde,shd->she", grad_in, key_f, precision=exact_mode
    )
    return (
        carry["grad_q"].astype(jnp.bfloat16).reshape(shape_flat),
        late["soft_dk"],
        late["soft_dv"],
        late["lin_dq"],
        lin_grad_k.astype(jnp.bfloat16).reshape(shape_flat),
        lin_grad_v.astype(jnp.bfloat16).reshape(shape_flat),
    )


def solution(mesh):
    in_specs = (
        P("ctx", "head"),
        P("ctx", "head"),
        P("ctx", "head"),
        P("ctx", "head"),
        P("ctx", "head"),
        P("ctx", "head"),
        P("ctx", "head"),
        P("head", "ctx"),
        P("ctx", "head"),
    )
    out_specs = (
        P("ctx", "head"),
        P("ctx", "head"),
        P("ctx", "head"),
        P("ctx", "head"),
        P("ctx", "head"),
        P("ctx", "head"),
    )
    return jax.shard_map(body, mesh=mesh, in_specs=in_specs, out_specs=out_specs, check_vma=False)
```

```python
import jax
import jax.numpy as jnp
from jax import lax
from jax.sharding import PartitionSpec as P

LOCAL_HEADS = 16
HEAD_DIM = 128


masked_fill = -1e30
exact_mode = lax.Precision.HIGHEST


def shifted(x, axis, by):
    peers = lax.axis_size(axis)
    pairs = [(i, i + by) for i in range(peers) if 0 <= i + by < peers]
    return lax.ppermute(x, axis, pairs)


def exclusive_scan(decay, value, axis, reverse, stages=(), carry=()):
    count = lax.axis_size(axis)
    heads, size = value.shape[0], value.shape[1]
    rows = lax.broadcasted_iota(jnp.int32, (heads, size + 8, value.shape[2]), 1)
    top = rows < size
    window = jnp.concatenate(
        [value, jnp.broadcast_to(decay[:, None, None], (heads, 8, value.shape[2]))], axis=1
    )
    result = jnp.where(top, 0.0, 1.0)
    step = 1
    turn = 0
    while step < count:
        send = window.astype(jnp.bfloat16)
        if turn < len(stages):
            send, carry = lax.optimization_barrier((send, carry))
        got = shifted(send, axis, -step if reverse else step)
        if turn < len(stages):
            carry = stages[turn](carry)
        got = got.astype(jnp.float32)
        window = jnp.where(top, window + window[:, size:size + 1, :1] * got, window * got)
        result = jnp.where(top, result + result[:, size:size + 1, :1] * got, result * got)
        step *= 2
        turn += 1
    for stage in stages[turn:]:
        carry = stage(carry)
    return result[:, :size], carry


def linear_parts(gates):
    running = jnp.cumsum(gates, axis=1)
    block_total = running[:, -1]
    length = gates.shape[1]
    row_ids = lax.broadcasted_iota(jnp.int32, (length, length), 0)
    col_ids = lax.broadcasted_iota(jnp.int32, (length, length), 1)
    lower = (col_ids <= row_ids)[None]
    spread = jnp.where(lower, running[:, :, None] - running[:, None, :], 0.0)
    window_weight = jnp.where(lower, jnp.exp(spread), 0.0)
    tail_weight = jnp.exp(block_total[:, None] - running)
    return (jnp.exp(running), jnp.exp(block_total), tail_weight, window_weight)


def body(soft_q, soft_k, soft_v, soft_dout, lin_q, lin_k, lin_v, lin_gate, lin_dy):
    heads_here = lin_gate.shape[0]
    length = soft_q.shape[0]
    head_size = soft_q.shape[1] // heads_here
    factor = head_size ** (-0.5)
    position = lax.axis_index("ctx")
    has_prev = position > 0
    has_next = position < lax.axis_size("ctx") - 1
    shape_heads = (length, heads_here, head_size)
    shape_flat = (length, heads_here * head_size)
    row_ids = lax.broadcasted_iota(jnp.int32, (length, length), 0)
    col_ids = lax.broadcasted_iota(jnp.int32, (length, length), 1)
    own_mask = (col_ids <= row_ids)[None]
    prev_mask = ((col_ids > row_ids) & has_prev)[None]
    next_mask = ((col_ids > row_ids) & has_next)[None]

    lin_queries = lin_q.reshape(shape_heads)
    lin_keys = lin_k.reshape(shape_heads)
    lin_values = lin_v.reshape(shape_heads)
    query_f = lin_queries.astype(jnp.float32)
    key_f = lin_keys.astype(jnp.float32)
    value_f = lin_values.astype(jnp.float32)
    lead_weight, block_decay, tail_weight, window_weight = linear_parts(lin_gate)
    summary = jnp.einsum("hs,shd,she->hde", tail_weight, key_f, value_f, precision=exact_mode)

    def soft_sends(c):
        c = dict(c)
        c["keys_prev"] = shifted(c["soft_k"], "ctx", 1).reshape(shape_heads)
        c["values_prev"] = shifted(c["soft_v"], "ctx", 1).reshape(shape_heads)
        c["queries_next"] = shifted(c["soft_q"], "ctx", -1).reshape(shape_heads)
        c["grad_out_next"] = shifted(c["soft_dout"], "ctx", -1).reshape(shape_heads)
        queries = c["soft_q"].reshape(shape_heads)
        keys_own = c["soft_k"].reshape(shape_heads)
        values_own = c["soft_v"].reshape(shape_heads)
        grad_out = c["soft_dout"].reshape(shape_heads)
        c["scores_own"] = (
            jnp.einsum("thd,shd->hts", queries, keys_own, preferred_element_type=jnp.float32)
            * factor
        )
        c["dprob_own"] = jnp.einsum(
            "thd,shd->hts", grad_out, values_own, preferred_element_type=jnp.float32
        )
        return c

    def soft_stats(c):
        c = dict(c)
        queries = c["soft_q"].reshape(shape_heads)
        grad_out = c["soft_dout"].reshape(shape_heads)
        scores_own = c["scores_own"]
        dprob_own = c["dprob_own"]
        scores_prev = (
            jnp.einsum("thd,shd->hts", queries, c["keys_prev"], preferred_element_type=jnp.float32)
            * factor
        )
        row_max = jnp.maximum(
            jnp.max(jnp.where(own_mask, scores_own, masked_fill), axis=2),
            jnp.max(jnp.where(prev_mask, scores_prev, masked_fill), axis=2),
        )
        total = jnp.sum(jnp.where(own_mask, jnp.exp(scores_own - row_max[..., None]), 0.0), axis=2)
        total = total + jnp.sum(
            jnp.where(prev_mask, jnp.exp(scores_prev - row_max[..., None]), 0.0), axis=2
        )
        log_total = row_max + jnp.log(total)
        probs_own = jnp.where(own_mask, jnp.exp(scores_own - log_total[..., None]), 0.0)
        probs_prev = jnp.where(prev_mask, jnp.exp(scores_prev - log_total[..., None]), 0.0)
        dprob_prev = jnp.einsum(
            "thd,shd->hts", grad_out, c["values_prev"], preferred_element_type=jnp.float32
        )
        row_delta = jnp.sum(probs_own * dprob_own, axis=2) + jnp.sum(
            probs_prev * dprob_prev, axis=2
        )
        c["stats_next"] = shifted(jnp.stack((log_total, row_delta)), "ctx", -1)
        c["dscore_own"] = (probs_own * (dprob_own - row_delta[..., None])).astype(jnp.bfloat16)
        c["dscore_prev"] = (probs_prev * (dprob_prev - row_delta[..., None])).astype(jnp.bfloat16)
        c["probs_own_b"] = probs_own.astype(jnp.bfloat16)
        for name in ("scores_own", "dprob_own"):
            del c[name]
        return c

    def soft_grads(c):
        c = dict(c)
        queries = c["soft_q"].reshape(shape_heads)
        keys_own = c["soft_k"].reshape(shape_heads)
        grad_out = c["soft_dout"].reshape(shape_heads)
        c["grad_q"] = (
            jnp.einsum("hts,shd->thd", c["dscore_own"], keys_own, preferred_element_type=jnp.float32)
            + jnp.einsum(
                "hts,shd->thd", c["dscore_prev"], c["keys_prev"], preferred_element_type=jnp.float32
            )
        ) * factor
        c["grad_k"] = (
            jnp.einsum("hts,thd->shd", c["dscore_own"], queries, preferred_element_type=jnp.float32)
            * factor
        )
        c["grad_v"] = jnp.einsum(
            "hts,thd->shd", c["probs_own_b"], grad_out, preferred_element_type=jnp.float32
        )
        lin_scores = jnp.einsum(
            "thd,shd->hts", c["lin_q"].reshape(shape_heads), c["lin_k"].reshape(shape_heads),
            preferred_element_type=jnp.float32,
        )
        c["attended"] = (lin_scores * factor * c["window_weight"]).astype(jnp.bfloat16)
        c["lin_intra"] = jnp.einsum(
            "hts,she->the", c["attended"], c["lin_v"].reshape(shape_heads),
            preferred_element_type=jnp.float32,
        )
        for name in ("dscore_own", "dscore_prev", "probs_own_b", "keys_prev", "values_prev"):
            del c[name]
        return c

    carry = dict(
        soft_q=soft_q, soft_k=soft_k, soft_v=soft_v, soft_dout=soft_dout,
        lin_q=lin_q, lin_k=lin_k, lin_v=lin_v, window_weight=window_weight,
    )
    state_in, carry = exclusive_scan(
        block_decay, summary, "ctx", False, (soft_sends, soft_stats, soft_grads), carry
    )

    lin_output = carry["lin_intra"] + factor * lead_weight.T[:, :, None] * jnp.einsum(
        "thd,hde->the", query_f, state_in, precision=exact_mode
    )
    dy_f = lin_dy.reshape(shape_heads).astype(jnp.float32)
    norm_sums = lax.psum(
        (jnp.sum(lin_output * lin_output, axis=(1, 2)), jnp.sum(lin_output * dy_f, axis=(1, 2))),
        "head",
    )
    width_all = LOCAL_HEADS * HEAD_DIM
    rms_value = jnp.sqrt(norm_sums[0] / width_all + 1e-06)
    lin_grad = (
        dy_f / rms_value[:, None, None]
        - lin_output * (norm_sums[1] / (rms_value**3 * width_all))[:, None, None]
    )
    lin_grad_b = lin_grad.astype(jnp.bfloat16)
    lin_grad_f = lin_grad_b.astype(jnp.float32)
    grad_summary = factor * jnp.einsum(
        "ht,thd,the->hde", lead_weight, query_f, lin_grad_f, precision=exact_mode
    )

    def linear_own(c):
        c = dict(c)
        grad_b = c["lin_grad_b"]
        grad_raw = jnp.einsum(
            "the,she->hts", grad_b, c["lin_v"].reshape(shape_heads),
            preferred_element_type=jnp.float32,
        )
        grad_scores = (grad_raw * factor * c["window_weight"]).astype(jnp.bfloat16)
        lin_grad_q = jnp.einsum(
            "hts,shd->thd", grad_scores, c["lin_k"].reshape(shape_heads),
            preferred_element_type=jnp.float32,
        )
        lin_grad_q = lin_grad_q + factor * c["lead_weight"].T[:, :, None] * jnp.einsum(
            "hde,the->thd", c["state_in"], grad_b.astype(jnp.float32), precision=exact_mode
        )
        c["lin_dq"] = lin_grad_q.astype(jnp.bfloat16).reshape(shape_flat)
        c["lin_dk"] = jnp.einsum(
            "hts,thd->shd", grad_scores, c["lin_q"].reshape(shape_heads),
            preferred_element_type=jnp.float32,
        )
        c["lin_dv"] = jnp.einsum(
            "hts,the->she", c["attended"], grad_b, preferred_element_type=jnp.float32
        )
        for name in ("lin_grad_b", "state_in", "lead_weight", "attended", "window_weight"):
            del c[name]
        return c

    def soft_next_scores(c):
        c = dict(c)
        keys_own = c["soft_k"].reshape(shape_heads)
        values_own = c["soft_v"].reshape(shape_heads)
        stats_next = c["stats_next"]
        scores_next = (
            jnp.einsum(
                "thd,shd->hts", c["queries_next"], keys_own, preferred_element_type=jnp.float32
            )
            * factor
        )
        probs_next = jnp.where(next_mask, jnp.exp(scores_next - stats_next[0][..., None]), 0.0)
        dprob_next = jnp.einsum(
            "thd,shd->hts", c["grad_out_next"], values_own, preferred_element_type=jnp.float32
        )
        c["dscore_next"] = (probs_next * (dprob_next - stats_next[1][..., None])).astype(
            jnp.bfloat16
        )
        c["probs_next_b"] = probs_next.astype(jnp.bfloat16)
        return c

    def soft_next_grads(c):
        c = dict(c)
        grad_k = c["grad_k"] + (
            jnp.einsum(
                "hts,thd->shd", c["dscore_next"], c["queries_next"],
                preferred_element_type=jnp.float32,
            )
            * factor
        )
        grad_v = c["grad_v"] + jnp.einsum(
            "hts,thd->shd", c["probs_next_b"], c["grad_out_next"],
            preferred_element_type=jnp.float32,
        )
        c["soft_dk"] = grad_k.astype(jnp.bfloat16).reshape(shape_flat)
        c["soft_dv"] = grad_v.astype(jnp.bfloat16).reshape(shape_flat)
        return c

    late = dict(
        lin_grad_b=lin_grad_b, state_in=state_in, lead_weight=lead_weight,
        attended=carry["attended"], window_weight=window_weight,
        lin_q=lin_q, lin_k=lin_k, lin_v=lin_v,
        soft_k=soft_k, soft_v=soft_v, stats_next=carry["stats_next"],
        queries_next=carry["queries_next"], grad_out_next=carry["grad_out_next"],
        grad_k=carry["grad_k"], grad_v=carry["grad_v"],
    )
    grad_in, late = exclusive_scan(
        block_decay, grad_summary, "ctx", True, (linear_own, soft_next_scores, soft_next_grads),
        late,
    )
    lin_grad_k = late["lin_dk"] + tail_weight.T[:, :, None] * jnp.einsum(
        "hde,she->shd", grad_in, value_f, precision=exact_mode
    )
    lin_grad_v = late["lin_dv"] + tail_weight.T[:, :, None] * jnp.einsum(
        "hde,shd->she", grad_in, key_f, precision=exact_mode
    )
    return (
        carry["grad_q"].astype(jnp.bfloat16).reshape(shape_flat),
        late["soft_dk"],
        late["soft_dv"],
        late["lin_dq"],
        lin_grad_k.astype(jnp.bfloat16).reshape(shape_flat),
        lin_grad_v.astype(jnp.bfloat16).reshape(shape_flat),
    )


def solution(mesh):
    in_specs = (
        P("ctx", "head"),
        P("ctx", "head"),
        P("ctx", "head"),
        P("ctx", "head"),
        P("ctx", "head"),
        P("ctx", "head"),
        P("ctx", "head"),
        P("head", "ctx"),
        P("ctx", "head"),
    )
    out_specs = (
        P("ctx", "head"),
        P("ctx", "head"),
        P("ctx", "head"),
        P("ctx", "head"),
        P("ctx", "head"),
        P("ctx", "head"),
    )
    return jax.shard_map(body, mesh=mesh, in_specs=in_specs, out_specs=out_specs, check_vma=False)
```

```python
import jax
import jax.numpy as jnp
from jax import lax
from jax.sharding import PartitionSpec as P

LOCAL_HEADS = 16
HEAD_DIM = 128


masked_fill = -1e30
exact_mode = lax.Precision.HIGHEST


def shifted(x, axis, by):
    peers = lax.axis_size(axis)
    pairs = [(i, i + by) for i in range(peers) if 0 <= i + by < peers]
    return lax.ppermute(x, axis, pairs)


def exclusive_scan(decay, value, axis, reverse, stages=(), carry=()):
    count = lax.axis_size(axis)
    heads, size, width = value.shape
    win_value, win_decay = value, decay
    res_value, res_decay = jnp.zeros_like(value), jnp.ones_like(decay)
    step = 1
    turn = 0
    while step < count:
        send = jnp.concatenate(
            [win_value, jnp.broadcast_to(win_decay[:, None, None], (heads, 8, width))], axis=1
        ).astype(jnp.bfloat16)
        if turn < len(stages):
            send, carry = lax.optimization_barrier((send, carry))
        got = shifted(send, axis, -step if reverse else step)
        if turn < len(stages):
            carry = stages[turn](carry)
        got_value = got[:, :size].astype(jnp.float32)
        got_decay = got[:, size, 0].astype(jnp.float32)
        win_value = win_value + win_decay[:, None, None] * got_value
        res_value = res_value + res_decay[:, None, None] * got_value
        win_decay = win_decay * got_decay
        res_decay = res_decay * got_decay
        step *= 2
        turn += 1
    for stage in stages[turn:]:
        carry = stage(carry)
    return res_value, carry


def linear_parts(gates):
    running = jnp.cumsum(gates, axis=1)
    block_total = running[:, -1]
    length = gates.shape[1]
    row_ids = lax.broadcasted_iota(jnp.int32, (length, length), 0)
    col_ids = lax.broadcasted_iota(jnp.int32, (length, length), 1)
    lower = (col_ids <= row_ids)[None]
    spread = jnp.where(lower, running[:, :, None] - running[:, None, :], 0.0)
    window_weight = jnp.where(lower, jnp.exp(spread), 0.0)
    tail_weight = jnp.exp(block_total[:, None] - running)
    return (jnp.exp(running), jnp.exp(block_total), tail_weight, window_weight)


def body(soft_q, soft_k, soft_v, soft_dout, lin_q, lin_k, lin_v, lin_gate, lin_dy):
    heads_here = lin_gate.shape[0]
    length = soft_q.shape[0]
    head_size = soft_q.shape[1] // heads_here
    factor = head_size ** (-0.5)
    position = lax.axis_index("ctx")
    has_prev = position > 0
    has_next = position < lax.axis_size("ctx") - 1
    shape_heads = (length, heads_here, head_size)
    shape_flat = (length, heads_here * head_size)
    row_ids = lax.broadcasted_iota(jnp.int32, (length, length), 0)
    col_ids = lax.broadcasted_iota(jnp.int32, (length, length), 1)
    own_mask = (col_ids <= row_ids)[None]
    prev_mask = ((col_ids > row_ids) & has_prev)[None]
    next_mask = ((col_ids > row_ids) & has_next)[None]

    lin_queries = lin_q.reshape(shape_heads)
    lin_keys = lin_k.reshape(shape_heads)
    lin_values = lin_v.reshape(shape_heads)
    query_f = lin_queries.astype(jnp.float32)
    key_f = lin_keys.astype(jnp.float32)
    value_f = lin_values.astype(jnp.float32)
    lead_weight, block_decay, tail_weight, window_weight = linear_parts(lin_gate)
    summary = jnp.einsum("hs,shd,she->hde", tail_weight, key_f, value_f, precision=exact_mode)

    def soft_sends(c):
        c = dict(c)
        pair_prev = shifted(jnp.stack((c["soft_k"], c["soft_v"])), "ctx", 1)
        pair_next = shifted(jnp.stack((c["soft_q"], c["soft_dout"])), "ctx", -1)
        c["keys_prev"] = pair_prev[0].reshape(shape_heads)
        c["values_prev"] = pair_prev[1].reshape(shape_heads)
        c["queries_next"] = pair_next[0].reshape(shape_heads)
        c["grad_out_next"] = pair_next[1].reshape(shape_heads)
        queries = c["soft_q"].reshape(shape_heads)
        keys_own = c["soft_k"].reshape(shape_heads)
        values_own = c["soft_v"].reshape(shape_heads)
        grad_out = c["soft_dout"].reshape(shape_heads)
        c["scores_own"] = (
            jnp.einsum("thd,shd->hts", queries, keys_own, preferred_element_type=jnp.float32)
            * factor
        )
        c["dprob_own"] = jnp.einsum(
            "thd,shd->hts", grad_out, values_own, preferred_element_type=jnp.float32
        )
        lin_scores = jnp.einsum(
            "thd,shd->hts", c["lin_q"].reshape(shape_heads), c["lin_k"].reshape(shape_heads),
            preferred_element_type=jnp.float32,
        )
        c["attended"] = (lin_scores * factor * c["window_weight"]).astype(jnp.bfloat16)
        c["lin_intra"] = jnp.einsum(
            "hts,she->the", c["attended"], c["lin_v"].reshape(shape_heads),
            preferred_element_type=jnp.float32,
        )
        return c

    def soft_stats(c):
        c = dict(c)
        queries = c["soft_q"].reshape(shape_heads)
        grad_out = c["soft_dout"].reshape(shape_heads)
        scores_own = c["scores_own"]
        dprob_own = c["dprob_own"]
        scores_prev = (
            jnp.einsum("thd,shd->hts", queries, c["keys_prev"], preferred_element_type=jnp.float32)
            * factor
        )
        row_max = jnp.maximum(
            jnp.max(jnp.where(own_mask, scores_own, masked_fill), axis=2),
            jnp.max(jnp.where(prev_mask, scores_prev, masked_fill), axis=2),
        )
        total = jnp.sum(jnp.where(own_mask, jnp.exp(scores_own - row_max[..., None]), 0.0), axis=2)
        total = total + jnp.sum(
            jnp.where(prev_mask, jnp.exp(scores_prev - row_max[..., None]), 0.0), axis=2
        )
        log_total = row_max + jnp.log(total)
        probs_own = jnp.where(own_mask, jnp.exp(scores_own - log_total[..., None]), 0.0)
        probs_prev = jnp.where(prev_mask, jnp.exp(scores_prev - log_total[..., None]), 0.0)
        dprob_prev = jnp.einsum(
            "thd,shd->hts", grad_out, c["values_prev"], preferred_element_type=jnp.float32
        )
        row_delta = jnp.sum(probs_own * dprob_own, axis=2) + jnp.sum(
            probs_prev * dprob_prev, axis=2
        )
        c["stats_next"] = shifted(jnp.stack((log_total, row_delta)), "ctx", -1)
        c["dscore_own"] = (probs_own * (dprob_own - row_delta[..., None])).astype(jnp.bfloat16)
        c["dscore_prev"] = (probs_prev * (dprob_prev - row_delta[..., None])).astype(jnp.bfloat16)
        c["probs_own_b"] = probs_own.astype(jnp.bfloat16)
        for name in ("scores_own", "dprob_own"):
            del c[name]
        return c

    def soft_grads(c):
        c = dict(c)
        queries = c["soft_q"].reshape(shape_heads)
        keys_own = c["soft_k"].reshape(shape_heads)
        grad_out = c["soft_dout"].reshape(shape_heads)
        c["grad_q"] = (
            jnp.einsum("hts,shd->thd", c["dscore_own"], keys_own, preferred_element_type=jnp.float32)
            + jnp.einsum(
                "hts,shd->thd", c["dscore_prev"], c["keys_prev"], preferred_element_type=jnp.float32
            )
        ) * factor
        c["grad_k"] = (
            jnp.einsum("hts,thd->shd", c["dscore_own"], queries, preferred_element_type=jnp.float32)
            * factor
        )
        c["grad_v"] = jnp.einsum(
            "hts,thd->shd", c["probs_own_b"], grad_out, preferred_element_type=jnp.float32
        )
        for name in ("dscore_own", "dscore_prev", "probs_own_b", "keys_prev", "values_prev"):
            del c[name]
        return c

    carry = dict(
        soft_q=soft_q, soft_k=soft_k, soft_v=soft_v, soft_dout=soft_dout,
        lin_q=lin_q, lin_k=lin_k, lin_v=lin_v, window_weight=window_weight,
    )
    state_in, carry = exclusive_scan(
        block_decay, summary, "ctx", False, (soft_sends, soft_stats, soft_grads), carry
    )

    lin_output = carry["lin_intra"] + factor * lead_weight.T[:, :, None] * jnp.einsum(
        "thd,hde->the", query_f, state_in, precision=exact_mode
    )
    dy_f = lin_dy.reshape(shape_heads).astype(jnp.float32)
    norm_sums = lax.psum(
        (jnp.sum(lin_output * lin_output, axis=(1, 2)), jnp.sum(lin_output * dy_f, axis=(1, 2))),
        "head",
    )
    width_all = LOCAL_HEADS * HEAD_DIM
    rms_value = jnp.sqrt(norm_sums[0] / width_all + 1e-06)
    lin_grad = (
        dy_f / rms_value[:, None, None]
        - lin_output * (norm_sums[1] / (rms_value**3 * width_all))[:, None, None]
    )
    lin_grad_b = lin_grad.astype(jnp.bfloat16)
    lin_grad_f = lin_grad_b.astype(jnp.float32)
    grad_summary = factor * jnp.einsum(
        "ht,thd,the->hde", lead_weight, query_f, lin_grad_f, precision=exact_mode
    )

    def linear_own(c):
        c = dict(c)
        grad_b = c["lin_grad_b"]
        grad_raw = jnp.einsum(
            "the,she->hts", grad_b, c["lin_v"].reshape(shape_heads),
            preferred_element_type=jnp.float32,
        )
        grad_scores = (grad_raw * factor * c["window_weight"]).astype(jnp.bfloat16)
        lin_grad_q = jnp.einsum(
            "hts,shd->thd", grad_scores, c["lin_k"].reshape(shape_heads),
            preferred_element_type=jnp.float32,
        )
        lin_grad_q = lin_grad_q + factor * c["lead_weight"].T[:, :, None] * jnp.einsum(
            "hde,the->thd", c["state_in"], grad_b.astype(jnp.float32), precision=exact_mode
        )
        c["lin_dq"] = lin_grad_q.astype(jnp.bfloat16).reshape(shape_flat)
        c["lin_dk"] = jnp.einsum(
            "hts,thd->shd", grad_scores, c["lin_q"].reshape(shape_heads),
            preferred_element_type=jnp.float32,
        )
        c["lin_dv"] = jnp.einsum(
            "hts,the->she", c["attended"], grad_b, preferred_element_type=jnp.float32
        )
        for name in ("lin_grad_b", "state_in", "lead_weight", "attended", "window_weight"):
            del c[name]
        return c

    def soft_next_scores(c):
        c = dict(c)
        keys_own = c["soft_k"].reshape(shape_heads)
        values_own = c["soft_v"].reshape(shape_heads)
        stats_next = c["stats_next"]
        scores_next = (
            jnp.einsum(
                "thd,shd->hts", c["queries_next"], keys_own, preferred_element_type=jnp.float32
            )
            * factor
        )
        probs_next = jnp.where(next_mask, jnp.exp(scores_next - stats_next[0][..., None]), 0.0)
        dprob_next = jnp.einsum(
            "thd,shd->hts", c["grad_out_next"], values_own, preferred_element_type=jnp.float32
        )
        c["dscore_next"] = (probs_next * (dprob_next - stats_next[1][..., None])).astype(
            jnp.bfloat16
        )
        c["probs_next_b"] = probs_next.astype(jnp.bfloat16)
        return c

    def soft_next_grads(c):
        c = dict(c)
        grad_k = c["grad_k"] + (
            jnp.einsum(
                "hts,thd->shd", c["dscore_next"], c["queries_next"],
                preferred_element_type=jnp.float32,
            )
            * factor
        )
        grad_v = c["grad_v"] + jnp.einsum(
            "hts,thd->shd", c["probs_next_b"], c["grad_out_next"],
            preferred_element_type=jnp.float32,
        )
        c["soft_dk"] = grad_k.astype(jnp.bfloat16).reshape(shape_flat)
        c["soft_dv"] = grad_v.astype(jnp.bfloat16).reshape(shape_flat)
        return c

    late = dict(
        lin_grad_b=lin_grad_b, state_in=state_in, lead_weight=lead_weight,
        attended=carry["attended"], window_weight=window_weight,
        lin_q=lin_q, lin_k=lin_k, lin_v=lin_v,
        soft_k=soft_k, soft_v=soft_v, stats_next=carry["stats_next"],
        queries_next=carry["queries_next"], grad_out_next=carry["grad_out_next"],
        grad_k=carry["grad_k"], grad_v=carry["grad_v"],
    )
    grad_in, late = exclusive_scan(
        block_decay, grad_summary, "ctx", True, (linear_own, soft_next_scores, soft_next_grads),
        late,
    )
    lin_grad_k = late["lin_dk"] + tail_weight.T[:, :, None] * jnp.einsum(
        "hde,she->shd", grad_in, value_f, precision=exact_mode
    )
    lin_grad_v = late["lin_dv"] + tail_weight.T[:, :, None] * jnp.einsum(
        "hde,shd->she", grad_in, key_f, precision=exact_mode
    )
    return (
        carry["grad_q"].astype(jnp.bfloat16).reshape(shape_flat),
        late["soft_dk"],
        late["soft_dv"],
        late["lin_dq"],
        lin_grad_k.astype(jnp.bfloat16).reshape(shape_flat),
        lin_grad_v.astype(jnp.bfloat16).reshape(shape_flat),
    )


def solution(mesh):
    in_specs = (
        P("ctx", "head"),
        P("ctx", "head"),
        P("ctx", "head"),
        P("ctx", "head"),
        P("ctx", "head"),
        P("ctx", "head"),
        P("ctx", "head"),
        P("head", "ctx"),
        P("ctx", "head"),
    )
    out_specs = (
        P("ctx", "head"),
        P("ctx", "head"),
        P("ctx", "head"),
        P("ctx", "head"),
        P("ctx", "head"),
        P("ctx", "head"),
    )
    return jax.shard_map(body, mesh=mesh, in_specs=in_specs, out_specs=out_specs, check_vma=False)
```

```python
import jax
import jax.numpy as jnp
from jax import lax
from jax.sharding import PartitionSpec as P

LOCAL_HEADS = 16
HEAD_DIM = 128


masked_fill = -1e30
exact_mode = lax.Precision.HIGHEST


def shifted(x, axis, by):
    peers = lax.axis_size(axis)
    pairs = [(i, i + by) for i in range(peers) if 0 <= i + by < peers]
    return lax.ppermute(x, axis, pairs)


def exclusive_scan(decay, value, axis, reverse, stages=(), carry=()):
    count = lax.axis_size(axis)
    heads, size, width = value.shape
    win_value, win_decay = value, decay
    res_value, res_decay = jnp.zeros_like(value), jnp.ones_like(decay)
    step = 1
    turn = 0
    while step < count:
        send = jnp.concatenate(
            [win_value, jnp.broadcast_to(win_decay[:, None, None], (heads, 8, width))], axis=1
        ).astype(jnp.bfloat16)
        if turn < len(stages):
            send, carry = lax.optimization_barrier((send, carry))
        got = shifted(send, axis, -step if reverse else step)
        if turn < len(stages):
            carry = stages[turn](carry)
        got_value = got[:, :size].astype(jnp.float32)
        got_decay = got[:, size, 0].astype(jnp.float32)
        win_value = win_value + win_decay[:, None, None] * got_value
        res_value = res_value + res_decay[:, None, None] * got_value
        win_decay = win_decay * got_decay
        res_decay = res_decay * got_decay
        step *= 2
        turn += 1
    for stage in stages[turn:]:
        carry = stage(carry)
    return res_value, carry


def linear_parts(gates):
    running = jnp.cumsum(gates, axis=1)
    block_total = running[:, -1]
    length = gates.shape[1]
    row_ids = lax.broadcasted_iota(jnp.int32, (length, length), 0)
    col_ids = lax.broadcasted_iota(jnp.int32, (length, length), 1)
    lower = (col_ids <= row_ids)[None]
    spread = jnp.where(lower, running[:, :, None] - running[:, None, :], 0.0)
    window_weight = jnp.where(lower, jnp.exp(spread), 0.0)
    tail_weight = jnp.exp(block_total[:, None] - running)
    return (jnp.exp(running), jnp.exp(block_total), tail_weight, window_weight)


def body(soft_q, soft_k, soft_v, soft_dout, lin_q, lin_k, lin_v, lin_gate, lin_dy):
    heads_here = lin_gate.shape[0]
    length = soft_q.shape[0]
    head_size = soft_q.shape[1] // heads_here
    factor = head_size ** (-0.5)
    position = lax.axis_index("ctx")
    has_prev = position > 0
    has_next = position < lax.axis_size("ctx") - 1
    shape_heads = (length, heads_here, head_size)
    shape_flat = (length, heads_here * head_size)
    row_ids = lax.broadcasted_iota(jnp.int32, (length, length), 0)
    col_ids = lax.broadcasted_iota(jnp.int32, (length, length), 1)
    own_mask = (col_ids <= row_ids)[None]
    prev_mask = ((col_ids > row_ids) & has_prev)[None]
    next_mask = ((col_ids > row_ids) & has_next)[None]

    lin_queries = lin_q.reshape(shape_heads)
    lin_keys = lin_k.reshape(shape_heads)
    lin_values = lin_v.reshape(shape_heads)
    query_f = lin_queries.astype(jnp.float32)
    key_f = lin_keys.astype(jnp.float32)
    value_f = lin_values.astype(jnp.float32)
    lead_weight, block_decay, tail_weight, window_weight = linear_parts(lin_gate)
    summary = jnp.einsum("hs,shd,she->hde", tail_weight, key_f, value_f, precision=exact_mode)

    def cols(array, head):
        return array[:, head * head_size:(head + 1) * head_size]

    def mm(a, b):
        return lax.dot_general(a, b, (((1,), (1,)), ((), ())), preferred_element_type=jnp.float32)

    def mm_t(a, b):
        return lax.dot_general(a, b, (((0,), (0,)), ((), ())), preferred_element_type=jnp.float32)

    def mm_n(a, b):
        return lax.dot_general(a, b, (((1,), (0,)), ((), ())), preferred_element_type=jnp.float32)

    own_mask2 = own_mask[0]
    prev_mask2 = prev_mask[0]
    next_mask2 = next_mask[0]
    heads_list = range(heads_here)

    def soft_sends(c):
        c = dict(c)
        c["pair_prev"] = shifted(jnp.stack((c["soft_k"], c["soft_v"])), "ctx", 1)
        c["pair_next"] = shifted(jnp.stack((c["soft_q"], c["soft_dout"])), "ctx", -1)
        c["scores_own"] = [mm(cols(c["soft_q"], h), cols(c["soft_k"], h)) * factor for h in heads_list]
        c["dprob_own"] = [mm(cols(c["soft_dout"], h), cols(c["soft_v"], h)) for h in heads_list]
        lin_scores = jnp.einsum(
            "thd,shd->hts", c["lin_q"].reshape(shape_heads), c["lin_k"].reshape(shape_heads),
            preferred_element_type=jnp.float32,
        )
        c["attended"] = (lin_scores * factor * c["window_weight"]).astype(jnp.bfloat16)
        c["lin_intra"] = jnp.einsum(
            "hts,she->the", c["attended"], c["lin_v"].reshape(shape_heads),
            preferred_element_type=jnp.float32,
        )
        return c

    def soft_stats(c):
        c = dict(c)
        keys_prev, values_prev = c["pair_prev"][0], c["pair_prev"][1]
        lts, deltas, ds_own, ds_prev, p_own = [], [], [], [], []
        for h in heads_list:
            scores_own = c["scores_own"][h]
            dprob_own = c["dprob_own"][h]
            scores_prev = mm(cols(c["soft_q"], h), cols(keys_prev, h)) * factor
            row_max = jnp.maximum(
                jnp.max(jnp.where(own_mask2, scores_own, masked_fill), axis=1),
                jnp.max(jnp.where(prev_mask2, scores_prev, masked_fill), axis=1),
            )
            total = jnp.sum(
                jnp.where(own_mask2, jnp.exp(scores_own - row_max[:, None]), 0.0), axis=1
            )
            total = total + jnp.sum(
                jnp.where(prev_mask2, jnp.exp(scores_prev - row_max[:, None]), 0.0), axis=1
            )
            log_total = row_max + jnp.log(total)
            probs_own = jnp.where(own_mask2, jnp.exp(scores_own - log_total[:, None]), 0.0)
            probs_prev = jnp.where(prev_mask2, jnp.exp(scores_prev - log_total[:, None]), 0.0)
            dprob_prev = mm(cols(c["soft_dout"], h), cols(values_prev, h))
            row_delta = jnp.sum(probs_own * dprob_own, axis=1) + jnp.sum(
                probs_prev * dprob_prev, axis=1
            )
            lts.append(log_total)
            deltas.append(row_delta)
            ds_own.append((probs_own * (dprob_own - row_delta[:, None])).astype(jnp.bfloat16))
            ds_prev.append((probs_prev * (dprob_prev - row_delta[:, None])).astype(jnp.bfloat16))
            p_own.append(probs_own.astype(jnp.bfloat16))
        c["stats_next"] = shifted(jnp.stack((jnp.stack(lts), jnp.stack(deltas))), "ctx", -1)
        c["dscore_own"], c["dscore_prev"], c["probs_own_b"] = ds_own, ds_prev, p_own
        for name in ("scores_own", "dprob_own"):
            del c[name]
        return c

    def soft_grads(c):
        c = dict(c)
        keys_prev = c["pair_prev"][0]
        dq, dk, dv = [], [], []
        for h in heads_list:
            dq.append(
                (mm_n(c["dscore_own"][h], cols(c["soft_k"], h))
                 + mm_n(c["dscore_prev"][h], cols(keys_prev, h))) * factor
            )
            dk.append(mm_t(c["dscore_own"][h], cols(c["soft_q"], h)) * factor)
            dv.append(mm_t(c["probs_own_b"][h], cols(c["soft_dout"], h)))
        c["grad_q"] = jnp.concatenate(dq, axis=1)
        c["grad_k"] = dk
        c["grad_v"] = dv
        for name in ("dscore_own", "dscore_prev", "probs_own_b", "pair_prev"):
            del c[name]
        return c

    carry = dict(
        soft_q=soft_q, soft_k=soft_k, soft_v=soft_v, soft_dout=soft_dout,
        lin_q=lin_q, lin_k=lin_k, lin_v=lin_v, window_weight=window_weight,
    )
    state_in, carry = exclusive_scan(
        block_decay, summary, "ctx", False, (soft_sends, soft_stats, soft_grads), carry
    )

    lin_output = carry["lin_intra"] + factor * lead_weight.T[:, :, None] * jnp.einsum(
        "thd,hde->the", query_f, state_in, precision=exact_mode
    )
    dy_f = lin_dy.reshape(shape_heads).astype(jnp.float32)
    norm_sums = lax.psum(
        (jnp.sum(lin_output * lin_output, axis=(1, 2)), jnp.sum(lin_output * dy_f, axis=(1, 2))),
        "head",
    )
    width_all = LOCAL_HEADS * HEAD_DIM
    rms_value = jnp.sqrt(norm_sums[0] / width_all + 1e-06)
    lin_grad = (
        dy_f / rms_value[:, None, None]
        - lin_output * (norm_sums[1] / (rms_value**3 * width_all))[:, None, None]
    )
    lin_grad_b = lin_grad.astype(jnp.bfloat16)
    lin_grad_f = lin_grad_b.astype(jnp.float32)
    grad_summary = factor * jnp.einsum(
        "ht,thd,the->hde", lead_weight, query_f, lin_grad_f, precision=exact_mode
    )

    def linear_own(c):
        c = dict(c)
        grad_b = c["lin_grad_b"]
        grad_raw = jnp.einsum(
            "the,she->hts", grad_b, c["lin_v"].reshape(shape_heads),
            preferred_element_type=jnp.float32,
        )
        grad_scores = (grad_raw * factor * c["window_weight"]).astype(jnp.bfloat16)
        lin_grad_q = jnp.einsum(
            "hts,shd->thd", grad_scores, c["lin_k"].reshape(shape_heads),
            preferred_element_type=jnp.float32,
        )
        lin_grad_q = lin_grad_q + factor * c["lead_weight"].T[:, :, None] * jnp.einsum(
            "hde,the->thd", c["state_in"], grad_b.astype(jnp.float32), precision=exact_mode
        )
        c["lin_dq"] = lin_grad_q.astype(jnp.bfloat16).reshape(shape_flat)
        c["lin_dk"] = jnp.einsum(
            "hts,thd->shd", grad_scores, c["lin_q"].reshape(shape_heads),
            preferred_element_type=jnp.float32,
        )
        c["lin_dv"] = jnp.einsum(
            "hts,the->she", c["attended"], grad_b, preferred_element_type=jnp.float32
        )
        for name in ("lin_grad_b", "state_in", "lead_weight", "attended", "window_weight"):
            del c[name]
        return c

    def soft_next_scores(c):
        c = dict(c)
        queries_next, grad_out_next = c["pair_next"][0], c["pair_next"][1]
        stats_next = c["stats_next"]
        ds_next, p_next = [], []
        for h in heads_list:
            scores_next = mm(cols(queries_next, h), cols(c["soft_k"], h)) * factor
            probs_next = jnp.where(
                next_mask2, jnp.exp(scores_next - stats_next[0, h][:, None]), 0.0
            )
            dprob_next = mm(cols(grad_out_next, h), cols(c["soft_v"], h))
            ds_next.append(
                (probs_next * (dprob_next - stats_next[1, h][:, None])).astype(jnp.bfloat16)
            )
            p_next.append(probs_next.astype(jnp.bfloat16))
        c["dscore_next"], c["probs_next_b"] = ds_next, p_next
        return c

    def soft_next_grads(c):
        c = dict(c)
        queries_next, grad_out_next = c["pair_next"][0], c["pair_next"][1]
        dk, dv = [], []
        for h in heads_list:
            dk.append(
                c["grad_k"][h] + mm_t(c["dscore_next"][h], cols(queries_next, h)) * factor
            )
            dv.append(c["grad_v"][h] + mm_t(c["probs_next_b"][h], cols(grad_out_next, h)))
        c["soft_dk"] = jnp.concatenate(dk, axis=1).astype(jnp.bfloat16)
        c["soft_dv"] = jnp.concatenate(dv, axis=1).astype(jnp.bfloat16)
        return c

    late = dict(
        lin_grad_b=lin_grad_b, state_in=state_in, lead_weight=lead_weight,
        attended=carry["attended"], window_weight=window_weight,
        lin_q=lin_q, lin_k=lin_k, lin_v=lin_v,
        soft_k=soft_k, soft_v=soft_v, stats_next=carry["stats_next"],
        pair_next=carry["pair_next"],
        grad_k=carry["grad_k"], grad_v=carry["grad_v"],
    )
    grad_in, late = exclusive_scan(
        block_decay, grad_summary, "ctx", True, (linear_own, soft_next_scores, soft_next_grads),
        late,
    )
    lin_grad_k = late["lin_dk"] + tail_weight.T[:, :, None] * jnp.einsum(
        "hde,she->shd", grad_in, value_f, precision=exact_mode
    )
    lin_grad_v = late["lin_dv"] + tail_weight.T[:, :, None] * jnp.einsum(
        "hde,shd->she", grad_in, key_f, precision=exact_mode
    )
    return (
        carry["grad_q"].astype(jnp.bfloat16),
        late["soft_dk"],
        late["soft_dv"],
        late["lin_dq"],
        lin_grad_k.astype(jnp.bfloat16).reshape(shape_flat),
        lin_grad_v.astype(jnp.bfloat16).reshape(shape_flat),
    )


def solution(mesh):
    in_specs = (
        P("ctx", "head"),
        P("ctx", "head"),
        P("ctx", "head"),
        P("ctx", "head"),
        P("ctx", "head"),
        P("ctx", "head"),
        P("ctx", "head"),
        P("head", "ctx"),
        P("ctx", "head"),
    )
    out_specs = (
        P("ctx", "head"),
        P("ctx", "head"),
        P("ctx", "head"),
        P("ctx", "head"),
        P("ctx", "head"),
        P("ctx", "head"),
    )
    return jax.shard_map(body, mesh=mesh, in_specs=in_specs, out_specs=out_specs, check_vma=False)
```

```python
import jax
import jax.numpy as jnp
from jax import lax
from jax.sharding import PartitionSpec as P

LOCAL_HEADS = 16
HEAD_DIM = 128


masked_fill = -1e30
exact_mode = lax.Precision.HIGHEST


def shifted(x, axis, by):
    peers = lax.axis_size(axis)
    pairs = [(i, i + by) for i in range(peers) if 0 <= i + by < peers]
    return lax.ppermute(x, axis, pairs)


def exclusive_scan(decay, value, axis, reverse, stages=(), carry=()):
    count = lax.axis_size(axis)
    heads, size, width = value.shape
    win_value, win_decay = value, decay
    res_value, res_decay = jnp.zeros_like(value), jnp.ones_like(decay)
    step = 1
    turn = 0
    while step < count:
        send = jnp.concatenate(
            [win_value, jnp.broadcast_to(win_decay[:, None, None], (heads, 8, width))], axis=1
        ).astype(jnp.bfloat16)
        if turn < len(stages):
            send, carry = lax.optimization_barrier((send, carry))
        got = shifted(send, axis, -step if reverse else step)
        if turn < len(stages):
            carry = stages[turn](carry)
        got_value = got[:, :size].astype(jnp.float32)
        got_decay = got[:, size, 0].astype(jnp.float32)
        win_value = win_value + win_decay[:, None, None] * got_value
        res_value = res_value + res_decay[:, None, None] * got_value
        win_decay = win_decay * got_decay
        res_decay = res_decay * got_decay
        step *= 2
        turn += 1
    for stage in stages[turn:]:
        carry = stage(carry)
    return res_value, carry


def linear_parts(gates):
    running = jnp.cumsum(gates, axis=1)
    block_total = running[:, -1]
    length = gates.shape[1]
    row_ids = lax.broadcasted_iota(jnp.int32, (length, length), 0)
    col_ids = lax.broadcasted_iota(jnp.int32, (length, length), 1)
    lower = (col_ids <= row_ids)[None]
    spread = jnp.where(lower, running[:, :, None] - running[:, None, :], 0.0)
    window_weight = jnp.where(lower, jnp.exp(spread), 0.0)
    tail_weight = jnp.exp(block_total[:, None] - running)
    return (jnp.exp(running), jnp.exp(block_total), tail_weight, window_weight)


def body(soft_q, soft_k, soft_v, soft_dout, lin_q, lin_k, lin_v, lin_gate, lin_dy):
    heads_here = lin_gate.shape[0]
    length = soft_q.shape[0]
    head_size = soft_q.shape[1] // heads_here
    factor = head_size ** (-0.5)
    position = lax.axis_index("ctx")
    has_prev = position > 0
    has_next = position < lax.axis_size("ctx") - 1
    shape_heads = (length, heads_here, head_size)
    shape_flat = (length, heads_here * head_size)
    row_ids = lax.broadcasted_iota(jnp.int32, (length, length), 0)
    col_ids = lax.broadcasted_iota(jnp.int32, (length, length), 1)
    own_mask = (col_ids <= row_ids)[None]
    prev_mask = ((col_ids > row_ids) & has_prev)[None]
    next_mask = ((col_ids > row_ids) & has_next)[None]

    lin_queries = lin_q.reshape(shape_heads)
    lin_keys = lin_k.reshape(shape_heads)
    lin_values = lin_v.reshape(shape_heads)
    query_f = lin_queries.astype(jnp.float32)
    key_f = lin_keys.astype(jnp.float32)
    value_f = lin_values.astype(jnp.float32)
    lead_weight, block_decay, tail_weight, window_weight = linear_parts(lin_gate)
    summary = jnp.einsum("hs,shd,she->hde", tail_weight, key_f, value_f, precision=exact_mode)

    def cols(array, head):
        return array[:, head * head_size:(head + 1) * head_size]

    def mm(a, b):
        return lax.dot_general(a, b, (((1,), (1,)), ((), ())), preferred_element_type=jnp.float32)

    def mm_t(a, b):
        return lax.dot_general(a, b, (((0,), (0,)), ((), ())), preferred_element_type=jnp.float32)

    def mm_n(a, b):
        return lax.dot_general(a, b, (((1,), (0,)), ((), ())), preferred_element_type=jnp.float32)

    own_mask2 = own_mask[0]
    prev_mask2 = prev_mask[0]
    next_mask2 = next_mask[0]
    heads_list = range(heads_here)

    received = {}

    def soft_sends(c):
        c = dict(c)
        received["prev"] = shifted(jnp.stack((c["soft_k"], c["soft_v"])), "ctx", 1)
        received["next"] = shifted(jnp.stack((c["soft_q"], c["soft_dout"])), "ctx", -1)
        c["scores_own"] = [mm(cols(c["soft_q"], h), cols(c["soft_k"], h)) * factor for h in heads_list]
        c["dprob_own"] = [mm(cols(c["soft_dout"], h), cols(c["soft_v"], h)) for h in heads_list]
        lin_scores = jnp.einsum(
            "thd,shd->hts", c["lin_q"].reshape(shape_heads), c["lin_k"].reshape(shape_heads),
            preferred_element_type=jnp.float32,
        )
        c["attended"] = (lin_scores * factor * c["window_weight"]).astype(jnp.bfloat16)
        c["lin_intra"] = jnp.einsum(
            "hts,she->the", c["attended"], c["lin_v"].reshape(shape_heads),
            preferred_element_type=jnp.float32,
        )
        return c

    def soft_stats(c):
        c = dict(c)
        keys_prev, values_prev = received["prev"][0], received["prev"][1]
        lts, deltas, ds_own, ds_prev, p_own = [], [], [], [], []
        for h in heads_list:
            scores_own = c["scores_own"][h]
            dprob_own = c["dprob_own"][h]
            scores_prev = mm(cols(c["soft_q"], h), cols(keys_prev, h)) * factor
            row_max = jnp.maximum(
                jnp.max(jnp.where(own_mask2, scores_own, masked_fill), axis=1),
                jnp.max(jnp.where(prev_mask2, scores_prev, masked_fill), axis=1),
            )
            total = jnp.sum(
                jnp.where(own_mask2, jnp.exp(scores_own - row_max[:, None]), 0.0), axis=1
            )
            total = total + jnp.sum(
                jnp.where(prev_mask2, jnp.exp(scores_prev - row_max[:, None]), 0.0), axis=1
            )
            log_total = row_max + jnp.log(total)
            probs_own = jnp.where(own_mask2, jnp.exp(scores_own - log_total[:, None]), 0.0)
            probs_prev = jnp.where(prev_mask2, jnp.exp(scores_prev - log_total[:, None]), 0.0)
            dprob_prev = mm(cols(c["soft_dout"], h), cols(values_prev, h))
            row_delta = jnp.sum(probs_own * dprob_own, axis=1) + jnp.sum(
                probs_prev * dprob_prev, axis=1
            )
            lts.append(log_total)
            deltas.append(row_delta)
            ds_own.append((probs_own * (dprob_own - row_delta[:, None])).astype(jnp.bfloat16))
            ds_prev.append((probs_prev * (dprob_prev - row_delta[:, None])).astype(jnp.bfloat16))
            p_own.append(probs_own.astype(jnp.bfloat16))
        received["stats"] = shifted(jnp.stack((jnp.stack(lts), jnp.stack(deltas))), "ctx", -1)
        c["dscore_own"], c["dscore_prev"], c["probs_own_b"] = ds_own, ds_prev, p_own
        for name in ("scores_own", "dprob_own"):
            del c[name]
        return c

    def soft_grads(c):
        c = dict(c)
        keys_prev = received["prev"][0]
        dq, dk, dv = [], [], []
        for h in heads_list:
            dq.append(
                (mm_n(c["dscore_own"][h], cols(c["soft_k"], h))
                 + mm_n(c["dscore_prev"][h], cols(keys_prev, h))) * factor
            )
            dk.append(mm_t(c["dscore_own"][h], cols(c["soft_q"], h)) * factor)
            dv.append(mm_t(c["probs_own_b"][h], cols(c["soft_dout"], h)))
        c["grad_q"] = jnp.concatenate(dq, axis=1)
        c["grad_k"] = dk
        c["grad_v"] = dv
        for name in ("dscore_own", "dscore_prev", "probs_own_b"):
            del c[name]
        return c

    carry = dict(
        soft_q=soft_q, soft_k=soft_k, soft_v=soft_v, soft_dout=soft_dout,
        lin_q=lin_q, lin_k=lin_k, lin_v=lin_v, window_weight=window_weight,
    )
    state_in, carry = exclusive_scan(
        block_decay, summary, "ctx", False, (soft_sends, soft_stats, soft_grads), carry
    )

    lin_output = carry["lin_intra"] + factor * lead_weight.T[:, :, None] * jnp.einsum(
        "thd,hde->the", query_f, state_in, precision=exact_mode
    )
    dy_f = lin_dy.reshape(shape_heads).astype(jnp.float32)
    norm_sums = lax.psum(
        (jnp.sum(lin_output * lin_output, axis=(1, 2)), jnp.sum(lin_output * dy_f, axis=(1, 2))),
        "head",
    )
    width_all = LOCAL_HEADS * HEAD_DIM
    rms_value = jnp.sqrt(norm_sums[0] / width_all + 1e-06)
    lin_grad = (
        dy_f / rms_value[:, None, None]
        - lin_output * (norm_sums[1] / (rms_value**3 * width_all))[:, None, None]
    )
    lin_grad_b = lin_grad.astype(jnp.bfloat16)
    lin_grad_f = lin_grad_b.astype(jnp.float32)
    grad_summary = factor * jnp.einsum(
        "ht,thd,the->hde", lead_weight, query_f, lin_grad_f, precision=exact_mode
    )

    def linear_own(c):
        c = dict(c)
        grad_b = c["lin_grad_b"]
        grad_raw = jnp.einsum(
            "the,she->hts", grad_b, c["lin_v"].reshape(shape_heads),
            preferred_element_type=jnp.float32,
        )
        grad_scores = (grad_raw * factor * c["window_weight"]).astype(jnp.bfloat16)
        lin_grad_q = jnp.einsum(
            "hts,shd->thd", grad_scores, c["lin_k"].reshape(shape_heads),
            preferred_element_type=jnp.float32,
        )
        lin_grad_q = lin_grad_q + factor * c["lead_weight"].T[:, :, None] * jnp.einsum(
            "hde,the->thd", c["state_in"], grad_b.astype(jnp.float32), precision=exact_mode
        )
        c["lin_dq"] = lin_grad_q.astype(jnp.bfloat16).reshape(shape_flat)
        c["lin_dk"] = jnp.einsum(
            "hts,thd->shd", grad_scores, c["lin_q"].reshape(shape_heads),
            preferred_element_type=jnp.float32,
        )
        c["lin_dv"] = jnp.einsum(
            "hts,the->she", c["attended"], grad_b, preferred_element_type=jnp.float32
        )
        for name in ("lin_grad_b", "state_in", "lead_weight", "attended", "window_weight"):
            del c[name]
        return c

    def soft_next_scores(c):
        c = dict(c)
        queries_next, grad_out_next = received["next"][0], received["next"][1]
        stats_next = received["stats"]
        ds_next, p_next = [], []
        for h in heads_list:
            scores_next = mm(cols(queries_next, h), cols(c["soft_k"], h)) * factor
            probs_next = jnp.where(
                next_mask2, jnp.exp(scores_next - stats_next[0, h][:, None]), 0.0
            )
            dprob_next = mm(cols(grad_out_next, h), cols(c["soft_v"], h))
            ds_next.append(
                (probs_next * (dprob_next - stats_next[1, h][:, None])).astype(jnp.bfloat16)
            )
            p_next.append(probs_next.astype(jnp.bfloat16))
        c["dscore_next"], c["probs_next_b"] = ds_next, p_next
        return c

    def soft_next_grads(c):
        c = dict(c)
        queries_next, grad_out_next = received["next"][0], received["next"][1]
        dk, dv = [], []
        for h in heads_list:
            dk.append(
                c["grad_k"][h] + mm_t(c["dscore_next"][h], cols(queries_next, h)) * factor
            )
            dv.append(c["grad_v"][h] + mm_t(c["probs_next_b"][h], cols(grad_out_next, h)))
        c["soft_dk"] = jnp.concatenate(dk, axis=1).astype(jnp.bfloat16)
        c["soft_dv"] = jnp.concatenate(dv, axis=1).astype(jnp.bfloat16)
        return c

    late = dict(
        lin_grad_b=lin_grad_b, state_in=state_in, lead_weight=lead_weight,
        attended=carry["attended"], window_weight=window_weight,
        lin_q=lin_q, lin_k=lin_k, lin_v=lin_v,
        soft_k=soft_k, soft_v=soft_v,
        grad_k=carry["grad_k"], grad_v=carry["grad_v"],
    )
    grad_in, late = exclusive_scan(
        block_decay, grad_summary, "ctx", True, (linear_own, soft_next_scores, soft_next_grads),
        late,
    )
    lin_grad_k = late["lin_dk"] + tail_weight.T[:, :, None] * jnp.einsum(
        "hde,she->shd", grad_in, value_f, precision=exact_mode
    )
    lin_grad_v = late["lin_dv"] + tail_weight.T[:, :, None] * jnp.einsum(
        "hde,shd->she", grad_in, key_f, precision=exact_mode
    )
    return (
        carry["grad_q"].astype(jnp.bfloat16),
        late["soft_dk"],
        late["soft_dv"],
        late["lin_dq"],
        lin_grad_k.astype(jnp.bfloat16).reshape(shape_flat),
        lin_grad_v.astype(jnp.bfloat16).reshape(shape_flat),
    )


def solution(mesh):
    in_specs = (
        P("ctx", "head"),
        P("ctx", "head"),
        P("ctx", "head"),
        P("ctx", "head"),
        P("ctx", "head"),
        P("ctx", "head"),
        P("ctx", "head"),
        P("head", "ctx"),
        P("ctx", "head"),
    )
    out_specs = (
        P("ctx", "head"),
        P("ctx", "head"),
        P("ctx", "head"),
        P("ctx", "head"),
        P("ctx", "head"),
        P("ctx", "head"),
    )
    return jax.shard_map(body, mesh=mesh, in_specs=in_specs, out_specs=out_specs, check_vma=False)
```

```python
import jax
import jax.numpy as jnp
from jax import lax
from jax.sharding import PartitionSpec as P

LOCAL_HEADS = 16
HEAD_DIM = 128


masked_fill = -1e30
exact_mode = lax.Precision.HIGHEST


def shifted(x, axis, by):
    peers = lax.axis_size(axis)
    pairs = [(i, i + by) for i in range(peers) if 0 <= i + by < peers]
    return lax.ppermute(x, axis, pairs)


def exclusive_scan(decay, value, axis, reverse, stages=(), carry=()):
    count = lax.axis_size(axis)
    heads, size, width = value.shape
    win_value, win_decay = value, decay
    res_value, res_decay = jnp.zeros_like(value), jnp.ones_like(decay)
    step = 1
    turn = 0
    while step < count:
        send = jnp.concatenate(
            [win_value, jnp.broadcast_to(win_decay[:, None, None], (heads, 8, width))], axis=1
        ).astype(jnp.bfloat16)
        if turn < len(stages):
            send, carry = lax.optimization_barrier((send, carry))
        got = shifted(send, axis, -step if reverse else step)
        if turn < len(stages):
            carry = stages[turn](carry)
        got_value = got[:, :size].astype(jnp.float32)
        got_decay = got[:, size, 0].astype(jnp.float32)
        win_value = win_value + win_decay[:, None, None] * got_value
        res_value = res_value + res_decay[:, None, None] * got_value
        win_decay = win_decay * got_decay
        res_decay = res_decay * got_decay
        step *= 2
        turn += 1
    for stage in stages[turn:]:
        carry = stage(carry)
    return res_value, carry


def linear_parts(gates):
    running = jnp.cumsum(gates, axis=1)
    block_total = running[:, -1]
    length = gates.shape[1]
    row_ids = lax.broadcasted_iota(jnp.int32, (length, length), 0)
    col_ids = lax.broadcasted_iota(jnp.int32, (length, length), 1)
    lower = (col_ids <= row_ids)[None]
    spread = jnp.where(lower, running[:, :, None] - running[:, None, :], 0.0)
    window_weight = jnp.where(lower, jnp.exp(spread), 0.0)
    tail_weight = jnp.exp(block_total[:, None] - running)
    return (jnp.exp(running), jnp.exp(block_total), tail_weight, window_weight)


def body(soft_q, soft_k, soft_v, soft_dout, lin_q, lin_k, lin_v, lin_gate, lin_dy):
    heads_here = lin_gate.shape[0]
    length = soft_q.shape[0]
    head_size = soft_q.shape[1] // heads_here
    factor = head_size ** (-0.5)
    position = lax.axis_index("ctx")
    has_prev = position > 0
    has_next = position < lax.axis_size("ctx") - 1
    shape_heads = (length, heads_here, head_size)
    shape_flat = (length, heads_here * head_size)
    row_ids = lax.broadcasted_iota(jnp.int32, (length, length), 0)
    col_ids = lax.broadcasted_iota(jnp.int32, (length, length), 1)
    own_mask = (col_ids <= row_ids)[None]
    prev_mask = ((col_ids > row_ids) & has_prev)[None]
    next_mask = ((col_ids > row_ids) & has_next)[None]

    lin_queries = lin_q.reshape(shape_heads)
    lin_keys = lin_k.reshape(shape_heads)
    lin_values = lin_v.reshape(shape_heads)
    query_f = lin_queries.astype(jnp.float32)
    key_f = lin_keys.astype(jnp.float32)
    value_f = lin_values.astype(jnp.float32)
    lead_weight, block_decay, tail_weight, window_weight = linear_parts(lin_gate)
    summary = jnp.einsum("hs,shd,she->hde", tail_weight, key_f, value_f, precision=exact_mode)

    def cols(array, head):
        return array[:, head * head_size:(head + 1) * head_size]

    def mm(a, b):
        return lax.dot_general(a, b, (((1,), (1,)), ((), ())), preferred_element_type=jnp.float32)

    def mm_t(a, b):
        return lax.dot_general(a, b, (((0,), (0,)), ((), ())), preferred_element_type=jnp.float32)

    def mm_n(a, b):
        return lax.dot_general(a, b, (((1,), (0,)), ((), ())), preferred_element_type=jnp.float32)

    own_mask2 = own_mask[0]
    prev_mask2 = prev_mask[0]
    next_mask2 = next_mask[0]
    heads_list = range(heads_here)

    received = {}

    def soft_sends(c):
        c = dict(c)
        received["prev"] = shifted(jnp.stack((c["soft_k"], c["soft_v"])), "ctx", 1)
        received["next"] = shifted(jnp.stack((c["soft_q"], c["soft_dout"])), "ctx", -1)
        for h in heads_list:
            c["scores_own%d" % h] = mm(cols(c["soft_q"], h), cols(c["soft_k"], h)) * factor
            c["dprob_own%d" % h] = mm(cols(c["soft_dout"], h), cols(c["soft_v"], h))
        lin_scores = jnp.einsum(
            "thd,shd->hts", c["lin_q"].reshape(shape_heads), c["lin_k"].reshape(shape_heads),
            preferred_element_type=jnp.float32,
        )
        c["attended"] = (lin_scores * factor * c["window_weight"]).astype(jnp.bfloat16)
        c["lin_intra"] = jnp.einsum(
            "hts,she->the", c["attended"], c["lin_v"].reshape(shape_heads),
            preferred_element_type=jnp.float32,
        )
        return c

    def soft_heads(part, last):
        def stage(c):
            c = dict(c)
            keys_prev, values_prev = received["prev"][0], received["prev"][1]
            for h in part:
                scores_own = c.pop("scores_own%d" % h)
                dprob_own = c.pop("dprob_own%d" % h)
                scores_prev = mm(cols(c["soft_q"], h), cols(keys_prev, h)) * factor
                row_max = jnp.maximum(
                    jnp.max(jnp.where(own_mask2, scores_own, masked_fill), axis=1),
                    jnp.max(jnp.where(prev_mask2, scores_prev, masked_fill), axis=1),
                )
                total = jnp.sum(
                    jnp.where(own_mask2, jnp.exp(scores_own - row_max[:, None]), 0.0), axis=1
                )
                total = total + jnp.sum(
                    jnp.where(prev_mask2, jnp.exp(scores_prev - row_max[:, None]), 0.0), axis=1
                )
                log_total = row_max + jnp.log(total)
                probs_own = jnp.where(own_mask2, jnp.exp(scores_own - log_total[:, None]), 0.0)
                probs_prev = jnp.where(
                    prev_mask2, jnp.exp(scores_prev - log_total[:, None]), 0.0
                )
                dprob_prev = mm(cols(c["soft_dout"], h), cols(values_prev, h))
                row_delta = jnp.sum(probs_own * dprob_own, axis=1) + jnp.sum(
                    probs_prev * dprob_prev, axis=1
                )
                ds_own = (probs_own * (dprob_own - row_delta[:, None])).astype(jnp.bfloat16)
                ds_prev = (probs_prev * (dprob_prev - row_delta[:, None])).astype(jnp.bfloat16)
                c["stat%d" % h] = jnp.stack((log_total, row_delta))
                c["dq%d" % h] = (
                    mm_n(ds_own, cols(c["soft_k"], h)) + mm_n(ds_prev, cols(keys_prev, h))
                ) * factor
                c["dk%d" % h] = mm_t(ds_own, cols(c["soft_q"], h)) * factor
                c["dv%d" % h] = mm_t(probs_own.astype(jnp.bfloat16), cols(c["soft_dout"], h))
            if last:
                received["stats"] = shifted(
                    jnp.stack([c.pop("stat%d" % h) for h in heads_list], axis=1), "ctx", -1
                )
                c["grad_q"] = jnp.concatenate([c.pop("dq%d" % h) for h in heads_list], axis=1)
                c["grad_k"] = [c.pop("dk%d" % h) for h in heads_list]
                c["grad_v"] = [c.pop("dv%d" % h) for h in heads_list]
            return c

        return stage

    split = (heads_here + 1) // 2
    soft_stats = soft_heads(heads_list[:split], False)
    soft_grads = soft_heads(heads_list[split:], True)

    carry = dict(
        soft_q=soft_q, soft_k=soft_k, soft_v=soft_v, soft_dout=soft_dout,
        lin_q=lin_q, lin_k=lin_k, lin_v=lin_v, window_weight=window_weight,
    )
    state_in, carry = exclusive_scan(
        block_decay, summary, "ctx", False, (soft_sends, soft_stats, soft_grads), carry
    )

    lin_output = carry["lin_intra"] + factor * lead_weight.T[:, :, None] * jnp.einsum(
        "thd,hde->the", query_f, state_in, precision=exact_mode
    )
    dy_f = lin_dy.reshape(shape_heads).astype(jnp.float32)
    norm_sums = lax.psum(
        (jnp.sum(lin_output * lin_output, axis=(1, 2)), jnp.sum(lin_output * dy_f, axis=(1, 2))),
        "head",
    )
    width_all = LOCAL_HEADS * HEAD_DIM
    rms_value = jnp.sqrt(norm_sums[0] / width_all + 1e-06)
    lin_grad = (
        dy_f / rms_value[:, None, None]
        - lin_output * (norm_sums[1] / (rms_value**3 * width_all))[:, None, None]
    )
    lin_grad_b = lin_grad.astype(jnp.bfloat16)
    lin_grad_f = lin_grad_b.astype(jnp.float32)
    grad_summary = factor * jnp.einsum(
        "ht,thd,the->hde", lead_weight, query_f, lin_grad_f, precision=exact_mode
    )

    def linear_own(c):
        c = dict(c)
        grad_b = c["lin_grad_b"]
        grad_raw = jnp.einsum(
            "the,she->hts", grad_b, c["lin_v"].reshape(shape_heads),
            preferred_element_type=jnp.float32,
        )
        grad_scores = (grad_raw * factor * c["window_weight"]).astype(jnp.bfloat16)
        lin_grad_q = jnp.einsum(
            "hts,shd->thd", grad_scores, c["lin_k"].reshape(shape_heads),
            preferred_element_type=jnp.float32,
        )
        lin_grad_q = lin_grad_q + factor * c["lead_weight"].T[:, :, None] * jnp.einsum(
            "hde,the->thd", c["state_in"], grad_b.astype(jnp.float32), precision=exact_mode
        )
        c["lin_dq"] = lin_grad_q.astype(jnp.bfloat16).reshape(shape_flat)
        c["lin_dk"] = jnp.einsum(
            "hts,thd->shd", grad_scores, c["lin_q"].reshape(shape_heads),
            preferred_element_type=jnp.float32,
        )
        c["lin_dv"] = jnp.einsum(
            "hts,the->she", c["attended"], grad_b, preferred_element_type=jnp.float32
        )
        for name in ("lin_grad_b", "state_in", "lead_weight", "attended", "window_weight"):
            del c[name]
        return c

    def soft_next_scores(c):
        c = dict(c)
        queries_next, grad_out_next = received["next"][0], received["next"][1]
        stats_next = received["stats"]
        ds_next, p_next = [], []
        for h in heads_list:
            scores_next = mm(cols(queries_next, h), cols(c["soft_k"], h)) * factor
            probs_next = jnp.where(
                next_mask2, jnp.exp(scores_next - stats_next[0, h][:, None]), 0.0
            )
            dprob_next = mm(cols(grad_out_next, h), cols(c["soft_v"], h))
            ds_next.append(
                (probs_next * (dprob_next - stats_next[1, h][:, None])).astype(jnp.bfloat16)
            )
            p_next.append(probs_next.astype(jnp.bfloat16))
        c["dscore_next"], c["probs_next_b"] = ds_next, p_next
        return c

    def soft_next_grads(c):
        c = dict(c)
        queries_next, grad_out_next = received["next"][0], received["next"][1]
        dk, dv = [], []
        for h in heads_list:
            dk.append(
                c["grad_k"][h] + mm_t(c["dscore_next"][h], cols(queries_next, h)) * factor
            )
            dv.append(c["grad_v"][h] + mm_t(c["probs_next_b"][h], cols(grad_out_next, h)))
        c["soft_dk"] = jnp.concatenate(dk, axis=1).astype(jnp.bfloat16)
        c["soft_dv"] = jnp.concatenate(dv, axis=1).astype(jnp.bfloat16)
        return c

    late = dict(
        lin_grad_b=lin_grad_b, state_in=state_in, lead_weight=lead_weight,
        attended=carry["attended"], window_weight=window_weight,
        lin_q=lin_q, lin_k=lin_k, lin_v=lin_v,
        soft_k=soft_k, soft_v=soft_v,
        grad_k=carry["grad_k"], grad_v=carry["grad_v"],
    )
    grad_in, late = exclusive_scan(
        block_decay, grad_summary, "ctx", True, (linear_own, soft_next_scores, soft_next_grads),
        late,
    )
    lin_grad_k = late["lin_dk"] + tail_weight.T[:, :, None] * jnp.einsum(
        "hde,she->shd", grad_in, value_f, precision=exact_mode
    )
    lin_grad_v = late["lin_dv"] + tail_weight.T[:, :, None] * jnp.einsum(
        "hde,shd->she", grad_in, key_f, precision=exact_mode
    )
    return (
        carry["grad_q"].astype(jnp.bfloat16),
        late["soft_dk"],
        late["soft_dv"],
        late["lin_dq"],
        lin_grad_k.astype(jnp.bfloat16).reshape(shape_flat),
        lin_grad_v.astype(jnp.bfloat16).reshape(shape_flat),
    )


def solution(mesh):
    in_specs = (
        P("ctx", "head"),
        P("ctx", "head"),
        P("ctx", "head"),
        P("ctx", "head"),
        P("ctx", "head"),
        P("ctx", "head"),
        P("ctx", "head"),
        P("head", "ctx"),
        P("ctx", "head"),
    )
    out_specs = (
        P("ctx", "head"),
        P("ctx", "head"),
        P("ctx", "head"),
        P("ctx", "head"),
        P("ctx", "head"),
        P("ctx", "head"),
    )
    return jax.shard_map(body, mesh=mesh, in_specs=in_specs, out_specs=out_specs, check_vma=False)
```

```python
import jax
import jax.numpy as jnp
from jax import lax
from jax.sharding import PartitionSpec as P

LOCAL_HEADS = 16
HEAD_DIM = 128


masked_fill = -1e30
exact_mode = lax.Precision.HIGHEST


def shifted(x, axis, by):
    peers = lax.axis_size(axis)
    pairs = [(i, i + by) for i in range(peers) if 0 <= i + by < peers]
    return lax.ppermute(x, axis, pairs)


def exclusive_scan(decay, value, axis, reverse, stages=(), carry=()):
    count = lax.axis_size(axis)
    heads, size, width = value.shape
    win_value, win_decay = value, decay
    res_value, res_decay = jnp.zeros_like(value), jnp.ones_like(decay)
    step = 1
    turn = 0
    while step < count:
        send = jnp.concatenate(
            [win_value, jnp.broadcast_to(win_decay[:, None, None], (heads, 8, width))], axis=1
        ).astype(jnp.bfloat16)
        if turn < len(stages):
            send, carry = lax.optimization_barrier((send, carry))
        got = shifted(send, axis, -step if reverse else step)
        if turn < len(stages):
            carry = stages[turn](carry)
        got_value = got[:, :size].astype(jnp.float32)
        got_decay = got[:, size, 0].astype(jnp.float32)
        win_value = win_value + win_decay[:, None, None] * got_value
        res_value = res_value + res_decay[:, None, None] * got_value
        win_decay = win_decay * got_decay
        res_decay = res_decay * got_decay
        step *= 2
        turn += 1
    for stage in stages[turn:]:
        carry = stage(carry)
    return res_value, carry


def linear_parts(gates):
    running = jnp.cumsum(gates, axis=1)
    block_total = running[:, -1]
    length = gates.shape[1]
    row_ids = lax.broadcasted_iota(jnp.int32, (length, length), 0)
    col_ids = lax.broadcasted_iota(jnp.int32, (length, length), 1)
    lower = (col_ids <= row_ids)[None]
    spread = jnp.where(lower, running[:, :, None] - running[:, None, :], 0.0)
    window_weight = jnp.where(lower, jnp.exp(spread), 0.0)
    tail_weight = jnp.exp(block_total[:, None] - running)
    return (jnp.exp(running), jnp.exp(block_total), tail_weight, window_weight)


def body(soft_q, soft_k, soft_v, soft_dout, lin_q, lin_k, lin_v, lin_gate, lin_dy):
    heads_here = lin_gate.shape[0]
    length = soft_q.shape[0]
    head_size = soft_q.shape[1] // heads_here
    factor = head_size ** (-0.5)
    position = lax.axis_index("ctx")
    has_prev = position > 0
    has_next = position < lax.axis_size("ctx") - 1
    shape_heads = (length, heads_here, head_size)
    shape_flat = (length, heads_here * head_size)
    row_ids = lax.broadcasted_iota(jnp.int32, (length, length), 0)
    col_ids = lax.broadcasted_iota(jnp.int32, (length, length), 1)
    own_mask = (col_ids <= row_ids)[None]
    prev_mask = ((col_ids > row_ids) & has_prev)[None]
    next_mask = ((col_ids > row_ids) & has_next)[None]

    lin_queries = lin_q.reshape(shape_heads)
    lin_keys = lin_k.reshape(shape_heads)
    lin_values = lin_v.reshape(shape_heads)
    query_f = lin_queries.astype(jnp.float32)
    key_f = lin_keys.astype(jnp.float32)
    value_f = lin_values.astype(jnp.float32)
    lead_weight, block_decay, tail_weight, window_weight = linear_parts(lin_gate)
    summary = jnp.einsum("hs,shd,she->hde", tail_weight, key_f, value_f, precision=exact_mode)

    def cols(array, head):
        return array[:, head * head_size:(head + 1) * head_size]

    def mm(a, b):
        return lax.dot_general(a, b, (((1,), (1,)), ((), ())), preferred_element_type=jnp.float32)

    def mm_t(a, b):
        return lax.dot_general(a, b, (((0,), (0,)), ((), ())), preferred_element_type=jnp.float32)

    def mm_n(a, b):
        return lax.dot_general(a, b, (((1,), (0,)), ((), ())), preferred_element_type=jnp.float32)

    own_mask2 = own_mask[0]
    prev_mask2 = prev_mask[0]
    next_mask2 = next_mask[0]
    heads_list = range(heads_here)

    received = {}

    def soft_sends(c):
        c = dict(c)
        received["prev"] = shifted(jnp.stack((c["soft_k"], c["soft_v"])), "ctx", 1)
        received["next"] = shifted(jnp.stack((c["soft_q"], c["soft_dout"])), "ctx", -1)
        for h in heads_list:
            c["scores_own%d" % h] = mm(cols(c["soft_q"], h), cols(c["soft_k"], h)) * factor
            c["dprob_own%d" % h] = mm(cols(c["soft_dout"], h), cols(c["soft_v"], h))
        lin_scores = jnp.einsum(
            "thd,shd->hts", c["lin_q"].reshape(shape_heads), c["lin_k"].reshape(shape_heads),
            preferred_element_type=jnp.float32,
        )
        c["attended"] = (lin_scores * factor * c["window_weight"]).astype(jnp.bfloat16)
        c["lin_intra"] = jnp.einsum(
            "hts,she->the", c["attended"], c["lin_v"].reshape(shape_heads),
            preferred_element_type=jnp.float32,
        )
        return c

    def soft_heads(part, last):
        def stage(c):
            c = dict(c)
            keys_prev, values_prev = received["prev"][0], received["prev"][1]
            for h in part:
                scores_own = c.pop("scores_own%d" % h)
                dprob_own = c.pop("dprob_own%d" % h)
                scores_prev = mm(cols(c["soft_q"], h), cols(keys_prev, h)) * factor
                row_max = jnp.maximum(
                    jnp.max(jnp.where(own_mask2, scores_own, masked_fill), axis=1),
                    jnp.max(jnp.where(prev_mask2, scores_prev, masked_fill), axis=1),
                )
                total = jnp.sum(
                    jnp.where(own_mask2, jnp.exp(scores_own - row_max[:, None]), 0.0), axis=1
                )
                total = total + jnp.sum(
                    jnp.where(prev_mask2, jnp.exp(scores_prev - row_max[:, None]), 0.0), axis=1
                )
                log_total = row_max + jnp.log(total)
                probs_own = jnp.where(own_mask2, jnp.exp(scores_own - log_total[:, None]), 0.0)
                probs_prev = jnp.where(
                    prev_mask2, jnp.exp(scores_prev - log_total[:, None]), 0.0
                )
                dprob_prev = mm(cols(c["soft_dout"], h), cols(values_prev, h))
                row_delta = jnp.sum(probs_own * dprob_own, axis=1) + jnp.sum(
                    probs_prev * dprob_prev, axis=1
                )
                ds_own = (probs_own * (dprob_own - row_delta[:, None])).astype(jnp.bfloat16)
                ds_prev = (probs_prev * (dprob_prev - row_delta[:, None])).astype(jnp.bfloat16)
                c["stat%d" % h] = jnp.stack((log_total, row_delta))
                c["dq%d" % h] = (
                    mm_n(ds_own, cols(c["soft_k"], h)) + mm_n(ds_prev, cols(keys_prev, h))
                ) * factor
                c["dk%d" % h] = mm_t(ds_own, cols(c["soft_q"], h)) * factor
                c["dv%d" % h] = mm_t(probs_own.astype(jnp.bfloat16), cols(c["soft_dout"], h))
            if last:
                received["stats"] = shifted(
                    jnp.stack([c.pop("stat%d" % h) for h in heads_list], axis=1), "ctx", -1
                )
                c["grad_q"] = jnp.concatenate([c.pop("dq%d" % h) for h in heads_list], axis=1)
                c["grad_k"] = [c.pop("dk%d" % h) for h in heads_list]
                c["grad_v"] = [c.pop("dv%d" % h) for h in heads_list]
            return c

        return stage

    split = (heads_here + 1) // 2
    soft_stats = soft_heads(heads_list[:split], False)
    soft_grads = soft_heads(heads_list[split:], True)

    carry = dict(
        soft_q=soft_q, soft_k=soft_k, soft_v=soft_v, soft_dout=soft_dout,
        lin_q=lin_q, lin_k=lin_k, lin_v=lin_v, window_weight=window_weight,
    )
    state_in, carry = exclusive_scan(
        block_decay, summary, "ctx", False, (soft_sends, soft_stats, soft_grads), carry
    )

    lin_output = carry["lin_intra"] + factor * lead_weight.T[:, :, None] * jnp.einsum(
        "thd,hde->the", query_f, state_in, precision=exact_mode
    )
    dy_f = lin_dy.reshape(shape_heads).astype(jnp.float32)
    norm_sums = lax.psum(
        (jnp.sum(lin_output * lin_output, axis=(1, 2)), jnp.sum(lin_output * dy_f, axis=(1, 2))),
        "head",
    )
    width_all = LOCAL_HEADS * HEAD_DIM
    rms_value = jnp.sqrt(norm_sums[0] / width_all + 1e-06)
    lin_grad = (
        dy_f / rms_value[:, None, None]
        - lin_output * (norm_sums[1] / (rms_value**3 * width_all))[:, None, None]
    )
    lin_grad_b = lin_grad.astype(jnp.bfloat16)
    lin_grad_f = lin_grad_b.astype(jnp.float32)
    grad_summary = factor * jnp.einsum(
        "ht,thd,the->hde", lead_weight, query_f, lin_grad_f, precision=exact_mode
    )

    def linear_own(c):
        c = dict(c)
        grad_b = c["lin_grad_b"]
        grad_raw = jnp.einsum(
            "the,she->hts", grad_b, c["lin_v"].reshape(shape_heads),
            preferred_element_type=jnp.float32,
        )
        grad_scores = (grad_raw * factor * c["window_weight"]).astype(jnp.bfloat16)
        lin_grad_q = jnp.einsum(
            "hts,shd->thd", grad_scores, c["lin_k"].reshape(shape_heads),
            preferred_element_type=jnp.float32,
        )
        lin_grad_q = lin_grad_q + factor * c["lead_weight"].T[:, :, None] * jnp.einsum(
            "hde,the->thd", c["state_in"], grad_b.astype(jnp.float32), precision=exact_mode
        )
        c["lin_dq"] = lin_grad_q.astype(jnp.bfloat16).reshape(shape_flat)
        c["lin_dk"] = jnp.einsum(
            "hts,thd->shd", grad_scores, c["lin_q"].reshape(shape_heads),
            preferred_element_type=jnp.float32,
        )
        c["lin_dv"] = jnp.einsum(
            "hts,the->she", c["attended"], grad_b, preferred_element_type=jnp.float32
        )
        for name in ("lin_grad_b", "state_in", "lead_weight", "attended", "window_weight"):
            del c[name]
        return c

    def soft_next_heads(part, last):
        def stage(c):
            c = dict(c)
            queries_next, grad_out_next = received["next"][0], received["next"][1]
            stats_next = received["stats"]
            for h in part:
                scores_next = mm(cols(queries_next, h), cols(c["soft_k"], h)) * factor
                probs_next = jnp.where(
                    next_mask2, jnp.exp(scores_next - stats_next[0, h][:, None]), 0.0
                )
                dprob_next = mm(cols(grad_out_next, h), cols(c["soft_v"], h))
                ds_next = (probs_next * (dprob_next - stats_next[1, h][:, None])).astype(
                    jnp.bfloat16
                )
                c["grad_k"][h] = (
                    c["grad_k"][h] + mm_t(ds_next, cols(queries_next, h)) * factor
                ).astype(jnp.bfloat16)
                c["grad_v"][h] = (
                    c["grad_v"][h]
                    + mm_t(probs_next.astype(jnp.bfloat16), cols(grad_out_next, h))
                ).astype(jnp.bfloat16)
            if last:
                c["soft_dk"] = jnp.concatenate(c.pop("grad_k"), axis=1)
                c["soft_dv"] = jnp.concatenate(c.pop("grad_v"), axis=1)
            return c

        return stage

    soft_next_scores = soft_next_heads(heads_list[:split], False)
    soft_next_grads = soft_next_heads(heads_list[split:], True)

    late = dict(
        lin_grad_b=lin_grad_b, state_in=state_in, lead_weight=lead_weight,
        attended=carry["attended"], window_weight=window_weight,
        lin_q=lin_q, lin_k=lin_k, lin_v=lin_v,
        soft_k=soft_k, soft_v=soft_v,
        grad_k=carry["grad_k"], grad_v=carry["grad_v"],
    )
    grad_in, late = exclusive_scan(
        block_decay, grad_summary, "ctx", True, (linear_own, soft_next_scores, soft_next_grads),
        late,
    )
    lin_grad_k = late["lin_dk"] + tail_weight.T[:, :, None] * jnp.einsum(
        "hde,she->shd", grad_in, value_f, precision=exact_mode
    )
    lin_grad_v = late["lin_dv"] + tail_weight.T[:, :, None] * jnp.einsum(
        "hde,shd->she", grad_in, key_f, precision=exact_mode
    )
    return (
        carry["grad_q"].astype(jnp.bfloat16),
        late["soft_dk"],
        late["soft_dv"],
        late["lin_dq"],
        lin_grad_k.astype(jnp.bfloat16).reshape(shape_flat),
        lin_grad_v.astype(jnp.bfloat16).reshape(shape_flat),
    )


def solution(mesh):
    in_specs = (
        P("ctx", "head"),
        P("ctx", "head"),
        P("ctx", "head"),
        P("ctx", "head"),
        P("ctx", "head"),
        P("ctx", "head"),
        P("ctx", "head"),
        P("head", "ctx"),
        P("ctx", "head"),
    )
    out_specs = (
        P("ctx", "head"),
        P("ctx", "head"),
        P("ctx", "head"),
        P("ctx", "head"),
        P("ctx", "head"),
        P("ctx", "head"),
    )
    return jax.shard_map(body, mesh=mesh, in_specs=in_specs, out_specs=out_specs, check_vma=False)
```

```python
import jax
import jax.numpy as jnp
from jax import lax
from jax.sharding import PartitionSpec as P

LOCAL_HEADS = 16
HEAD_DIM = 128


masked_fill = -1e30
exact_mode = lax.Precision.HIGHEST


def shifted(x, axis, by):
    peers = lax.axis_size(axis)
    pairs = [(i, i + by) for i in range(peers) if 0 <= i + by < peers]
    return lax.ppermute(x, axis, pairs)


def exclusive_scan(decay, value, axis, reverse, stages=(), carry=()):
    count = lax.axis_size(axis)
    heads, size, width = value.shape
    win_value, win_decay = value, decay
    res_value, res_decay = jnp.zeros_like(value), jnp.ones_like(decay)
    step = 1
    turn = 0
    while step < count:
        send = jnp.concatenate(
            [win_value, jnp.broadcast_to(win_decay[:, None, None], (heads, 8, width))], axis=1
        ).astype(jnp.bfloat16)
        if turn < len(stages):
            send, carry = lax.optimization_barrier((send, carry))
        got = shifted(send, axis, -step if reverse else step)
        if turn < len(stages):
            carry = stages[turn](carry)
        got_value = got[:, :size].astype(jnp.float32)
        got_decay = got[:, size, 0].astype(jnp.float32)
        win_value = win_value + win_decay[:, None, None] * got_value
        res_value = res_value + res_decay[:, None, None] * got_value
        win_decay = win_decay * got_decay
        res_decay = res_decay * got_decay
        step *= 2
        turn += 1
    for stage in stages[turn:]:
        carry = stage(carry)
    return res_value, carry


def linear_parts(gates):
    running = jnp.cumsum(gates, axis=1)
    block_total = running[:, -1]
    length = gates.shape[1]
    row_ids = lax.broadcasted_iota(jnp.int32, (length, length), 0)
    col_ids = lax.broadcasted_iota(jnp.int32, (length, length), 1)
    lower = (col_ids <= row_ids)[None]
    spread = jnp.where(lower, running[:, :, None] - running[:, None, :], 0.0)
    window_weight = jnp.where(lower, jnp.exp(spread), 0.0)
    tail_weight = jnp.exp(block_total[:, None] - running)
    return (jnp.exp(running), jnp.exp(block_total), tail_weight, window_weight)


def body(soft_q, soft_k, soft_v, soft_dout, lin_q, lin_k, lin_v, lin_gate, lin_dy):
    heads_here = lin_gate.shape[0]
    length = soft_q.shape[0]
    head_size = soft_q.shape[1] // heads_here
    factor = head_size ** (-0.5)
    position = lax.axis_index("ctx")
    has_prev = position > 0
    has_next = position < lax.axis_size("ctx") - 1
    shape_heads = (length, heads_here, head_size)
    shape_flat = (length, heads_here * head_size)
    row_ids = lax.broadcasted_iota(jnp.int32, (length, length), 0)
    col_ids = lax.broadcasted_iota(jnp.int32, (length, length), 1)
    own_mask = (col_ids <= row_ids)[None]
    prev_mask = ((col_ids > row_ids) & has_prev)[None]
    next_mask = ((col_ids > row_ids) & has_next)[None]

    lin_queries = lin_q.reshape(shape_heads)
    lin_keys = lin_k.reshape(shape_heads)
    lin_values = lin_v.reshape(shape_heads)
    query_f = lin_queries.astype(jnp.float32)
    key_f = lin_keys.astype(jnp.float32)
    value_f = lin_values.astype(jnp.float32)
    lead_weight, block_decay, tail_weight, window_weight = linear_parts(lin_gate)
    summary = jnp.einsum("hs,shd,she->hde", tail_weight, key_f, value_f, precision=exact_mode)

    def cols(array, head):
        return array[:, head * head_size:(head + 1) * head_size]

    def mm(a, b):
        return lax.dot_general(a, b, (((1,), (1,)), ((), ())), preferred_element_type=jnp.float32)

    def mm_t(a, b):
        return lax.dot_general(a, b, (((0,), (0,)), ((), ())), preferred_element_type=jnp.float32)

    def mm_n(a, b):
        return lax.dot_general(a, b, (((1,), (0,)), ((), ())), preferred_element_type=jnp.float32)

    own_mask2 = own_mask[0]
    prev_mask2 = prev_mask[0]
    next_mask2 = next_mask[0]
    heads_list = range(heads_here)

    received = {}

    def soft_sends(c):
        c = dict(c)
        received["prev"] = shifted(jnp.stack((c["soft_k"], c["soft_v"])), "ctx", 1)
        received["next"] = shifted(jnp.stack((c["soft_q"], c["soft_dout"])), "ctx", -1)
        lin_scores = jnp.einsum(
            "thd,shd->hts", c["lin_q"].reshape(shape_heads), c["lin_k"].reshape(shape_heads),
            preferred_element_type=jnp.float32,
        )
        c["attended"] = (lin_scores * factor * c["window_weight"]).astype(jnp.bfloat16)
        c["lin_intra"] = jnp.einsum(
            "hts,she->the", c["attended"], c["lin_v"].reshape(shape_heads),
            preferred_element_type=jnp.float32,
        )
        return c

    def soft_heads(part, last):
        def stage(c):
            c = dict(c)
            keys_prev, values_prev = received["prev"][0], received["prev"][1]
            for h in part:
                scores_own = mm(cols(c["soft_q"], h), cols(c["soft_k"], h)) * factor
                dprob_own = mm(cols(c["soft_dout"], h), cols(c["soft_v"], h))
                scores_prev = mm(cols(c["soft_q"], h), cols(keys_prev, h)) * factor
                row_max = jnp.maximum(
                    jnp.max(jnp.where(own_mask2, scores_own, masked_fill), axis=1),
                    jnp.max(jnp.where(prev_mask2, scores_prev, masked_fill), axis=1),
                )
                total = jnp.sum(
                    jnp.where(own_mask2, jnp.exp(scores_own - row_max[:, None]), 0.0), axis=1
                )
                total = total + jnp.sum(
                    jnp.where(prev_mask2, jnp.exp(scores_prev - row_max[:, None]), 0.0), axis=1
                )
                log_total = row_max + jnp.log(total)
                probs_own = jnp.where(own_mask2, jnp.exp(scores_own - log_total[:, None]), 0.0)
                probs_prev = jnp.where(
                    prev_mask2, jnp.exp(scores_prev - log_total[:, None]), 0.0
                )
                dprob_prev = mm(cols(c["soft_dout"], h), cols(values_prev, h))
                row_delta = jnp.sum(probs_own * dprob_own, axis=1) + jnp.sum(
                    probs_prev * dprob_prev, axis=1
                )
                ds_own = (probs_own * (dprob_own - row_delta[:, None])).astype(jnp.bfloat16)
                ds_prev = (probs_prev * (dprob_prev - row_delta[:, None])).astype(jnp.bfloat16)
                c["stat%d" % h] = jnp.stack((log_total, row_delta))
                c["dq%d" % h] = (
                    mm_n(ds_own, cols(c["soft_k"], h)) + mm_n(ds_prev, cols(keys_prev, h))
                ) * factor
                c["dk%d" % h] = mm_t(ds_own, cols(c["soft_q"], h)) * factor
                c["dv%d" % h] = mm_t(probs_own.astype(jnp.bfloat16), cols(c["soft_dout"], h))
            if last:
                received["stats"] = shifted(
                    jnp.stack([c.pop("stat%d" % h) for h in heads_list], axis=1), "ctx", -1
                )
                c["grad_q"] = jnp.concatenate([c.pop("dq%d" % h) for h in heads_list], axis=1)
                c["grad_k"] = [c.pop("dk%d" % h) for h in heads_list]
                c["grad_v"] = [c.pop("dv%d" % h) for h in heads_list]
            return c

        return stage

    split = (heads_here + 1) // 2
    soft_stats = soft_heads(heads_list[:split], False)
    soft_grads = soft_heads(heads_list[split:], True)

    carry = dict(
        soft_q=soft_q, soft_k=soft_k, soft_v=soft_v, soft_dout=soft_dout,
        lin_q=lin_q, lin_k=lin_k, lin_v=lin_v, window_weight=window_weight,
    )
    state_in, carry = exclusive_scan(
        block_decay, summary, "ctx", False, (soft_sends, soft_stats, soft_grads), carry
    )

    lin_output = carry["lin_intra"] + factor * lead_weight.T[:, :, None] * jnp.einsum(
        "thd,hde->the", query_f, state_in, precision=exact_mode
    )
    dy_f = lin_dy.reshape(shape_heads).astype(jnp.float32)
    norm_sums = lax.psum(
        (jnp.sum(lin_output * lin_output, axis=(1, 2)), jnp.sum(lin_output * dy_f, axis=(1, 2))),
        "head",
    )
    width_all = LOCAL_HEADS * HEAD_DIM
    rms_value = jnp.sqrt(norm_sums[0] / width_all + 1e-06)
    lin_grad = (
        dy_f / rms_value[:, None, None]
        - lin_output * (norm_sums[1] / (rms_value**3 * width_all))[:, None, None]
    )
    lin_grad_b = lin_grad.astype(jnp.bfloat16)
    lin_grad_f = lin_grad_b.astype(jnp.float32)
    grad_summary = factor * jnp.einsum(
        "ht,thd,the->hde", lead_weight, query_f, lin_grad_f, precision=exact_mode
    )

    def linear_own(c):
        c = dict(c)
        grad_b = c["lin_grad_b"]
        grad_raw = jnp.einsum(
            "the,she->hts", grad_b, c["lin_v"].reshape(shape_heads),
            preferred_element_type=jnp.float32,
        )
        grad_scores = (grad_raw * factor * c["window_weight"]).astype(jnp.bfloat16)
        lin_grad_q = jnp.einsum(
            "hts,shd->thd", grad_scores, c["lin_k"].reshape(shape_heads),
            preferred_element_type=jnp.float32,
        )
        lin_grad_q = lin_grad_q + factor * c["lead_weight"].T[:, :, None] * jnp.einsum(
            "hde,the->thd", c["state_in"], grad_b.astype(jnp.float32), precision=exact_mode
        )
        c["lin_dq"] = lin_grad_q.astype(jnp.bfloat16).reshape(shape_flat)
        c["lin_dk"] = jnp.einsum(
            "hts,thd->shd", grad_scores, c["lin_q"].reshape(shape_heads),
            preferred_element_type=jnp.float32,
        )
        c["lin_dv"] = jnp.einsum(
            "hts,the->she", c["attended"], grad_b, preferred_element_type=jnp.float32
        )
        for name in ("lin_grad_b", "state_in", "lead_weight", "attended", "window_weight"):
            del c[name]
        return c

    def soft_next_scores(c):
        c = dict(c)
        queries_next, grad_out_next = received["next"][0], received["next"][1]
        stats_next = received["stats"]
        ds_next, p_next = [], []
        for h in heads_list:
            scores_next = mm(cols(queries_next, h), cols(c["soft_k"], h)) * factor
            probs_next = jnp.where(
                next_mask2, jnp.exp(scores_next - stats_next[0, h][:, None]), 0.0
            )
            dprob_next = mm(cols(grad_out_next, h), cols(c["soft_v"], h))
            ds_next.append(
                (probs_next * (dprob_next - stats_next[1, h][:, None])).astype(jnp.bfloat16)
            )
            p_next.append(probs_next.astype(jnp.bfloat16))
        c["dscore_next"], c["probs_next_b"] = ds_next, p_next
        return c

    def soft_next_grads(c):
        c = dict(c)
        queries_next, grad_out_next = received["next"][0], received["next"][1]
        dk, dv = [], []
        for h in heads_list:
            dk.append(
                c["grad_k"][h] + mm_t(c["dscore_next"][h], cols(queries_next, h)) * factor
            )
            dv.append(c["grad_v"][h] + mm_t(c["probs_next_b"][h], cols(grad_out_next, h)))
        c["soft_dk"] = jnp.concatenate(dk, axis=1).astype(jnp.bfloat16)
        c["soft_dv"] = jnp.concatenate(dv, axis=1).astype(jnp.bfloat16)
        return c

    late = dict(
        lin_grad_b=lin_grad_b, state_in=state_in, lead_weight=lead_weight,
        attended=carry["attended"], window_weight=window_weight,
        lin_q=lin_q, lin_k=lin_k, lin_v=lin_v,
        soft_k=soft_k, soft_v=soft_v,
        grad_k=carry["grad_k"], grad_v=carry["grad_v"],
    )
    grad_in, late = exclusive_scan(
        block_decay, grad_summary, "ctx", True, (linear_own, soft_next_scores, soft_next_grads),
        late,
    )
    lin_grad_k = late["lin_dk"] + tail_weight.T[:, :, None] * jnp.einsum(
        "hde,she->shd", grad_in, value_f, precision=exact_mode
    )
    lin_grad_v = late["lin_dv"] + tail_weight.T[:, :, None] * jnp.einsum(
        "hde,shd->she", grad_in, key_f, precision=exact_mode
    )
    return (
        carry["grad_q"].astype(jnp.bfloat16),
        late["soft_dk"],
        late["soft_dv"],
        late["lin_dq"],
        lin_grad_k.astype(jnp.bfloat16).reshape(shape_flat),
        lin_grad_v.astype(jnp.bfloat16).reshape(shape_flat),
    )


def solution(mesh):
    in_specs = (
        P("ctx", "head"),
        P("ctx", "head"),
        P("ctx", "head"),
        P("ctx", "head"),
        P("ctx", "head"),
        P("ctx", "head"),
        P("ctx", "head"),
        P("head", "ctx"),
        P("ctx", "head"),
    )
    out_specs = (
        P("ctx", "head"),
        P("ctx", "head"),
        P("ctx", "head"),
        P("ctx", "head"),
        P("ctx", "head"),
        P("ctx", "head"),
    )
    return jax.shard_map(body, mesh=mesh, in_specs=in_specs, out_specs=out_specs, check_vma=False)
```

```python
import jax
import jax.numpy as jnp
from jax import lax
from jax.sharding import PartitionSpec as P

LOCAL_HEADS = 16
HEAD_DIM = 128


masked_fill = -1e30
exact_mode = lax.Precision.HIGHEST


def shifted(x, axis, by):
    peers = lax.axis_size(axis)
    pairs = [(i, i + by) for i in range(peers) if 0 <= i + by < peers]
    return lax.ppermute(x, axis, pairs)


def exclusive_scan(decay, value, axis, reverse, stages=(), carry=()):
    count = lax.axis_size(axis)
    heads, size, width = value.shape
    win_value, win_decay = value, decay
    res_value, res_decay = jnp.zeros_like(value), jnp.ones_like(decay)
    step = 1
    turn = 0
    while step < count:
        send = jnp.concatenate(
            [win_value, jnp.broadcast_to(win_decay[:, None, None], (heads, 8, width))], axis=1
        ).astype(jnp.bfloat16)
        if turn < len(stages):
            send, carry = lax.optimization_barrier((send, carry))
        got = shifted(send, axis, -step if reverse else step)
        if turn < len(stages):
            carry = stages[turn](carry)
        got_value = got[:, :size].astype(jnp.float32)
        got_decay = got[:, size, 0].astype(jnp.float32)
        win_value = win_value + win_decay[:, None, None] * got_value
        res_value = res_value + res_decay[:, None, None] * got_value
        win_decay = win_decay * got_decay
        res_decay = res_decay * got_decay
        step *= 2
        turn += 1
    for stage in stages[turn:]:
        carry = stage(carry)
    return res_value, carry


def linear_parts(gates):
    running = jnp.cumsum(gates, axis=1)
    block_total = running[:, -1]
    length = gates.shape[1]
    row_ids = lax.broadcasted_iota(jnp.int32, (length, length), 0)
    col_ids = lax.broadcasted_iota(jnp.int32, (length, length), 1)
    lower = (col_ids <= row_ids)[None]
    spread = jnp.where(lower, running[:, :, None] - running[:, None, :], 0.0)
    window_weight = jnp.where(lower, jnp.exp(spread), 0.0)
    tail_weight = jnp.exp(block_total[:, None] - running)
    return (jnp.exp(running), jnp.exp(block_total), tail_weight, window_weight)


def body(soft_q, soft_k, soft_v, soft_dout, lin_q, lin_k, lin_v, lin_gate, lin_dy):
    heads_here = lin_gate.shape[0]
    length = soft_q.shape[0]
    head_size = soft_q.shape[1] // heads_here
    factor = head_size ** (-0.5)
    position = lax.axis_index("ctx")
    has_prev = position > 0
    has_next = position < lax.axis_size("ctx") - 1
    shape_heads = (length, heads_here, head_size)
    shape_flat = (length, heads_here * head_size)
    row_ids = lax.broadcasted_iota(jnp.int32, (length, length), 0)
    col_ids = lax.broadcasted_iota(jnp.int32, (length, length), 1)
    own_mask = (col_ids <= row_ids)[None]
    prev_mask = ((col_ids > row_ids) & has_prev)[None]
    next_mask = ((col_ids > row_ids) & has_next)[None]

    lin_queries = lin_q.reshape(shape_heads)
    lin_keys = lin_k.reshape(shape_heads)
    lin_values = lin_v.reshape(shape_heads)
    query_f = lin_queries.astype(jnp.float32)
    key_f = lin_keys.astype(jnp.float32)
    value_f = lin_values.astype(jnp.float32)
    lead_weight, block_decay, tail_weight, window_weight = linear_parts(lin_gate)
    summary = jnp.einsum("hs,shd,she->hde", tail_weight, key_f, value_f, precision=exact_mode)

    def cols(array, head):
        return array[:, head * head_size:(head + 1) * head_size]

    def mm(a, b):
        return lax.dot_general(a, b, (((1,), (1,)), ((), ())), preferred_element_type=jnp.float32)

    def mm_t(a, b):
        return lax.dot_general(a, b, (((0,), (0,)), ((), ())), preferred_element_type=jnp.float32)

    def mm_n(a, b):
        return lax.dot_general(a, b, (((1,), (0,)), ((), ())), preferred_element_type=jnp.float32)

    own_mask2 = own_mask[0]
    prev_mask2 = prev_mask[0]
    next_mask2 = next_mask[0]
    heads_list = range(heads_here)

    received = {}

    def soft_sends(c):
        c = dict(c)
        received["prev"] = shifted(jnp.stack((c["soft_k"], c["soft_v"])), "ctx", 1)
        received["next"] = shifted(jnp.stack((c["soft_q"], c["soft_dout"])), "ctx", -1)
        lin_scores = jnp.einsum(
            "thd,shd->hts", c["lin_q"].reshape(shape_heads), c["lin_k"].reshape(shape_heads),
            preferred_element_type=jnp.float32,
        )
        c["attended"] = (lin_scores * factor * c["window_weight"]).astype(jnp.bfloat16)
        c["lin_intra"] = jnp.einsum(
            "hts,she->the", c["attended"], c["lin_v"].reshape(shape_heads),
            preferred_element_type=jnp.float32,
        )
        return c

    def soft_heads(part, last):
        def stage(c):
            c = dict(c)
            keys_prev, values_prev = received["prev"][0], received["prev"][1]
            for h in part:
                scores_own = mm(cols(c["soft_q"], h), cols(c["soft_k"], h)) * factor
                dprob_own = mm(cols(c["soft_dout"], h), cols(c["soft_v"], h))
                scores_prev = mm(cols(c["soft_q"], h), cols(keys_prev, h)) * factor
                row_max = jnp.maximum(
                    jnp.max(jnp.where(own_mask2, scores_own, masked_fill), axis=1),
                    jnp.max(jnp.where(prev_mask2, scores_prev, masked_fill), axis=1),
                )
                total = jnp.sum(
                    jnp.where(own_mask2, jnp.exp(scores_own - row_max[:, None]), 0.0), axis=1
                )
                total = total + jnp.sum(
                    jnp.where(prev_mask2, jnp.exp(scores_prev - row_max[:, None]), 0.0), axis=1
                )
                log_total = row_max + jnp.log(total)
                probs_own = jnp.where(own_mask2, jnp.exp(scores_own - log_total[:, None]), 0.0)
                probs_prev = jnp.where(
                    prev_mask2, jnp.exp(scores_prev - log_total[:, None]), 0.0
                )
                dprob_prev = mm(cols(c["soft_dout"], h), cols(values_prev, h))
                row_delta = jnp.sum(probs_own * dprob_own, axis=1) + jnp.sum(
                    probs_prev * dprob_prev, axis=1
                )
                ds_own = (probs_own * (dprob_own - row_delta[:, None])).astype(jnp.bfloat16)
                ds_prev = (probs_prev * (dprob_prev - row_delta[:, None])).astype(jnp.bfloat16)
                c["stat%d" % h] = jnp.stack((log_total, row_delta))
                c["dq%d" % h] = (
                    mm_n(ds_own, cols(c["soft_k"], h)) + mm_n(ds_prev, cols(keys_prev, h))
                ) * factor
                c["dk%d" % h] = mm_t(ds_own, cols(c["soft_q"], h)) * factor
                c["dv%d" % h] = mm_t(probs_own.astype(jnp.bfloat16), cols(c["soft_dout"], h))
            if last:
                received["stats"] = shifted(
                    jnp.stack([c.pop("stat%d" % h) for h in heads_list], axis=1), "ctx", -1
                )
                c["grad_q"] = jnp.concatenate([c.pop("dq%d" % h) for h in heads_list], axis=1)
                c["grad_k"] = [c.pop("dk%d" % h) for h in heads_list]
                c["grad_v"] = [c.pop("dv%d" % h) for h in heads_list]
            return c

        return stage

    split = (heads_here + 1) // 2
    soft_stats = soft_heads(heads_list[:split], False)
    soft_grads = soft_heads(heads_list[split:], True)

    carry = dict(
        soft_q=soft_q, soft_k=soft_k, soft_v=soft_v, soft_dout=soft_dout,
        lin_q=lin_q, lin_k=lin_k, lin_v=lin_v, window_weight=window_weight,
    )
    state_in, carry = exclusive_scan(
        block_decay, summary, "ctx", False, (soft_sends, soft_stats, soft_grads), carry
    )

    lin_output = carry["lin_intra"] + factor * lead_weight.T[:, :, None] * jnp.einsum(
        "thd,hde->the", query_f, state_in, precision=exact_mode
    )
    dy_f = lin_dy.reshape(shape_heads).astype(jnp.float32)
    norm_sums = lax.psum(
        (jnp.sum(lin_output * lin_output, axis=(1, 2)), jnp.sum(lin_output * dy_f, axis=(1, 2))),
        "head",
    )
    width_all = LOCAL_HEADS * HEAD_DIM
    rms_value = jnp.sqrt(norm_sums[0] / width_all + 1e-06)
    lin_grad = (
        dy_f / rms_value[:, None, None]
        - lin_output * (norm_sums[1] / (rms_value**3 * width_all))[:, None, None]
    )
    lin_grad_b = lin_grad.astype(jnp.bfloat16)
    lin_grad_f = lin_grad_b.astype(jnp.float32)
    grad_summary = factor * jnp.einsum(
        "ht,thd,the->hde", lead_weight, query_f, lin_grad_f, precision=exact_mode
    )

    def linear_own(c):
        c = dict(c)
        grad_b = c["lin_grad_b"]
        grad_raw = jnp.einsum(
            "the,she->hts", grad_b, c["lin_v"].reshape(shape_heads),
            preferred_element_type=jnp.float32,
        )
        grad_scores = (grad_raw * factor * c["window_weight"]).astype(jnp.bfloat16)
        lin_grad_q = jnp.einsum(
            "hts,shd->thd", grad_scores, c["lin_k"].reshape(shape_heads),
            preferred_element_type=jnp.float32,
        )
        lin_grad_q = lin_grad_q + factor * c["lead_weight"].T[:, :, None] * jnp.einsum(
            "hde,the->thd", c["state_in"], grad_b.astype(jnp.float32), precision=exact_mode
        )
        c["lin_dq"] = lin_grad_q.astype(jnp.bfloat16).reshape(shape_flat)
        c["lin_dk"] = jnp.einsum(
            "hts,thd->shd", grad_scores, c["lin_q"].reshape(shape_heads),
            preferred_element_type=jnp.float32,
        )
        c["lin_dv"] = jnp.einsum(
            "hts,the->she", c["attended"], grad_b, preferred_element_type=jnp.float32
        )
        for name in ("lin_grad_b", "state_in", "lead_weight", "attended", "window_weight"):
            del c[name]
        return c

    def soft_next_scores(c):
        c = dict(c)
        queries_next, grad_out_next = received["next"][0], received["next"][1]
        stats_next = received["stats"]
        ds_next, p_next = [], []
        for h in heads_list:
            scores_next = mm(cols(queries_next, h), cols(c["soft_k"], h)) * factor
            probs_next = jnp.where(
                next_mask2, jnp.exp(scores_next - stats_next[0, h][:, None]), 0.0
            )
            dprob_next = mm(cols(grad_out_next, h), cols(c["soft_v"], h))
            ds_next.append(
                (probs_next * (dprob_next - stats_next[1, h][:, None])).astype(jnp.bfloat16)
            )
            p_next.append(probs_next.astype(jnp.bfloat16))
        c["dscore_next"], c["probs_next_b"] = ds_next, p_next
        return c

    def soft_next_grads(c):
        c = dict(c)
        queries_next, grad_out_next = received["next"][0], received["next"][1]
        dk, dv = [], []
        for h in heads_list:
            dk.append(
                c["grad_k"][h] + mm_t(c["dscore_next"][h], cols(queries_next, h)) * factor
            )
            dv.append(c["grad_v"][h] + mm_t(c["probs_next_b"][h], cols(grad_out_next, h)))
        c["soft_dk"] = jnp.concatenate(dk, axis=1).astype(jnp.bfloat16)
        c["soft_dv"] = jnp.concatenate(dv, axis=1).astype(jnp.bfloat16)
        return c

    late = dict(
        lin_grad_b=lin_grad_b, state_in=state_in, lead_weight=lead_weight,
        attended=carry["attended"], window_weight=window_weight,
        lin_q=lin_q, lin_k=lin_k, lin_v=lin_v,
        soft_k=soft_k, soft_v=soft_v,
        grad_k=carry["grad_k"], grad_v=carry["grad_v"],
    )
    grad_in, late = exclusive_scan(
        block_decay, grad_summary, "ctx", True,
        (linear_own, lambda c: soft_next_grads(soft_next_scores(c))),
        late,
    )
    lin_grad_k = late["lin_dk"] + tail_weight.T[:, :, None] * jnp.einsum(
        "hde,she->shd", grad_in, value_f, precision=exact_mode
    )
    lin_grad_v = late["lin_dv"] + tail_weight.T[:, :, None] * jnp.einsum(
        "hde,shd->she", grad_in, key_f, precision=exact_mode
    )
    return (
        carry["grad_q"].astype(jnp.bfloat16),
        late["soft_dk"],
        late["soft_dv"],
        late["lin_dq"],
        lin_grad_k.astype(jnp.bfloat16).reshape(shape_flat),
        lin_grad_v.astype(jnp.bfloat16).reshape(shape_flat),
    )


def solution(mesh):
    in_specs = (
        P("ctx", "head"),
        P("ctx", "head"),
        P("ctx", "head"),
        P("ctx", "head"),
        P("ctx", "head"),
        P("ctx", "head"),
        P("ctx", "head"),
        P("head", "ctx"),
        P("ctx", "head"),
    )
    out_specs = (
        P("ctx", "head"),
        P("ctx", "head"),
        P("ctx", "head"),
        P("ctx", "head"),
        P("ctx", "head"),
        P("ctx", "head"),
    )
    return jax.shard_map(body, mesh=mesh, in_specs=in_specs, out_specs=out_specs, check_vma=False)
```

```python
import jax
import jax.numpy as jnp
from jax import lax
from jax.sharding import PartitionSpec as P

LOCAL_HEADS = 16
HEAD_DIM = 128


masked_fill = -1e30
exact_mode = lax.Precision.HIGHEST


def shifted(x, axis, by):
    peers = lax.axis_size(axis)
    pairs = [(i, i + by) for i in range(peers) if 0 <= i + by < peers]
    return lax.ppermute(x, axis, pairs)


def exclusive_scan(decay, value, axis, reverse, stages=(), carry=()):
    count = lax.axis_size(axis)
    heads, size, width = value.shape
    win_value, win_decay = value, decay
    res_value, res_decay = jnp.zeros_like(value), jnp.ones_like(decay)
    step = 1
    turn = 0
    while step < count:
        send = jnp.concatenate(
            [win_value, jnp.broadcast_to(win_decay[:, None, None], (heads, 8, width))], axis=1
        ).astype(jnp.bfloat16)
        if turn < len(stages):
            send, carry = lax.optimization_barrier((send, carry))
        got = shifted(send, axis, -step if reverse else step)
        if turn < len(stages):
            carry = stages[turn](carry)
        got_value = got[:, :size].astype(jnp.float32)
        got_decay = got[:, size, 0].astype(jnp.float32)
        win_value = win_value + win_decay[:, None, None] * got_value
        res_value = res_value + res_decay[:, None, None] * got_value
        win_decay = win_decay * got_decay
        res_decay = res_decay * got_decay
        step *= 2
        turn += 1
    for stage in stages[turn:]:
        carry = stage(carry)
    return res_value, carry


def linear_parts(gates):
    running = jnp.cumsum(gates, axis=1)
    block_total = running[:, -1]
    length = gates.shape[1]
    row_ids = lax.broadcasted_iota(jnp.int32, (length, length), 0)
    col_ids = lax.broadcasted_iota(jnp.int32, (length, length), 1)
    lower = (col_ids <= row_ids)[None]
    spread = jnp.where(lower, running[:, :, None] - running[:, None, :], 0.0)
    window_weight = jnp.where(lower, jnp.exp(spread), 0.0)
    tail_weight = jnp.exp(block_total[:, None] - running)
    return (jnp.exp(running), jnp.exp(block_total), tail_weight, window_weight)


def body(soft_q, soft_k, soft_v, soft_dout, lin_q, lin_k, lin_v, lin_gate, lin_dy):
    heads_here = lin_gate.shape[0]
    length = soft_q.shape[0]
    head_size = soft_q.shape[1] // heads_here
    factor = head_size ** (-0.5)
    position = lax.axis_index("ctx")
    has_prev = position > 0
    has_next = position < lax.axis_size("ctx") - 1
    shape_heads = (length, heads_here, head_size)
    shape_flat = (length, heads_here * head_size)
    row_ids = lax.broadcasted_iota(jnp.int32, (length, length), 0)
    col_ids = lax.broadcasted_iota(jnp.int32, (length, length), 1)
    own_mask = (col_ids <= row_ids)[None]
    prev_mask = ((col_ids > row_ids) & has_prev)[None]
    next_mask = ((col_ids > row_ids) & has_next)[None]

    lin_queries = lin_q.reshape(shape_heads)
    lin_keys = lin_k.reshape(shape_heads)
    lin_values = lin_v.reshape(shape_heads)
    query_f = lin_queries.astype(jnp.float32)
    key_f = lin_keys.astype(jnp.float32)
    value_f = lin_values.astype(jnp.float32)
    lead_weight, block_decay, tail_weight, window_weight = linear_parts(lin_gate)
    summary = jnp.einsum("hs,shd,she->hde", tail_weight, key_f, value_f, precision=exact_mode)

    def cols(array, head):
        return array[:, head * head_size:(head + 1) * head_size]

    def mm(a, b):
        return lax.dot_general(a, b, (((1,), (1,)), ((), ())), preferred_element_type=jnp.float32)

    def mm_t(a, b):
        return lax.dot_general(a, b, (((0,), (0,)), ((), ())), preferred_element_type=jnp.float32)

    def mm_n(a, b):
        return lax.dot_general(a, b, (((1,), (0,)), ((), ())), preferred_element_type=jnp.float32)

    own_mask2 = own_mask[0]
    prev_mask2 = prev_mask[0]
    next_mask2 = next_mask[0]
    heads_list = range(heads_here)

    received = {}

    def soft_sends(c):
        c = dict(c)
        received["prev"] = shifted(jnp.stack((c["soft_k"], c["soft_v"])), "ctx", 1)
        received["next"] = shifted(jnp.stack((c["soft_q"], c["soft_dout"])), "ctx", -1)
        lin_scores = jnp.einsum(
            "thd,shd->hts", c["lin_q"].reshape(shape_heads), c["lin_k"].reshape(shape_heads),
            preferred_element_type=jnp.float32,
        )
        c["attended"] = (lin_scores * factor * c["window_weight"]).astype(jnp.bfloat16)
        c["lin_intra"] = jnp.einsum(
            "hts,she->the", c["attended"], c["lin_v"].reshape(shape_heads),
            preferred_element_type=jnp.float32,
        )
        return c

    def soft_heads(part, last):
        def stage(c):
            c = dict(c)
            keys_prev, values_prev = received["prev"][0], received["prev"][1]
            for h in part:
                scores_own = mm(cols(c["soft_q"], h), cols(c["soft_k"], h)) * factor
                dprob_own = mm(cols(c["soft_dout"], h), cols(c["soft_v"], h))
                scores_prev = mm(cols(c["soft_q"], h), cols(keys_prev, h)) * factor
                row_max = jnp.maximum(
                    jnp.max(jnp.where(own_mask2, scores_own, masked_fill), axis=1),
                    jnp.max(jnp.where(prev_mask2, scores_prev, masked_fill), axis=1),
                )
                total = jnp.sum(
                    jnp.where(own_mask2, jnp.exp(scores_own - row_max[:, None]), 0.0), axis=1
                )
                total = total + jnp.sum(
                    jnp.where(prev_mask2, jnp.exp(scores_prev - row_max[:, None]), 0.0), axis=1
                )
                log_total = row_max + jnp.log(total)
                probs_own = jnp.where(own_mask2, jnp.exp(scores_own - log_total[:, None]), 0.0)
                probs_prev = jnp.where(
                    prev_mask2, jnp.exp(scores_prev - log_total[:, None]), 0.0
                )
                dprob_prev = mm(cols(c["soft_dout"], h), cols(values_prev, h))
                row_delta = jnp.sum(probs_own * dprob_own, axis=1) + jnp.sum(
                    probs_prev * dprob_prev, axis=1
                )
                ds_own = (probs_own * (dprob_own - row_delta[:, None])).astype(jnp.bfloat16)
                ds_prev = (probs_prev * (dprob_prev - row_delta[:, None])).astype(jnp.bfloat16)
                c["stat%d" % h] = jnp.stack((log_total, row_delta))
                c["dq%d" % h] = (
                    mm_n(ds_own, cols(c["soft_k"], h)) + mm_n(ds_prev, cols(keys_prev, h))
                ) * factor
                c["dk%d" % h] = mm_t(ds_own, cols(c["soft_q"], h)) * factor
                c["dv%d" % h] = mm_t(probs_own.astype(jnp.bfloat16), cols(c["soft_dout"], h))
            if last:
                received["stats"] = shifted(
                    jnp.stack([c.pop("stat%d" % h) for h in heads_list], axis=1), "ctx", -1
                )
                c["grad_q"] = jnp.concatenate([c.pop("dq%d" % h) for h in heads_list], axis=1)
                c["grad_k"] = [c.pop("dk%d" % h) for h in heads_list]
                c["grad_v"] = [c.pop("dv%d" % h) for h in heads_list]
            return c

        return stage

    split = (heads_here + 1) // 2
    soft_stats = soft_heads(heads_list[:split], False)
    soft_grads = soft_heads(heads_list[split:], True)

    carry = dict(
        soft_q=soft_q, soft_k=soft_k, soft_v=soft_v, soft_dout=soft_dout,
        lin_q=lin_q, lin_k=lin_k, lin_v=lin_v, window_weight=window_weight,
    )
    state_in, carry = exclusive_scan(
        block_decay, summary, "ctx", False, (soft_sends, soft_stats, soft_grads), carry
    )

    lin_output = carry["lin_intra"] + factor * lead_weight.T[:, :, None] * jnp.einsum(
        "thd,hde->the", query_f, state_in, precision=exact_mode
    )
    dy_f = lin_dy.reshape(shape_heads).astype(jnp.float32)
    norm_sums = lax.psum(
        (jnp.sum(lin_output * lin_output, axis=(1, 2)), jnp.sum(lin_output * dy_f, axis=(1, 2))),
        "head",
    )
    width_all = LOCAL_HEADS * HEAD_DIM
    rms_value = jnp.sqrt(norm_sums[0] / width_all + 1e-06)
    lin_grad = (
        dy_f / rms_value[:, None, None]
        - lin_output * (norm_sums[1] / (rms_value**3 * width_all))[:, None, None]
    )
    lin_grad_b = lin_grad.astype(jnp.bfloat16)
    lin_grad_f = lin_grad_b.astype(jnp.float32)
    grad_summary = factor * jnp.einsum(
        "ht,thd,the->hde", lead_weight, query_f, lin_grad_f, precision=exact_mode
    )

    def linear_own(c):
        c = dict(c)
        grad_b = c["lin_grad_b"]
        grad_raw = jnp.einsum(
            "the,she->hts", grad_b, c["lin_v"].reshape(shape_heads),
            preferred_element_type=jnp.float32,
        )
        grad_scores = (grad_raw * factor * c["window_weight"]).astype(jnp.bfloat16)
        lin_grad_q = jnp.einsum(
            "hts,shd->thd", grad_scores, c["lin_k"].reshape(shape_heads),
            preferred_element_type=jnp.float32,
        )
        lin_grad_q = lin_grad_q + factor * c["lead_weight"].T[:, :, None] * jnp.einsum(
            "hde,the->thd", c["state_in"], grad_b.astype(jnp.float32), precision=exact_mode
        )
        c["lin_dq"] = lin_grad_q.astype(jnp.bfloat16).reshape(shape_flat)
        c["lin_dk"] = jnp.einsum(
            "hts,thd->shd", grad_scores, c["lin_q"].reshape(shape_heads),
            preferred_element_type=jnp.float32,
        )
        c["lin_dv"] = jnp.einsum(
            "hts,the->she", c["attended"], grad_b, preferred_element_type=jnp.float32
        )
        for name in ("lin_grad_b", "state_in", "lead_weight", "attended", "window_weight"):
            del c[name]
        return c

    def soft_next_scores(c):
        c = dict(c)
        queries_next, grad_out_next = received["next"][0], received["next"][1]
        stats_next = received["stats"]
        ds_next, p_next = [], []
        for h in heads_list:
            scores_next = mm(cols(queries_next, h), cols(c["soft_k"], h)) * factor
            probs_next = jnp.where(
                next_mask2, jnp.exp(scores_next - stats_next[0, h][:, None]), 0.0
            )
            dprob_next = mm(cols(grad_out_next, h), cols(c["soft_v"], h))
            ds_next.append(
                (probs_next * (dprob_next - stats_next[1, h][:, None])).astype(jnp.bfloat16)
            )
            p_next.append(probs_next.astype(jnp.bfloat16))
        c["dscore_next"], c["probs_next_b"] = ds_next, p_next
        return c

    def soft_next_grads(c):
        c = dict(c)
        queries_next, grad_out_next = received["next"][0], received["next"][1]
        dk, dv = [], []
        for h in heads_list:
            dk.append(
                own_grads["k"][h] + mm_t(c["dscore_next"][h], cols(queries_next, h)) * factor
            )
            dv.append(own_grads["v"][h] + mm_t(c["probs_next_b"][h], cols(grad_out_next, h)))
        c["soft_dk"] = jnp.concatenate(dk, axis=1).astype(jnp.bfloat16)
        c["soft_dv"] = jnp.concatenate(dv, axis=1).astype(jnp.bfloat16)
        return c

    late = dict(
        lin_grad_b=lin_grad_b, state_in=state_in, lead_weight=lead_weight,
        attended=carry["attended"], window_weight=window_weight,
        lin_q=lin_q, lin_k=lin_k, lin_v=lin_v,
        soft_k=soft_k, soft_v=soft_v,
    )
    own_grads = {"k": carry["grad_k"], "v": carry["grad_v"]}
    grad_in, late = exclusive_scan(
        block_decay, grad_summary, "ctx", True, (linear_own, soft_next_scores, soft_next_grads),
        late,
    )
    lin_grad_k = late["lin_dk"] + tail_weight.T[:, :, None] * jnp.einsum(
        "hde,she->shd", grad_in, value_f, precision=exact_mode
    )
    lin_grad_v = late["lin_dv"] + tail_weight.T[:, :, None] * jnp.einsum(
        "hde,shd->she", grad_in, key_f, precision=exact_mode
    )
    return (
        carry["grad_q"].astype(jnp.bfloat16),
        late["soft_dk"],
        late["soft_dv"],
        late["lin_dq"],
        lin_grad_k.astype(jnp.bfloat16).reshape(shape_flat),
        lin_grad_v.astype(jnp.bfloat16).reshape(shape_flat),
    )


def solution(mesh):
    in_specs = (
        P("ctx", "head"),
        P("ctx", "head"),
        P("ctx", "head"),
        P("ctx", "head"),
        P("ctx", "head"),
        P("ctx", "head"),
        P("ctx", "head"),
        P("head", "ctx"),
        P("ctx", "head"),
    )
    out_specs = (
        P("ctx", "head"),
        P("ctx", "head"),
        P("ctx", "head"),
        P("ctx", "head"),
        P("ctx", "head"),
        P("ctx", "head"),
    )
    return jax.shard_map(body, mesh=mesh, in_specs=in_specs, out_specs=out_specs, check_vma=False)
```

```python
import jax
import jax.numpy as jnp
from jax import lax
from jax.sharding import PartitionSpec as P

LOCAL_HEADS = 16
HEAD_DIM = 128


masked_fill = -1e30
exact_mode = lax.Precision.HIGHEST


def shifted(x, axis, by):
    peers = lax.axis_size(axis)
    pairs = [(i, i + by) for i in range(peers) if 0 <= i + by < peers]
    return lax.ppermute(x, axis, pairs)


def exclusive_scan(decay, value, axis, reverse, stages=(), carry=()):
    count = lax.axis_size(axis)
    heads, size, width = value.shape
    win_value, win_decay = value, decay
    res_value, res_decay = jnp.zeros_like(value), jnp.ones_like(decay)
    step = 1
    turn = 0
    while step < count:
        send = jnp.concatenate(
            [win_value, jnp.broadcast_to(win_decay[:, None, None], (heads, 8, width))], axis=1
        ).astype(jnp.bfloat16)
        if turn < len(stages):
            send, carry = lax.optimization_barrier((send, carry))
        got = shifted(send, axis, -step if reverse else step)
        if turn < len(stages):
            carry = stages[turn](carry)
        got_value = got[:, :size].astype(jnp.float32)
        got_decay = got[:, size, 0].astype(jnp.float32)
        win_value = win_value + win_decay[:, None, None] * got_value
        res_value = res_value + res_decay[:, None, None] * got_value
        win_decay = win_decay * got_decay
        res_decay = res_decay * got_decay
        step *= 2
        turn += 1
    for stage in stages[turn:]:
        carry = stage(carry)
    return res_value, carry


def linear_parts(gates):
    running = jnp.cumsum(gates, axis=1)
    block_total = running[:, -1]
    length = gates.shape[1]
    row_ids = lax.broadcasted_iota(jnp.int32, (length, length), 0)
    col_ids = lax.broadcasted_iota(jnp.int32, (length, length), 1)
    lower = (col_ids <= row_ids)[None]
    spread = jnp.where(lower, running[:, :, None] - running[:, None, :], 0.0)
    window_weight = jnp.where(lower, jnp.exp(spread), 0.0)
    tail_weight = jnp.exp(block_total[:, None] - running)
    return (jnp.exp(running), jnp.exp(block_total), tail_weight, window_weight)


def body(soft_q, soft_k, soft_v, soft_dout, lin_q, lin_k, lin_v, lin_gate, lin_dy):
    heads_here = lin_gate.shape[0]
    length = soft_q.shape[0]
    head_size = soft_q.shape[1] // heads_here
    factor = head_size ** (-0.5)
    position = lax.axis_index("ctx")
    has_prev = position > 0
    has_next = position < lax.axis_size("ctx") - 1
    shape_heads = (length, heads_here, head_size)
    shape_flat = (length, heads_here * head_size)
    row_ids = lax.broadcasted_iota(jnp.int32, (length, length), 0)
    col_ids = lax.broadcasted_iota(jnp.int32, (length, length), 1)
    own_mask = (col_ids <= row_ids)[None]
    prev_mask = ((col_ids > row_ids) & has_prev)[None]
    next_mask = ((col_ids > row_ids) & has_next)[None]

    lin_queries = lin_q.reshape(shape_heads)
    lin_keys = lin_k.reshape(shape_heads)
    lin_values = lin_v.reshape(shape_heads)
    query_f = lin_queries.astype(jnp.float32)
    key_f = lin_keys.astype(jnp.float32)
    value_f = lin_values.astype(jnp.float32)
    lead_weight, block_decay, tail_weight, window_weight = linear_parts(lin_gate)
    summary = jnp.einsum("hs,shd,she->hde", tail_weight, key_f, value_f, precision=exact_mode)

    def cols(array, head):
        return array[:, head * head_size:(head + 1) * head_size]

    def mm(a, b):
        return lax.dot_general(a, b, (((1,), (1,)), ((), ())), preferred_element_type=jnp.float32)

    def mm_t(a, b):
        return lax.dot_general(a, b, (((0,), (0,)), ((), ())), preferred_element_type=jnp.float32)

    def mm_n(a, b):
        return lax.dot_general(a, b, (((1,), (0,)), ((), ())), preferred_element_type=jnp.float32)

    own_mask2 = own_mask[0]
    prev_mask2 = prev_mask[0]
    next_mask2 = next_mask[0]
    heads_list = range(heads_here)

    received = {}

    def soft_sends(c):
        c = dict(c)
        received["prev"] = shifted(jnp.stack((c["soft_k"], c["soft_v"])), "ctx", 1)
        received["next"] = shifted(jnp.stack((c["soft_q"], c["soft_dout"])), "ctx", -1)
        lin_scores = jnp.einsum(
            "thd,shd->hts", c["lin_q"].reshape(shape_heads), c["lin_k"].reshape(shape_heads),
            preferred_element_type=jnp.float32,
        )
        c["attended"] = (lin_scores * factor * c["window_weight"]).astype(jnp.bfloat16)
        c["lin_intra"] = jnp.einsum(
            "hts,she->the", c["attended"], c["lin_v"].reshape(shape_heads),
            preferred_element_type=jnp.float32,
        )
        return c

    def soft_heads(part, last):
        def stage(c):
            c = dict(c)
            keys_prev, values_prev = received["prev"][0], received["prev"][1]
            for h in part:
                scores_own = mm(cols(c["soft_q"], h), cols(c["soft_k"], h)) * factor
                dprob_own = mm(cols(c["soft_dout"], h), cols(c["soft_v"], h))
                scores_prev = mm(cols(c["soft_q"], h), cols(keys_prev, h)) * factor
                row_max = jnp.maximum(
                    jnp.max(jnp.where(own_mask2, scores_own, masked_fill), axis=1),
                    jnp.max(jnp.where(prev_mask2, scores_prev, masked_fill), axis=1),
                )
                total = jnp.sum(
                    jnp.where(own_mask2, jnp.exp(scores_own - row_max[:, None]), 0.0), axis=1
                )
                total = total + jnp.sum(
                    jnp.where(prev_mask2, jnp.exp(scores_prev - row_max[:, None]), 0.0), axis=1
                )
                log_total = row_max + jnp.log(total)
                probs_own = jnp.where(own_mask2, jnp.exp(scores_own - log_total[:, None]), 0.0)
                probs_prev = jnp.where(
                    prev_mask2, jnp.exp(scores_prev - log_total[:, None]), 0.0
                )
                dprob_prev = mm(cols(c["soft_dout"], h), cols(values_prev, h))
                row_delta = jnp.sum(probs_own * dprob_own, axis=1) + jnp.sum(
                    probs_prev * dprob_prev, axis=1
                )
                ds_own = (probs_own * (dprob_own - row_delta[:, None])).astype(jnp.bfloat16)
                ds_prev = (probs_prev * (dprob_prev - row_delta[:, None])).astype(jnp.bfloat16)
                c["stat%d" % h] = jnp.stack((log_total, row_delta))
                c["dq%d" % h] = (
                    mm_n(ds_own, cols(c["soft_k"], h)) + mm_n(ds_prev, cols(keys_prev, h))
                ) * factor
                c["dk%d" % h] = mm_t(ds_own, cols(c["soft_q"], h)) * factor
                c["dv%d" % h] = mm_t(probs_own.astype(jnp.bfloat16), cols(c["soft_dout"], h))
            if last:
                received["stats"] = shifted(
                    jnp.stack([c.pop("stat%d" % h) for h in heads_list], axis=1), "ctx", -1
                )
                c["grad_q"] = jnp.concatenate([c.pop("dq%d" % h) for h in heads_list], axis=1)
                c["grad_k"] = [c.pop("dk%d" % h) for h in heads_list]
                c["grad_v"] = [c.pop("dv%d" % h) for h in heads_list]
            return c

        return stage

    split = (heads_here + 1) // 2
    soft_stats = soft_heads(heads_list[:split], False)
    soft_grads = soft_heads(heads_list[split:], True)

    carry = dict(
        soft_q=soft_q, soft_k=soft_k, soft_v=soft_v, soft_dout=soft_dout,
        lin_q=lin_q, lin_k=lin_k, lin_v=lin_v, window_weight=window_weight,
    )
    state_in, carry = exclusive_scan(
        block_decay, summary, "ctx", False, (soft_sends, dict, soft_stats, soft_grads), carry
    )

    lin_output = carry["lin_intra"] + factor * lead_weight.T[:, :, None] * jnp.einsum(
        "thd,hde->the", query_f, state_in, precision=exact_mode
    )
    dy_f = lin_dy.reshape(shape_heads).astype(jnp.float32)
    norm_sums = lax.psum(
        (jnp.sum(lin_output * lin_output, axis=(1, 2)), jnp.sum(lin_output * dy_f, axis=(1, 2))),
        "head",
    )
    width_all = LOCAL_HEADS * HEAD_DIM
    rms_value = jnp.sqrt(norm_sums[0] / width_all + 1e-06)
    lin_grad = (
        dy_f / rms_value[:, None, None]
        - lin_output * (norm_sums[1] / (rms_value**3 * width_all))[:, None, None]
    )
    lin_grad_b = lin_grad.astype(jnp.bfloat16)
    lin_grad_f = lin_grad_b.astype(jnp.float32)
    grad_summary = factor * jnp.einsum(
        "ht,thd,the->hde", lead_weight, query_f, lin_grad_f, precision=exact_mode
    )

    def linear_own(c):
        c = dict(c)
        grad_b = c["lin_grad_b"]
        grad_raw = jnp.einsum(
            "the,she->hts", grad_b, c["lin_v"].reshape(shape_heads),
            preferred_element_type=jnp.float32,
        )
        grad_scores = (grad_raw * factor * c["window_weight"]).astype(jnp.bfloat16)
        lin_grad_q = jnp.einsum(
            "hts,shd->thd", grad_scores, c["lin_k"].reshape(shape_heads),
            preferred_element_type=jnp.float32,
        )
        lin_grad_q = lin_grad_q + factor * c["lead_weight"].T[:, :, None] * jnp.einsum(
            "hde,the->thd", c["state_in"], grad_b.astype(jnp.float32), precision=exact_mode
        )
        c["lin_dq"] = lin_grad_q.astype(jnp.bfloat16).reshape(shape_flat)
        c["lin_dk"] = jnp.einsum(
            "hts,thd->shd", grad_scores, c["lin_q"].reshape(shape_heads),
            preferred_element_type=jnp.float32,
        )
        c["lin_dv"] = jnp.einsum(
            "hts,the->she", c["attended"], grad_b, preferred_element_type=jnp.float32
        )
        for name in ("lin_grad_b", "state_in", "lead_weight", "attended", "window_weight"):
            del c[name]
        return c

    def soft_next_scores(c):
        c = dict(c)
        queries_next, grad_out_next = received["next"][0], received["next"][1]
        stats_next = received["stats"]
        ds_next, p_next = [], []
        for h in heads_list:
            scores_next = mm(cols(queries_next, h), cols(c["soft_k"], h)) * factor
            probs_next = jnp.where(
                next_mask2, jnp.exp(scores_next - stats_next[0, h][:, None]), 0.0
            )
            dprob_next = mm(cols(grad_out_next, h), cols(c["soft_v"], h))
            ds_next.append(
                (probs_next * (dprob_next - stats_next[1, h][:, None])).astype(jnp.bfloat16)
            )
            p_next.append(probs_next.astype(jnp.bfloat16))
        c["dscore_next"], c["probs_next_b"] = ds_next, p_next
        return c

    def soft_next_grads(c):
        c = dict(c)
        queries_next, grad_out_next = received["next"][0], received["next"][1]
        dk, dv = [], []
        for h in heads_list:
            dk.append(
                own_grads["k"][h] + mm_t(c["dscore_next"][h], cols(queries_next, h)) * factor
            )
            dv.append(own_grads["v"][h] + mm_t(c["probs_next_b"][h], cols(grad_out_next, h)))
        c["soft_dk"] = jnp.concatenate(dk, axis=1).astype(jnp.bfloat16)
        c["soft_dv"] = jnp.concatenate(dv, axis=1).astype(jnp.bfloat16)
        return c

    late = dict(
        lin_grad_b=lin_grad_b, state_in=state_in, lead_weight=lead_weight,
        attended=carry["attended"], window_weight=window_weight,
        lin_q=lin_q, lin_k=lin_k, lin_v=lin_v,
        soft_k=soft_k, soft_v=soft_v,
    )
    own_grads = {"k": carry["grad_k"], "v": carry["grad_v"]}
    grad_in, late = exclusive_scan(
        block_decay, grad_summary, "ctx", True, (linear_own, soft_next_scores, soft_next_grads),
        late,
    )
    lin_grad_k = late["lin_dk"] + tail_weight.T[:, :, None] * jnp.einsum(
        "hde,she->shd", grad_in, value_f, precision=exact_mode
    )
    lin_grad_v = late["lin_dv"] + tail_weight.T[:, :, None] * jnp.einsum(
        "hde,shd->she", grad_in, key_f, precision=exact_mode
    )
    return (
        carry["grad_q"].astype(jnp.bfloat16),
        late["soft_dk"],
        late["soft_dv"],
        late["lin_dq"],
        lin_grad_k.astype(jnp.bfloat16).reshape(shape_flat),
        lin_grad_v.astype(jnp.bfloat16).reshape(shape_flat),
    )


def solution(mesh):
    in_specs = (
        P("ctx", "head"),
        P("ctx", "head"),
        P("ctx", "head"),
        P("ctx", "head"),
        P("ctx", "head"),
        P("ctx", "head"),
        P("ctx", "head"),
        P("head", "ctx"),
        P("ctx", "head"),
    )
    out_specs = (
        P("ctx", "head"),
        P("ctx", "head"),
        P("ctx", "head"),
        P("ctx", "head"),
        P("ctx", "head"),
        P("ctx", "head"),
    )
    return jax.shard_map(body, mesh=mesh, in_specs=in_specs, out_specs=out_specs, check_vma=False)
```

```python
import jax
import jax.numpy as jnp
from jax import lax
from jax.sharding import PartitionSpec as P

LOCAL_HEADS = 16
HEAD_DIM = 128


masked_fill = -1e30
exact_mode = lax.Precision.HIGHEST


def shifted(x, axis, by):
    peers = lax.axis_size(axis)
    pairs = [(i, i + by) for i in range(peers) if 0 <= i + by < peers]
    return lax.ppermute(x, axis, pairs)


def exclusive_scan(decay, value, axis, reverse, stages=(), carry=()):
    count = lax.axis_size(axis)
    heads, size, width = value.shape
    win_value, win_decay = value, decay
    res_value, res_decay = jnp.zeros_like(value), jnp.ones_like(decay)
    step = 1
    turn = 0
    while step < count:
        send = jnp.concatenate(
            [win_value, jnp.broadcast_to(win_decay[:, None, None], (heads, 8, width))], axis=1
        ).astype(jnp.bfloat16)
        if turn < len(stages):
            send, carry = lax.optimization_barrier((send, carry))
        got = shifted(send, axis, -step if reverse else step)
        if turn < len(stages):
            carry = stages[turn](carry)
        got_value = got[:, :size].astype(jnp.float32)
        got_decay = got[:, size, 0].astype(jnp.float32)
        win_value = win_value + win_decay[:, None, None] * got_value
        res_value = res_value + res_decay[:, None, None] * got_value
        win_decay = win_decay * got_decay
        res_decay = res_decay * got_decay
        step *= 2
        turn += 1
    for stage in stages[turn:]:
        carry = stage(carry)
    return res_value, carry


def linear_parts(gates):
    running = jnp.cumsum(gates, axis=1)
    block_total = running[:, -1]
    length = gates.shape[1]
    row_ids = lax.broadcasted_iota(jnp.int32, (length, length), 0)
    col_ids = lax.broadcasted_iota(jnp.int32, (length, length), 1)
    lower = (col_ids <= row_ids)[None]
    spread = jnp.where(lower, running[:, :, None] - running[:, None, :], 0.0)
    window_weight = jnp.where(lower, jnp.exp(spread), 0.0)
    tail_weight = jnp.exp(block_total[:, None] - running)
    return (jnp.exp(running), jnp.exp(block_total), tail_weight, window_weight)


def body(soft_q, soft_k, soft_v, soft_dout, lin_q, lin_k, lin_v, lin_gate, lin_dy):
    heads_here = lin_gate.shape[0]
    length = soft_q.shape[0]
    head_size = soft_q.shape[1] // heads_here
    factor = head_size ** (-0.5)
    position = lax.axis_index("ctx")
    has_prev = position > 0
    has_next = position < lax.axis_size("ctx") - 1
    shape_heads = (length, heads_here, head_size)
    shape_flat = (length, heads_here * head_size)
    row_ids = lax.broadcasted_iota(jnp.int32, (length, length), 0)
    col_ids = lax.broadcasted_iota(jnp.int32, (length, length), 1)
    own_mask = (col_ids <= row_ids)[None]
    prev_mask = ((col_ids > row_ids) & has_prev)[None]
    next_mask = ((col_ids > row_ids) & has_next)[None]

    lin_queries = lin_q.reshape(shape_heads)
    lin_keys = lin_k.reshape(shape_heads)
    lin_values = lin_v.reshape(shape_heads)
    query_f = lin_queries.astype(jnp.float32)
    key_f = lin_keys.astype(jnp.float32)
    value_f = lin_values.astype(jnp.float32)
    lead_weight, block_decay, tail_weight, window_weight = linear_parts(lin_gate)
    summary = jnp.einsum("hs,shd,she->hde", tail_weight, key_f, value_f, precision=exact_mode)

    def cols(array, head):
        return array[:, head * head_size:(head + 1) * head_size]

    def mm(a, b):
        return lax.dot_general(a, b, (((1,), (1,)), ((), ())), preferred_element_type=jnp.float32)

    def mm_t(a, b):
        return lax.dot_general(a, b, (((0,), (0,)), ((), ())), preferred_element_type=jnp.float32)

    def mm_n(a, b):
        return lax.dot_general(a, b, (((1,), (0,)), ((), ())), preferred_element_type=jnp.float32)

    own_mask2 = own_mask[0]
    prev_mask2 = prev_mask[0]
    next_mask2 = next_mask[0]
    heads_list = range(heads_here)

    received = {}

    def soft_sends(c):
        c = dict(c)
        received["prev"] = shifted(jnp.stack((c["soft_k"], c["soft_v"])), "ctx", 1)
        received["next"] = shifted(jnp.stack((c["soft_q"], c["soft_dout"])), "ctx", -1)
        return c

    def soft_heads(part, last):
        def stage(c):
            c = dict(c)
            keys_prev, values_prev = received["prev"][0], received["prev"][1]
            for h in part:
                scores_own = mm(cols(c["soft_q"], h), cols(c["soft_k"], h)) * factor
                dprob_own = mm(cols(c["soft_dout"], h), cols(c["soft_v"], h))
                scores_prev = mm(cols(c["soft_q"], h), cols(keys_prev, h)) * factor
                row_max = jnp.maximum(
                    jnp.max(jnp.where(own_mask2, scores_own, masked_fill), axis=1),
                    jnp.max(jnp.where(prev_mask2, scores_prev, masked_fill), axis=1),
                )
                total = jnp.sum(
                    jnp.where(own_mask2, jnp.exp(scores_own - row_max[:, None]), 0.0), axis=1
                )
                total = total + jnp.sum(
                    jnp.where(prev_mask2, jnp.exp(scores_prev - row_max[:, None]), 0.0), axis=1
                )
                log_total = row_max + jnp.log(total)
                probs_own = jnp.where(own_mask2, jnp.exp(scores_own - log_total[:, None]), 0.0)
                probs_prev = jnp.where(
                    prev_mask2, jnp.exp(scores_prev - log_total[:, None]), 0.0
                )
                dprob_prev = mm(cols(c["soft_dout"], h), cols(values_prev, h))
                row_delta = jnp.sum(probs_own * dprob_own, axis=1) + jnp.sum(
                    probs_prev * dprob_prev, axis=1
                )
                ds_own = (probs_own * (dprob_own - row_delta[:, None])).astype(jnp.bfloat16)
                ds_prev = (probs_prev * (dprob_prev - row_delta[:, None])).astype(jnp.bfloat16)
                c["stat%d" % h] = jnp.stack((log_total, row_delta))
                c["dq%d" % h] = (
                    mm_n(ds_own, cols(c["soft_k"], h)) + mm_n(ds_prev, cols(keys_prev, h))
                ) * factor
                c["dk%d" % h] = mm_t(ds_own, cols(c["soft_q"], h)) * factor
                c["dv%d" % h] = mm_t(probs_own.astype(jnp.bfloat16), cols(c["soft_dout"], h))
            if last:
                lin_scores = jnp.einsum(
                    "thd,shd->hts", c["lin_q"].reshape(shape_heads),
                    c["lin_k"].reshape(shape_heads), preferred_element_type=jnp.float32,
                )
                c["attended"] = (lin_scores * factor * window_weight).astype(jnp.bfloat16)
                c["lin_intra"] = jnp.einsum(
                    "hts,she->the", c["attended"], c["lin_v"].reshape(shape_heads),
                    preferred_element_type=jnp.float32,
                )
                received["stats"] = shifted(
                    jnp.stack([c.pop("stat%d" % h) for h in heads_list], axis=1), "ctx", -1
                )
                c["grad_q"] = jnp.concatenate([c.pop("dq%d" % h) for h in heads_list], axis=1)
                c["grad_k"] = [c.pop("dk%d" % h) for h in heads_list]
                c["grad_v"] = [c.pop("dv%d" % h) for h in heads_list]
            return c

        return stage

    split = (heads_here + 1) // 2
    soft_stats = soft_heads(heads_list[:split], False)
    soft_grads = soft_heads(heads_list[split:], True)

    carry = dict(
        soft_q=soft_q, soft_k=soft_k, soft_v=soft_v, soft_dout=soft_dout,
        lin_q=lin_q, lin_k=lin_k, lin_v=lin_v,
    )
    state_in, carry = exclusive_scan(
        block_decay, summary, "ctx", False, (soft_sends, soft_stats, soft_grads), carry
    )

    lin_output = carry["lin_intra"] + factor * lead_weight.T[:, :, None] * jnp.einsum(
        "thd,hde->the", query_f, state_in, precision=exact_mode
    )
    dy_f = lin_dy.reshape(shape_heads).astype(jnp.float32)
    norm_sums = lax.psum(
        (jnp.sum(lin_output * lin_output, axis=(1, 2)), jnp.sum(lin_output * dy_f, axis=(1, 2))),
        "head",
    )
    width_all = LOCAL_HEADS * HEAD_DIM
    rms_value = jnp.sqrt(norm_sums[0] / width_all + 1e-06)
    lin_grad = (
        dy_f / rms_value[:, None, None]
        - lin_output * (norm_sums[1] / (rms_value**3 * width_all))[:, None, None]
    )
    lin_grad_b = lin_grad.astype(jnp.bfloat16)
    lin_grad_f = lin_grad_b.astype(jnp.float32)
    grad_summary = factor * jnp.einsum(
        "ht,thd,the->hde", lead_weight, query_f, lin_grad_f, precision=exact_mode
    )

    def linear_own(c):
        c = dict(c)
        grad_b = c["lin_grad_b"]
        grad_raw = jnp.einsum(
            "the,she->hts", grad_b, c["lin_v"].reshape(shape_heads),
            preferred_element_type=jnp.float32,
        )
        grad_scores = (grad_raw * factor * window_weight).astype(jnp.bfloat16)
        lin_grad_q = jnp.einsum(
            "hts,shd->thd", grad_scores, c["lin_k"].reshape(shape_heads),
            preferred_element_type=jnp.float32,
        )
        lin_grad_q = lin_grad_q + factor * c["lead_weight"].T[:, :, None] * jnp.einsum(
            "hde,the->thd", c["state_in"], grad_b.astype(jnp.float32), precision=exact_mode
        )
        c["lin_dq"] = lin_grad_q.astype(jnp.bfloat16).reshape(shape_flat)
        c["lin_dk"] = jnp.einsum(
            "hts,thd->shd", grad_scores, c["lin_q"].reshape(shape_heads),
            preferred_element_type=jnp.float32,
        )
        c["lin_dv"] = jnp.einsum(
            "hts,the->she", carry["attended"], grad_b, preferred_element_type=jnp.float32
        )
        for name in ("lin_grad_b", "state_in", "lead_weight"):
            del c[name]
        return c

    def soft_next_scores(c):
        c = dict(c)
        queries_next, grad_out_next = received["next"][0], received["next"][1]
        stats_next = received["stats"]
        ds_next, p_next = [], []
        for h in heads_list:
            scores_next = mm(cols(queries_next, h), cols(c["soft_k"], h)) * factor
            probs_next = jnp.where(
                next_mask2, jnp.exp(scores_next - stats_next[0, h][:, None]), 0.0
            )
            dprob_next = mm(cols(grad_out_next, h), cols(c["soft_v"], h))
            ds_next.append(
                (probs_next * (dprob_next - stats_next[1, h][:, None])).astype(jnp.bfloat16)
            )
            p_next.append(probs_next.astype(jnp.bfloat16))
        c["dscore_next"], c["probs_next_b"] = ds_next, p_next
        return c

    def soft_next_grads(c):
        c = dict(c)
        queries_next, grad_out_next = received["next"][0], received["next"][1]
        dk, dv = [], []
        for h in heads_list:
            dk.append(
                c["grad_k"][h] + mm_t(c["dscore_next"][h], cols(queries_next, h)) * factor
            )
            dv.append(c["grad_v"][h] + mm_t(c["probs_next_b"][h], cols(grad_out_next, h)))
        c["soft_dk"] = jnp.concatenate(dk, axis=1).astype(jnp.bfloat16)
        c["soft_dv"] = jnp.concatenate(dv, axis=1).astype(jnp.bfloat16)
        return c

    late = dict(
        lin_grad_b=lin_grad_b, state_in=state_in, lead_weight=lead_weight,
        lin_q=lin_q, lin_k=lin_k, lin_v=lin_v,
        soft_k=soft_k, soft_v=soft_v,
        grad_k=carry["grad_k"], grad_v=carry["grad_v"],
    )
    grad_in, late = exclusive_scan(
        block_decay, grad_summary, "ctx", True, (linear_own, soft_next_scores, soft_next_grads),
        late,
    )
    lin_grad_k = late["lin_dk"] + tail_weight.T[:, :, None] * jnp.einsum(
        "hde,she->shd", grad_in, value_f, precision=exact_mode
    )
    lin_grad_v = late["lin_dv"] + tail_weight.T[:, :, None] * jnp.einsum(
        "hde,shd->she", grad_in, key_f, precision=exact_mode
    )
    return (
        carry["grad_q"].astype(jnp.bfloat16),
        late["soft_dk"],
        late["soft_dv"],
        late["lin_dq"],
        lin_grad_k.astype(jnp.bfloat16).reshape(shape_flat),
        lin_grad_v.astype(jnp.bfloat16).reshape(shape_flat),
    )


def solution(mesh):
    in_specs = (
        P("ctx", "head"),
        P("ctx", "head"),
        P("ctx", "head"),
        P("ctx", "head"),
        P("ctx", "head"),
        P("ctx", "head"),
        P("ctx", "head"),
        P("head", "ctx"),
        P("ctx", "head"),
    )
    out_specs = (
        P("ctx", "head"),
        P("ctx", "head"),
        P("ctx", "head"),
        P("ctx", "head"),
        P("ctx", "head"),
        P("ctx", "head"),
    )
    return jax.shard_map(body, mesh=mesh, in_specs=in_specs, out_specs=out_specs, check_vma=False)
```

```python
import jax
import jax.numpy as jnp
from jax import lax
from jax.sharding import PartitionSpec as P

LOCAL_HEADS = 16
HEAD_DIM = 128


masked_fill = -1e30
exact_mode = lax.Precision.HIGHEST


def shifted(x, axis, by):
    peers = lax.axis_size(axis)
    pairs = [(i, i + by) for i in range(peers) if 0 <= i + by < peers]
    return lax.ppermute(x, axis, pairs)


def exclusive_scan(decay, value, axis, reverse, stages=(), carry=()):
    count = lax.axis_size(axis)
    heads, size, width = value.shape
    win_value, win_decay = value, decay
    res_value, res_decay = jnp.zeros_like(value), jnp.ones_like(decay)
    step = 1
    turn = 0
    while step < count:
        send = jnp.concatenate(
            [win_value, jnp.broadcast_to(win_decay[:, None, None], (heads, 8, width))], axis=1
        ).astype(jnp.bfloat16)
        if turn < len(stages):
            send, carry = lax.optimization_barrier((send, carry))
        got = shifted(send, axis, -step if reverse else step)
        if turn < len(stages):
            carry = stages[turn](carry)
        got_value = got[:, :size].astype(jnp.float32)
        got_decay = got[:, size, 0].astype(jnp.float32)
        win_value = win_value + win_decay[:, None, None] * got_value
        res_value = res_value + res_decay[:, None, None] * got_value
        win_decay = win_decay * got_decay
        res_decay = res_decay * got_decay
        step *= 2
        turn += 1
    for stage in stages[turn:]:
        carry = stage(carry)
    return res_value, carry


def linear_parts(gates):
    running = jnp.cumsum(gates, axis=1)
    block_total = running[:, -1]
    length = gates.shape[1]
    row_ids = lax.broadcasted_iota(jnp.int32, (length, length), 0)
    col_ids = lax.broadcasted_iota(jnp.int32, (length, length), 1)
    lower = (col_ids <= row_ids)[None]
    spread = jnp.where(lower, running[:, :, None] - running[:, None, :], 0.0)
    window_weight = jnp.where(lower, jnp.exp(spread), 0.0)
    tail_weight = jnp.exp(block_total[:, None] - running)
    return (jnp.exp(running), jnp.exp(block_total), tail_weight, window_weight)


def body(soft_q, soft_k, soft_v, soft_dout, lin_q, lin_k, lin_v, lin_gate, lin_dy):
    heads_here = lin_gate.shape[0]
    length = soft_q.shape[0]
    head_size = soft_q.shape[1] // heads_here
    factor = head_size ** (-0.5)
    position = lax.axis_index("ctx")
    has_prev = position > 0
    has_next = position < lax.axis_size("ctx") - 1
    shape_heads = (length, heads_here, head_size)
    shape_flat = (length, heads_here * head_size)
    row_ids = lax.broadcasted_iota(jnp.int32, (length, length), 0)
    col_ids = lax.broadcasted_iota(jnp.int32, (length, length), 1)
    own_mask = (col_ids <= row_ids)[None]
    prev_mask = ((col_ids > row_ids) & has_prev)[None]
    next_mask = ((col_ids > row_ids) & has_next)[None]

    lin_queries = lin_q.reshape(shape_heads)
    lin_keys = lin_k.reshape(shape_heads)
    lin_values = lin_v.reshape(shape_heads)
    query_f = lin_queries.astype(jnp.float32)
    key_f = lin_keys.astype(jnp.float32)
    value_f = lin_values.astype(jnp.float32)
    lead_weight, block_decay, tail_weight, window_weight = linear_parts(lin_gate)
    summary = jnp.einsum("hs,shd,she->hde", tail_weight, key_f, value_f, precision=exact_mode)

    def cols(array, head):
        return array[:, head * head_size:(head + 1) * head_size]

    def mm(a, b):
        return lax.dot_general(a, b, (((1,), (1,)), ((), ())), preferred_element_type=jnp.float32)

    def mm_t(a, b):
        return lax.dot_general(a, b, (((0,), (0,)), ((), ())), preferred_element_type=jnp.float32)

    def mm_n(a, b):
        return lax.dot_general(a, b, (((1,), (0,)), ((), ())), preferred_element_type=jnp.float32)

    own_mask2 = own_mask[0]
    prev_mask2 = prev_mask[0]
    next_mask2 = next_mask[0]
    heads_list = range(heads_here)

    received = {}

    def soft_sends(c):
        c = dict(c)
        received["prev"] = shifted(jnp.stack((c["soft_k"], c["soft_v"])), "ctx", 1)
        received["next"] = shifted(jnp.stack((c["soft_q"], c["soft_dout"])), "ctx", -1)
        lin_scores = jnp.einsum(
            "thd,shd->hts", c["lin_q"].reshape(shape_heads), c["lin_k"].reshape(shape_heads),
            preferred_element_type=jnp.float32,
        )
        c["attended"] = (lin_scores * factor * c["window_weight"]).astype(jnp.bfloat16)
        c["lin_intra"] = jnp.einsum(
            "hts,she->the", c["attended"], c["lin_v"].reshape(shape_heads),
            preferred_element_type=jnp.float32,
        )
        return c

    def soft_heads(part, last):
        def stage(c):
            c = dict(c)
            keys_prev, values_prev = received["prev"][0], received["prev"][1]
            for h in part:
                scores_own = mm(cols(c["soft_q"], h), cols(c["soft_k"], h)) * factor
                dprob_own = mm(cols(c["soft_dout"], h), cols(c["soft_v"], h))
                scores_prev = mm(cols(c["soft_q"], h), cols(keys_prev, h)) * factor
                row_max = jnp.maximum(
                    jnp.max(jnp.where(own_mask2, scores_own, masked_fill), axis=1),
                    jnp.max(jnp.where(prev_mask2, scores_prev, masked_fill), axis=1),
                )
                total = jnp.sum(
                    jnp.where(own_mask2, jnp.exp(scores_own - row_max[:, None]), 0.0), axis=1
                )
                total = total + jnp.sum(
                    jnp.where(prev_mask2, jnp.exp(scores_prev - row_max[:, None]), 0.0), axis=1
                )
                log_total = row_max + jnp.log(total)
                probs_own = jnp.where(own_mask2, jnp.exp(scores_own - log_total[:, None]), 0.0)
                probs_prev = jnp.where(
                    prev_mask2, jnp.exp(scores_prev - log_total[:, None]), 0.0
                )
                dprob_prev = mm(cols(c["soft_dout"], h), cols(values_prev, h))
                row_delta = jnp.sum(probs_own * dprob_own, axis=1) + jnp.sum(
                    probs_prev * dprob_prev, axis=1
                )
                ds_own = (probs_own * (dprob_own - row_delta[:, None])).astype(jnp.bfloat16)
                ds_prev = (probs_prev * (dprob_prev - row_delta[:, None])).astype(jnp.bfloat16)
                c["stat%d" % h] = jnp.stack((log_total, row_delta))
                c["dq%d" % h] = (
                    mm_n(ds_own, cols(c["soft_k"], h)) + mm_n(ds_prev, cols(keys_prev, h))
                ) * factor
                c["dk%d" % h] = mm_t(ds_own, cols(c["soft_q"], h)) * factor
                c["dv%d" % h] = mm_t(probs_own.astype(jnp.bfloat16), cols(c["soft_dout"], h))
            if last:
                received["stats"] = shifted(
                    jnp.stack([c.pop("stat%d" % h) for h in heads_list], axis=1), "ctx", -1
                )
                c["grad_q"] = jnp.concatenate([c.pop("dq%d" % h) for h in heads_list], axis=1)
                c["grad_k"] = [c.pop("dk%d" % h) for h in heads_list]
                c["grad_v"] = [c.pop("dv%d" % h) for h in heads_list]
            return c

        return stage

    split = (heads_here + 1) // 2
    soft_stats = soft_heads(heads_list[:split], False)
    soft_grads = soft_heads(heads_list[split:], True)

    carry = dict(
        soft_q=soft_q, soft_k=soft_k, soft_v=soft_v, soft_dout=soft_dout,
        lin_q=lin_q, lin_k=lin_k, lin_v=lin_v, window_weight=window_weight,
    )
    state_in, carry = exclusive_scan(
        block_decay, summary, "ctx", False, (soft_sends, soft_stats, soft_grads), carry
    )

    lin_output = carry["lin_intra"] + factor * lead_weight.T[:, :, None] * jnp.einsum(
        "thd,hde->the", query_f, state_in, precision=exact_mode
    )
    dy_f = lin_dy.reshape(shape_heads).astype(jnp.float32)
    norm_sums = lax.psum(
        (jnp.sum(lin_output * lin_output, axis=(1, 2)), jnp.sum(lin_output * dy_f, axis=(1, 2))),
        "head",
    )
    width_all = LOCAL_HEADS * HEAD_DIM
    rms_value = jnp.sqrt(norm_sums[0] / width_all + 1e-06)
    lin_grad = (
        dy_f / rms_value[:, None, None]
        - lin_output * (norm_sums[1] / (rms_value**3 * width_all))[:, None, None]
    )
    lin_grad_b = lin_grad.astype(jnp.bfloat16)
    lin_grad_f = lin_grad_b.astype(jnp.float32)
    grad_summary = factor * jnp.einsum(
        "ht,thd,the->hde", lead_weight, query_f, lin_grad_f, precision=exact_mode
    )

    def linear_own(c):
        c = dict(c)
        grad_b = c["lin_grad_b"]
        grad_raw = jnp.einsum(
            "the,she->hts", grad_b, c["lin_v"].reshape(shape_heads),
            preferred_element_type=jnp.float32,
        )
        grad_scores = (grad_raw * factor * c["window_weight"]).astype(jnp.bfloat16)
        lin_grad_q = jnp.einsum(
            "hts,shd->thd", grad_scores, c["lin_k"].reshape(shape_heads),
            preferred_element_type=jnp.float32,
        )
        lin_grad_q = lin_grad_q + factor * c["lead_weight"].T[:, :, None] * jnp.einsum(
            "hde,the->thd", c["state_in"], grad_b.astype(jnp.float32), precision=exact_mode
        )
        c["lin_dq"] = lin_grad_q.astype(jnp.bfloat16).reshape(shape_flat)
        c["lin_dk"] = jnp.einsum(
            "hts,thd->shd", grad_scores, c["lin_q"].reshape(shape_heads),
            preferred_element_type=jnp.float32,
        )
        c["lin_dv"] = jnp.einsum(
            "hts,the->she", c["attended"], grad_b, preferred_element_type=jnp.float32
        )
        for name in ("lin_grad_b", "state_in", "lead_weight", "attended", "window_weight"):
            del c[name]
        return c

    def soft_next_scores(c):
        c = dict(c)
        queries_next, grad_out_next = received["next"][0], received["next"][1]
        stats_next = received["stats"]
        ds_next, p_next = [], []
        for h in heads_list:
            scores_next = mm(cols(queries_next, h), cols(c["soft_k"], h)) * factor
            probs_next = jnp.where(
                next_mask2, jnp.exp(scores_next - stats_next[0, h][:, None]), 0.0
            )
            dprob_next = mm(cols(grad_out_next, h), cols(c["soft_v"], h))
            ds_next.append(
                (probs_next * (dprob_next - stats_next[1, h][:, None])).astype(jnp.bfloat16)
            )
            p_next.append(probs_next.astype(jnp.bfloat16))
        c["dscore_next"], c["probs_next_b"] = ds_next, p_next
        return c

    def soft_next_grads(c):
        c = dict(c)
        queries_next, grad_out_next = received["next"][0], received["next"][1]
        dk, dv = [], []
        for h in heads_list:
            dk.append(
                c["grad_k"][h] + mm_t(c["dscore_next"][h], cols(queries_next, h)) * factor
            )
            dv.append(c["grad_v"][h] + mm_t(c["probs_next_b"][h], cols(grad_out_next, h)))
        c["soft_dk"] = jnp.concatenate(dk, axis=1).astype(jnp.bfloat16)
        c["soft_dv"] = jnp.concatenate(dv, axis=1).astype(jnp.bfloat16)
        return c

    late = dict(
        lin_grad_b=lin_grad_b, state_in=state_in, lead_weight=lead_weight,
        attended=carry["attended"], window_weight=window_weight,
        lin_q=lin_q, lin_k=lin_k, lin_v=lin_v,
        soft_k=soft_k, soft_v=soft_v,
        grad_k=carry["grad_k"], grad_v=carry["grad_v"],
    )
    grad_in, late = exclusive_scan(
        block_decay, grad_summary, "ctx", True, (soft_next_scores, linear_own, soft_next_grads),
        late,
    )
    lin_grad_k = late["lin_dk"] + tail_weight.T[:, :, None] * jnp.einsum(
        "hde,she->shd", grad_in, value_f, precision=exact_mode
    )
    lin_grad_v = late["lin_dv"] + tail_weight.T[:, :, None] * jnp.einsum(
        "hde,shd->she", grad_in, key_f, precision=exact_mode
    )
    return (
        carry["grad_q"].astype(jnp.bfloat16),
        late["soft_dk"],
        late["soft_dv"],
        late["lin_dq"],
        lin_grad_k.astype(jnp.bfloat16).reshape(shape_flat),
        lin_grad_v.astype(jnp.bfloat16).reshape(shape_flat),
    )


def solution(mesh):
    in_specs = (
        P("ctx", "head"),
        P("ctx", "head"),
        P("ctx", "head"),
        P("ctx", "head"),
        P("ctx", "head"),
        P("ctx", "head"),
        P("ctx", "head"),
        P("head", "ctx"),
        P("ctx", "head"),
    )
    out_specs = (
        P("ctx", "head"),
        P("ctx", "head"),
        P("ctx", "head"),
        P("ctx", "head"),
        P("ctx", "head"),
        P("ctx", "head"),
    )
    return jax.shard_map(body, mesh=mesh, in_specs=in_specs, out_specs=out_specs, check_vma=False)
```

```python
import jax
import jax.numpy as jnp
from jax import lax
from jax.sharding import PartitionSpec as P

LOCAL_HEADS = 16
HEAD_DIM = 128


masked_fill = -1e30
exact_mode = lax.Precision.HIGHEST


def shifted(x, axis, by):
    peers = lax.axis_size(axis)
    pairs = [(i, i + by) for i in range(peers) if 0 <= i + by < peers]
    return lax.ppermute(x, axis, pairs)


def exclusive_scan(decay, value, axis, reverse, stages=(), carry=()):
    count = lax.axis_size(axis)
    heads, size, width = value.shape
    win_value, win_decay = value, decay
    res_value, res_decay = jnp.zeros_like(value), jnp.ones_like(decay)
    step = 1
    turn = 0
    while step < count:
        send = jnp.concatenate(
            [win_value, jnp.broadcast_to(win_decay[:, None, None], (heads, 8, width))], axis=1
        ).astype(jnp.bfloat16)
        if turn < len(stages):
            send, carry = lax.optimization_barrier((send, carry))
        got = shifted(send, axis, -step if reverse else step)
        if turn < len(stages):
            carry = stages[turn](carry)
        got_value = got[:, :size].astype(jnp.float32)
        got_decay = got[:, size, 0].astype(jnp.float32)
        win_value = win_value + win_decay[:, None, None] * got_value
        res_value = res_value + res_decay[:, None, None] * got_value
        win_decay = win_decay * got_decay
        res_decay = res_decay * got_decay
        step *= 2
        turn += 1
    for stage in stages[turn:]:
        carry = stage(carry)
    return res_value, carry


def linear_parts(gates):
    running = jnp.cumsum(gates, axis=1)
    block_total = running[:, -1]
    length = gates.shape[1]
    row_ids = lax.broadcasted_iota(jnp.int32, (length, length), 0)
    col_ids = lax.broadcasted_iota(jnp.int32, (length, length), 1)
    lower = (col_ids <= row_ids)[None]
    spread = jnp.where(lower, running[:, :, None] - running[:, None, :], 0.0)
    window_weight = jnp.where(lower, jnp.exp(spread), 0.0)
    tail_weight = jnp.exp(block_total[:, None] - running)
    return (jnp.exp(running), jnp.exp(block_total), tail_weight, window_weight)


def body(soft_q, soft_k, soft_v, soft_dout, lin_q, lin_k, lin_v, lin_gate, lin_dy):
    heads_here = lin_gate.shape[0]
    length = soft_q.shape[0]
    head_size = soft_q.shape[1] // heads_here
    factor = head_size ** (-0.5)
    position = lax.axis_index("ctx")
    has_prev = position > 0
    has_next = position < lax.axis_size("ctx") - 1
    shape_heads = (length, heads_here, head_size)
    shape_flat = (length, heads_here * head_size)
    row_ids = lax.broadcasted_iota(jnp.int32, (length, length), 0)
    col_ids = lax.broadcasted_iota(jnp.int32, (length, length), 1)
    own_mask = (col_ids <= row_ids)[None]
    prev_mask = ((col_ids > row_ids) & has_prev)[None]
    next_mask = ((col_ids > row_ids) & has_next)[None]

    lin_queries = lin_q.reshape(shape_heads)
    lin_keys = lin_k.reshape(shape_heads)
    lin_values = lin_v.reshape(shape_heads)
    query_f = lin_queries.astype(jnp.float32)
    key_f = lin_keys.astype(jnp.float32)
    value_f = lin_values.astype(jnp.float32)
    lead_weight, block_decay, tail_weight, window_weight = linear_parts(lin_gate)
    summary = jnp.einsum("hs,shd,she->hde", tail_weight, key_f, value_f, precision=exact_mode)

    def cols(array, head):
        return array[:, head * head_size:(head + 1) * head_size]

    def mm(a, b):
        return lax.dot_general(a, b, (((1,), (1,)), ((), ())), preferred_element_type=jnp.float32)

    def mm_t(a, b):
        return lax.dot_general(a, b, (((0,), (0,)), ((), ())), preferred_element_type=jnp.float32)

    def mm_n(a, b):
        return lax.dot_general(a, b, (((1,), (0,)), ((), ())), preferred_element_type=jnp.float32)

    own_mask2 = own_mask[0]
    prev_mask2 = prev_mask[0]
    next_mask2 = next_mask[0]
    heads_list = range(heads_here)

    received = {}

    def soft_sends(c):
        c = dict(c)
        received["prev"] = shifted(jnp.stack((c["soft_k"], c["soft_v"])), "ctx", 1)
        received["next"] = shifted(jnp.stack((c["soft_q"], c["soft_dout"])), "ctx", -1)
        lin_scores = jnp.einsum(
            "thd,shd->hts", c["lin_q"].reshape(shape_heads), c["lin_k"].reshape(shape_heads),
            preferred_element_type=jnp.float32,
        )
        c["attended"] = (lin_scores * factor * c["window_weight"]).astype(jnp.bfloat16)
        c["lin_intra"] = jnp.einsum(
            "hts,she->the", c["attended"], c["lin_v"].reshape(shape_heads),
            preferred_element_type=jnp.float32,
        )
        return c

    def soft_heads(part, last):
        def stage(c):
            c = dict(c)
            keys_prev, values_prev = received["prev"][0], received["prev"][1]
            for h in part:
                scores_own = mm(cols(c["soft_q"], h), cols(c["soft_k"], h)) * factor
                dprob_own = mm(cols(c["soft_dout"], h), cols(c["soft_v"], h))
                scores_prev = mm(cols(c["soft_q"], h), cols(keys_prev, h)) * factor
                row_max = jnp.maximum(
                    jnp.max(jnp.where(own_mask2, scores_own, masked_fill), axis=1),
                    jnp.max(jnp.where(prev_mask2, scores_prev, masked_fill), axis=1),
                )
                total = jnp.sum(
                    jnp.where(own_mask2, jnp.exp(scores_own - row_max[:, None]), 0.0), axis=1
                )
                total = total + jnp.sum(
                    jnp.where(prev_mask2, jnp.exp(scores_prev - row_max[:, None]), 0.0), axis=1
                )
                log_total = row_max + jnp.log(total)
                probs_own = jnp.where(own_mask2, jnp.exp(scores_own - log_total[:, None]), 0.0)
                probs_prev = jnp.where(
                    prev_mask2, jnp.exp(scores_prev - log_total[:, None]), 0.0
                )
                dprob_prev = mm(cols(c["soft_dout"], h), cols(values_prev, h))
                row_delta = jnp.sum(probs_own * dprob_own, axis=1) + jnp.sum(
                    probs_prev * dprob_prev, axis=1
                )
                ds_own = (probs_own * (dprob_own - row_delta[:, None])).astype(jnp.bfloat16)
                ds_prev = (probs_prev * (dprob_prev - row_delta[:, None])).astype(jnp.bfloat16)
                c["stat%d" % h] = jnp.stack((log_total, row_delta))
                c["dq%d" % h] = (
                    mm_n(ds_own, cols(c["soft_k"], h)) + mm_n(ds_prev, cols(keys_prev, h))
                ) * factor
                c["dk%d" % h] = mm_t(ds_own, cols(c["soft_q"], h)) * factor
                c["dv%d" % h] = mm_t(probs_own.astype(jnp.bfloat16), cols(c["soft_dout"], h))
            if last:
                received["stats"] = shifted(
                    jnp.stack([c.pop("stat%d" % h) for h in heads_list], axis=1), "ctx", -1
                )
                c["grad_q"] = jnp.concatenate([c.pop("dq%d" % h) for h in heads_list], axis=1)
                c["grad_k"] = [c.pop("dk%d" % h) for h in heads_list]
                c["grad_v"] = [c.pop("dv%d" % h) for h in heads_list]
            return c

        return stage

    split = (heads_here + 1) // 2
    soft_stats = soft_heads(heads_list[:split], False)
    soft_grads = soft_heads(heads_list[split:], True)

    carry = dict(
        soft_q=soft_q, soft_k=soft_k, soft_v=soft_v, soft_dout=soft_dout,
        lin_q=lin_q, lin_k=lin_k, lin_v=lin_v, window_weight=window_weight,
    )
    state_in, carry = exclusive_scan(
        block_decay, summary, "ctx", False, (soft_sends, soft_stats, soft_grads), carry
    )

    lin_output = carry["lin_intra"] + factor * lead_weight.T[:, :, None] * jnp.einsum(
        "thd,hde->the", query_f, state_in, precision=exact_mode
    )
    dy_f = lin_dy.reshape(shape_heads).astype(jnp.float32)
    norm_sums = lax.psum(
        (jnp.sum(lin_output * lin_output, axis=(1, 2)), jnp.sum(lin_output * dy_f, axis=(1, 2))),
        "head",
    )
    width_all = LOCAL_HEADS * HEAD_DIM
    rms_value = jnp.sqrt(norm_sums[0] / width_all + 1e-06)
    lin_grad = (
        dy_f / rms_value[:, None, None]
        - lin_output * (norm_sums[1] / (rms_value**3 * width_all))[:, None, None]
    )
    lin_grad_b = lin_grad.astype(jnp.bfloat16)
    lin_grad_f = lin_grad_b.astype(jnp.float32)
    grad_summary = factor * jnp.einsum(
        "ht,thd,the->hde", lead_weight, query_f, lin_grad_f, precision=exact_mode
    )

    def linear_own(c):
        c = dict(c)
        grad_b = c["lin_grad_b"]
        grad_raw = jnp.einsum(
            "the,she->hts", grad_b, c["lin_v"].reshape(shape_heads),
            preferred_element_type=jnp.float32,
        )
        grad_scores = (grad_raw * factor * c["window_weight"]).astype(jnp.bfloat16)
        lin_grad_q = jnp.einsum(
            "hts,shd->thd", grad_scores, c["lin_k"].reshape(shape_heads),
            preferred_element_type=jnp.float32,
        )
        lin_grad_q = lin_grad_q + factor * c["lead_weight"].T[:, :, None] * jnp.einsum(
            "hde,the->thd", c["state_in"], grad_b.astype(jnp.float32), precision=exact_mode
        )
        c["lin_dq"] = lin_grad_q.astype(jnp.bfloat16).reshape(shape_flat)
        c["lin_dk"] = jnp.einsum(
            "hts,thd->shd", grad_scores, c["lin_q"].reshape(shape_heads),
            preferred_element_type=jnp.float32,
        )
        c["lin_dv"] = jnp.einsum(
            "hts,the->she", c["attended"], grad_b, preferred_element_type=jnp.float32
        )
        for name in ("lin_grad_b", "state_in", "lead_weight", "attended", "window_weight"):
            del c[name]
        return c

    def soft_next_heads(part, last):
        def stage(c):
            c = dict(c)
            queries_next, grad_out_next = received["next"][0], received["next"][1]
            stats_next = received["stats"]
            for h in part:
                scores_next = mm(cols(queries_next, h), cols(c["soft_k"], h)) * factor
                probs_next = jnp.where(
                    next_mask2, jnp.exp(scores_next - stats_next[0, h][:, None]), 0.0
                )
                dprob_next = mm(cols(grad_out_next, h), cols(c["soft_v"], h))
                ds_next = (probs_next * (dprob_next - stats_next[1, h][:, None])).astype(
                    jnp.bfloat16
                )
                c["grad_k"][h] = (
                    c["grad_k"][h] + mm_t(ds_next, cols(queries_next, h)) * factor
                ).astype(jnp.bfloat16)
                c["grad_v"][h] = (
                    c["grad_v"][h]
                    + mm_t(probs_next.astype(jnp.bfloat16), cols(grad_out_next, h))
                ).astype(jnp.bfloat16)
            if last:
                c["soft_dk"] = jnp.concatenate(c.pop("grad_k"), axis=1)
                c["soft_dv"] = jnp.concatenate(c.pop("grad_v"), axis=1)
            return c

        return stage

    soft_next_scores = soft_next_heads(heads_list[:split], False)
    soft_next_grads = soft_next_heads(heads_list[split:], True)

    late = dict(
        lin_grad_b=lin_grad_b, state_in=state_in, lead_weight=lead_weight,
        attended=carry["attended"], window_weight=window_weight,
        lin_q=lin_q, lin_k=lin_k, lin_v=lin_v,
        soft_k=soft_k, soft_v=soft_v,
        grad_k=carry["grad_k"], grad_v=carry["grad_v"],
    )
    grad_in, late = exclusive_scan(
        block_decay, grad_summary, "ctx", True, (linear_own, soft_next_scores, soft_next_grads),
        late,
    )
    lin_grad_k = late["lin_dk"] + tail_weight.T[:, :, None] * jnp.einsum(
        "hde,she->shd", grad_in, value_f, precision=exact_mode
    )
    lin_grad_v = late["lin_dv"] + tail_weight.T[:, :, None] * jnp.einsum(
        "hde,shd->she", grad_in, key_f, precision=exact_mode
    )
    return (
        carry["grad_q"].astype(jnp.bfloat16),
        late["soft_dk"],
        late["soft_dv"],
        late["lin_dq"],
        lin_grad_k.astype(jnp.bfloat16).reshape(shape_flat),
        lin_grad_v.astype(jnp.bfloat16).reshape(shape_flat),
    )


def solution(mesh):
    in_specs = (
        P("ctx", "head"),
        P("ctx", "head"),
        P("ctx", "head"),
        P("ctx", "head"),
        P("ctx", "head"),
        P("ctx", "head"),
        P("ctx", "head"),
        P("head", "ctx"),
        P("ctx", "head"),
    )
    out_specs = (
        P("ctx", "head"),
        P("ctx", "head"),
        P("ctx", "head"),
        P("ctx", "head"),
        P("ctx", "head"),
        P("ctx", "head"),
    )
    return jax.shard_map(body, mesh=mesh, in_specs=in_specs, out_specs=out_specs, check_vma=False)
```

```python
import jax
import jax.numpy as jnp
from jax import lax
from jax.sharding import PartitionSpec as P

LOCAL_HEADS = 16
HEAD_DIM = 128


masked_fill = -1e30
exact_mode = lax.Precision.HIGHEST


def shifted(x, axis, by):
    peers = lax.axis_size(axis)
    pairs = [(i, i + by) for i in range(peers) if 0 <= i + by < peers]
    return lax.ppermute(x, axis, pairs)


def exclusive_scan(decay, value, axis, reverse, stages=(), carry=()):
    count = lax.axis_size(axis)
    heads, size, width = value.shape
    win_value, win_decay = value, decay
    res_value, res_decay = jnp.zeros_like(value), jnp.ones_like(decay)
    step = 1
    turn = 0
    while step < count:
        send = jnp.concatenate(
            [win_value, jnp.broadcast_to(win_decay[:, None, None], (heads, 8, width))], axis=1
        ).astype(jnp.bfloat16)
        if turn < len(stages):
            send, carry = lax.optimization_barrier((send, carry))
        got = shifted(send, axis, -step if reverse else step)
        if turn < len(stages):
            carry = stages[turn](carry)
        got_value = got[:, :size].astype(jnp.float32)
        got_decay = got[:, size, 0].astype(jnp.float32)
        win_value = win_value + win_decay[:, None, None] * got_value
        res_value = res_value + res_decay[:, None, None] * got_value
        win_decay = win_decay * got_decay
        res_decay = res_decay * got_decay
        step *= 2
        turn += 1
    for stage in stages[turn:]:
        carry = stage(carry)
    return res_value, carry


def linear_parts(gates):
    running = jnp.cumsum(gates, axis=1)
    block_total = running[:, -1]
    length = gates.shape[1]
    row_ids = lax.broadcasted_iota(jnp.int32, (length, length), 0)
    col_ids = lax.broadcasted_iota(jnp.int32, (length, length), 1)
    lower = (col_ids <= row_ids)[None]
    spread = jnp.where(lower, running[:, :, None] - running[:, None, :], 0.0)
    window_weight = jnp.where(lower, jnp.exp(spread), 0.0)
    tail_weight = jnp.exp(block_total[:, None] - running)
    return (jnp.exp(running), jnp.exp(block_total), tail_weight, window_weight)


def body(soft_q, soft_k, soft_v, soft_dout, lin_q, lin_k, lin_v, lin_gate, lin_dy):
    heads_here = lin_gate.shape[0]
    length = soft_q.shape[0]
    head_size = soft_q.shape[1] // heads_here
    factor = head_size ** (-0.5)
    position = lax.axis_index("ctx")
    has_prev = position > 0
    has_next = position < lax.axis_size("ctx") - 1
    shape_heads = (length, heads_here, head_size)
    shape_flat = (length, heads_here * head_size)
    row_ids = lax.broadcasted_iota(jnp.int32, (length, length), 0)
    col_ids = lax.broadcasted_iota(jnp.int32, (length, length), 1)
    own_mask = (col_ids <= row_ids)[None]
    prev_mask = ((col_ids > row_ids) & has_prev)[None]
    next_mask = ((col_ids > row_ids) & has_next)[None]

    lin_queries = lin_q.reshape(shape_heads)
    lin_keys = lin_k.reshape(shape_heads)
    lin_values = lin_v.reshape(shape_heads)
    query_f = lin_queries.astype(jnp.float32)
    key_f = lin_keys.astype(jnp.float32)
    value_f = lin_values.astype(jnp.float32)
    lead_weight, block_decay, tail_weight, window_weight = linear_parts(lin_gate)
    summary = jnp.einsum("hs,shd,she->hde", tail_weight, key_f, value_f, precision=exact_mode)

    def cols(array, head):
        return array[:, head * head_size:(head + 1) * head_size]

    def mm(a, b):
        return lax.dot_general(a, b, (((1,), (1,)), ((), ())), preferred_element_type=jnp.float32)

    def mm_t(a, b):
        return lax.dot_general(a, b, (((0,), (0,)), ((), ())), preferred_element_type=jnp.float32)

    def mm_n(a, b):
        return lax.dot_general(a, b, (((1,), (0,)), ((), ())), preferred_element_type=jnp.float32)

    own_mask2 = own_mask[0]
    prev_mask2 = prev_mask[0]
    next_mask2 = next_mask[0]
    heads_list = range(heads_here)

    received = {}

    def soft_sends(c):
        c = dict(c)
        received["prev"] = shifted(jnp.stack((c["soft_k"], c["soft_v"])), "ctx", 1)
        received["next"] = shifted(jnp.stack((c["soft_q"], c["soft_dout"])), "ctx", -1)
        lin_scores = jnp.einsum(
            "thd,shd->hts", c["lin_q"].reshape(shape_heads), c["lin_k"].reshape(shape_heads),
            preferred_element_type=jnp.float32,
        )
        c["attended"] = (lin_scores * factor * c["window_weight"]).astype(jnp.bfloat16)
        c["lin_intra"] = jnp.einsum(
            "hts,she->the", c["attended"], c["lin_v"].reshape(shape_heads),
            preferred_element_type=jnp.float32,
        )
        return c

    def soft_heads(part, last):
        def stage(c):
            c = dict(c)
            keys_prev, values_prev = received["prev"][0], received["prev"][1]
            for h in part:
                scores_own = mm(cols(c["soft_q"], h), cols(c["soft_k"], h)) * factor
                dprob_own = mm(cols(c["soft_dout"], h), cols(c["soft_v"], h))
                scores_prev = mm(cols(c["soft_q"], h), cols(keys_prev, h)) * factor
                row_max = jnp.maximum(
                    jnp.max(jnp.where(own_mask2, scores_own, masked_fill), axis=1),
                    jnp.max(jnp.where(prev_mask2, scores_prev, masked_fill), axis=1),
                )
                total = jnp.sum(
                    jnp.where(own_mask2, jnp.exp(scores_own - row_max[:, None]), 0.0), axis=1
                )
                total = total + jnp.sum(
                    jnp.where(prev_mask2, jnp.exp(scores_prev - row_max[:, None]), 0.0), axis=1
                )
                log_total = row_max + jnp.log(total)
                probs_own = jnp.where(own_mask2, jnp.exp(scores_own - log_total[:, None]), 0.0)
                probs_prev = jnp.where(
                    prev_mask2, jnp.exp(scores_prev - log_total[:, None]), 0.0
                )
                dprob_prev = mm(cols(c["soft_dout"], h), cols(values_prev, h))
                row_delta = jnp.sum(probs_own * dprob_own, axis=1) + jnp.sum(
                    probs_prev * dprob_prev, axis=1
                )
                ds_own = (probs_own * (dprob_own - row_delta[:, None])).astype(jnp.bfloat16)
                ds_prev = (probs_prev * (dprob_prev - row_delta[:, None])).astype(jnp.bfloat16)
                c["stat%d" % h] = jnp.stack((log_total, row_delta))
                c["dq%d" % h] = (
                    mm_n(ds_own, cols(c["soft_k"], h)) + mm_n(ds_prev, cols(keys_prev, h))
                ) * factor
                c["dk%d" % h] = mm_t(ds_own, cols(c["soft_q"], h)) * factor
                c["dv%d" % h] = mm_t(probs_own.astype(jnp.bfloat16), cols(c["soft_dout"], h))
            if last:
                received["stats"] = shifted(
                    jnp.stack([c.pop("stat%d" % h) for h in heads_list], axis=1), "ctx", -1
                )
                c["grad_q"] = jnp.concatenate([c.pop("dq%d" % h) for h in heads_list], axis=1)
                c["grad_k"] = [c.pop("dk%d" % h) for h in heads_list]
                c["grad_v"] = [c.pop("dv%d" % h) for h in heads_list]
            return c

        return stage

    split = max(1, heads_here // 4)
    soft_stats = soft_heads(heads_list[:split], False)
    soft_grads = soft_heads(heads_list[split:], True)

    carry = dict(
        soft_q=soft_q, soft_k=soft_k, soft_v=soft_v, soft_dout=soft_dout,
        lin_q=lin_q, lin_k=lin_k, lin_v=lin_v, window_weight=window_weight,
    )
    state_in, carry = exclusive_scan(
        block_decay, summary, "ctx", False, (soft_sends, soft_stats, soft_grads), carry
    )

    lin_output = carry["lin_intra"] + factor * lead_weight.T[:, :, None] * jnp.einsum(
        "thd,hde->the", query_f, state_in, precision=exact_mode
    )
    dy_f = lin_dy.reshape(shape_heads).astype(jnp.float32)
    norm_sums = lax.psum(
        (jnp.sum(lin_output * lin_output, axis=(1, 2)), jnp.sum(lin_output * dy_f, axis=(1, 2))),
        "head",
    )
    width_all = LOCAL_HEADS * HEAD_DIM
    rms_value = jnp.sqrt(norm_sums[0] / width_all + 1e-06)
    lin_grad = (
        dy_f / rms_value[:, None, None]
        - lin_output * (norm_sums[1] / (rms_value**3 * width_all))[:, None, None]
    )
    lin_grad_b = lin_grad.astype(jnp.bfloat16)
    lin_grad_f = lin_grad_b.astype(jnp.float32)
    grad_summary = factor * jnp.einsum(
        "ht,thd,the->hde", lead_weight, query_f, lin_grad_f, precision=exact_mode
    )

    def linear_own(c):
        c = dict(c)
        grad_b = c["lin_grad_b"]
        grad_raw = jnp.einsum(
            "the,she->hts", grad_b, c["lin_v"].reshape(shape_heads),
            preferred_element_type=jnp.float32,
        )
        grad_scores = (grad_raw * factor * c["window_weight"]).astype(jnp.bfloat16)
        lin_grad_q = jnp.einsum(
            "hts,shd->thd", grad_scores, c["lin_k"].reshape(shape_heads),
            preferred_element_type=jnp.float32,
        )
        lin_grad_q = lin_grad_q + factor * c["lead_weight"].T[:, :, None] * jnp.einsum(
            "hde,the->thd", c["state_in"], grad_b.astype(jnp.float32), precision=exact_mode
        )
        c["lin_dq"] = lin_grad_q.astype(jnp.bfloat16).reshape(shape_flat)
        c["lin_dk"] = jnp.einsum(
            "hts,thd->shd", grad_scores, c["lin_q"].reshape(shape_heads),
            preferred_element_type=jnp.float32,
        )
        c["lin_dv"] = jnp.einsum(
            "hts,the->she", c["attended"], grad_b, preferred_element_type=jnp.float32
        )
        for name in ("lin_grad_b", "state_in", "lead_weight", "attended", "window_weight"):
            del c[name]
        return c

    def soft_next_scores(c):
        c = dict(c)
        queries_next, grad_out_next = received["next"][0], received["next"][1]
        stats_next = received["stats"]
        ds_next, p_next = [], []
        for h in heads_list:
            scores_next = mm(cols(queries_next, h), cols(c["soft_k"], h)) * factor
            probs_next = jnp.where(
                next_mask2, jnp.exp(scores_next - stats_next[0, h][:, None]), 0.0
            )
            dprob_next = mm(cols(grad_out_next, h), cols(c["soft_v"], h))
            ds_next.append(
                (probs_next * (dprob_next - stats_next[1, h][:, None])).astype(jnp.bfloat16)
            )
            p_next.append(probs_next.astype(jnp.bfloat16))
        c["dscore_next"], c["probs_next_b"] = ds_next, p_next
        return c

    def soft_next_grads(c):
        c = dict(c)
        queries_next, grad_out_next = received["next"][0], received["next"][1]
        dk, dv = [], []
        for h in heads_list:
            dk.append(
                c["grad_k"][h] + mm_t(c["dscore_next"][h], cols(queries_next, h)) * factor
            )
            dv.append(c["grad_v"][h] + mm_t(c["probs_next_b"][h], cols(grad_out_next, h)))
        c["soft_dk"] = jnp.concatenate(dk, axis=1).astype(jnp.bfloat16)
        c["soft_dv"] = jnp.concatenate(dv, axis=1).astype(jnp.bfloat16)
        return c

    late = dict(
        lin_grad_b=lin_grad_b, state_in=state_in, lead_weight=lead_weight,
        attended=carry["attended"], window_weight=window_weight,
        lin_q=lin_q, lin_k=lin_k, lin_v=lin_v,
        soft_k=soft_k, soft_v=soft_v,
        grad_k=carry["grad_k"], grad_v=carry["grad_v"],
    )
    grad_in, late = exclusive_scan(
        block_decay, grad_summary, "ctx", True, (linear_own, soft_next_scores, soft_next_grads),
        late,
    )
    lin_grad_k = late["lin_dk"] + tail_weight.T[:, :, None] * jnp.einsum(
        "hde,she->shd", grad_in, value_f, precision=exact_mode
    )
    lin_grad_v = late["lin_dv"] + tail_weight.T[:, :, None] * jnp.einsum(
        "hde,shd->she", grad_in, key_f, precision=exact_mode
    )
    return (
        carry["grad_q"].astype(jnp.bfloat16),
        late["soft_dk"],
        late["soft_dv"],
        late["lin_dq"],
        lin_grad_k.astype(jnp.bfloat16).reshape(shape_flat),
        lin_grad_v.astype(jnp.bfloat16).reshape(shape_flat),
    )


def solution(mesh):
    in_specs = (
        P("ctx", "head"),
        P("ctx", "head"),
        P("ctx", "head"),
        P("ctx", "head"),
        P("ctx", "head"),
        P("ctx", "head"),
        P("ctx", "head"),
        P("head", "ctx"),
        P("ctx", "head"),
    )
    out_specs = (
        P("ctx", "head"),
        P("ctx", "head"),
        P("ctx", "head"),
        P("ctx", "head"),
        P("ctx", "head"),
        P("ctx", "head"),
    )
    return jax.shard_map(body, mesh=mesh, in_specs=in_specs, out_specs=out_specs, check_vma=False)
```

```python
import jax
import jax.numpy as jnp
from jax import lax
from jax.sharding import PartitionSpec as P

LOCAL_HEADS = 16
HEAD_DIM = 128


masked_fill = -1e30
exact_mode = lax.Precision.HIGHEST


def shifted(x, axis, by):
    peers = lax.axis_size(axis)
    pairs = [(i, i + by) for i in range(peers) if 0 <= i + by < peers]
    return lax.ppermute(x, axis, pairs)


def exclusive_scan(decay, value, axis, reverse, stages=(), carry=()):
    count = lax.axis_size(axis)
    heads, size, width = value.shape
    win_value, win_decay = value, decay
    res_value, res_decay = jnp.zeros_like(value), jnp.ones_like(decay)
    step = 1
    turn = 0
    while step < count:
        send = jnp.concatenate(
            [win_value, jnp.broadcast_to(win_decay[:, None, None], (heads, 8, width))], axis=1
        ).astype(jnp.bfloat16)
        if turn < len(stages):
            send, carry = lax.optimization_barrier((send, carry))
        got = shifted(send, axis, -step if reverse else step)
        if turn < len(stages):
            carry = stages[turn](carry)
        got_value = got[:, :size].astype(jnp.float32)
        got_decay = got[:, size, 0].astype(jnp.float32)
        win_value = win_value + win_decay[:, None, None] * got_value
        res_value = res_value + res_decay[:, None, None] * got_value
        win_decay = win_decay * got_decay
        res_decay = res_decay * got_decay
        step *= 2
        turn += 1
    for stage in stages[turn:]:
        carry = stage(carry)
    return res_value, carry


def linear_parts(gates):
    running = jnp.cumsum(gates, axis=1)
    block_total = running[:, -1]
    length = gates.shape[1]
    row_ids = lax.broadcasted_iota(jnp.int32, (length, length), 0)
    col_ids = lax.broadcasted_iota(jnp.int32, (length, length), 1)
    lower = (col_ids <= row_ids)[None]
    spread = jnp.where(lower, running[:, :, None] - running[:, None, :], 0.0)
    window_weight = jnp.where(lower, jnp.exp(spread), 0.0)
    tail_weight = jnp.exp(block_total[:, None] - running)
    return (jnp.exp(running), jnp.exp(block_total), tail_weight, window_weight)


def body(soft_q, soft_k, soft_v, soft_dout, lin_q, lin_k, lin_v, lin_gate, lin_dy):
    heads_here = lin_gate.shape[0]
    length = soft_q.shape[0]
    head_size = soft_q.shape[1] // heads_here
    factor = head_size ** (-0.5)
    position = lax.axis_index("ctx")
    has_prev = position > 0
    has_next = position < lax.axis_size("ctx") - 1
    shape_heads = (length, heads_here, head_size)
    shape_flat = (length, heads_here * head_size)
    row_ids = lax.broadcasted_iota(jnp.int32, (length, length), 0)
    col_ids = lax.broadcasted_iota(jnp.int32, (length, length), 1)
    own_mask = (col_ids <= row_ids)[None]
    prev_mask = ((col_ids > row_ids) & has_prev)[None]
    next_mask = ((col_ids > row_ids) & has_next)[None]

    lin_queries = lin_q.reshape(shape_heads)
    lin_keys = lin_k.reshape(shape_heads)
    lin_values = lin_v.reshape(shape_heads)
    query_f = lin_queries.astype(jnp.float32)
    key_f = lin_keys.astype(jnp.float32)
    value_f = lin_values.astype(jnp.float32)
    lead_weight, block_decay, tail_weight, window_weight = linear_parts(lin_gate)
    summary = jnp.einsum("hs,shd,she->hde", tail_weight, key_f, value_f, precision=exact_mode)

    def cols(array, head):
        return array[:, head * head_size:(head + 1) * head_size]

    def mm(a, b):
        return lax.dot_general(a, b, (((1,), (1,)), ((), ())), preferred_element_type=jnp.float32)

    def mm_t(a, b):
        return lax.dot_general(a, b, (((0,), (0,)), ((), ())), preferred_element_type=jnp.float32)

    def mm_n(a, b):
        return lax.dot_general(a, b, (((1,), (0,)), ((), ())), preferred_element_type=jnp.float32)

    own_mask2 = own_mask[0]
    prev_mask2 = prev_mask[0]
    next_mask2 = next_mask[0]
    heads_list = range(heads_here)

    received = {}

    def soft_sends(c):
        c = dict(c)
        received["prev"] = shifted(jnp.stack((c["soft_k"], c["soft_v"])), "ctx", 1)
        received["next"] = shifted(jnp.stack((c["soft_q"], c["soft_dout"])), "ctx", -1)
        lin_scores = jnp.einsum(
            "thd,shd->hts", c["lin_q"].reshape(shape_heads), c["lin_k"].reshape(shape_heads),
            preferred_element_type=jnp.float32,
        )
        c["attended"] = (lin_scores * factor * c["window_weight"]).astype(jnp.bfloat16)
        c["lin_intra"] = jnp.einsum(
            "hts,she->the", c["attended"], c["lin_v"].reshape(shape_heads),
            preferred_element_type=jnp.float32,
        )
        return c

    def soft_heads(part, last):
        def stage(c):
            c = dict(c)
            keys_prev, values_prev = received["prev"][0], received["prev"][1]
            for h in part:
                scores_own = mm(cols(c["soft_q"], h), cols(c["soft_k"], h)) * factor
                dprob_own = mm(cols(c["soft_dout"], h), cols(c["soft_v"], h))
                scores_prev = mm(cols(c["soft_q"], h), cols(keys_prev, h)) * factor
                row_max = jnp.maximum(
                    jnp.max(jnp.where(own_mask2, scores_own, masked_fill), axis=1),
                    jnp.max(jnp.where(prev_mask2, scores_prev, masked_fill), axis=1),
                )
                total = jnp.sum(
                    jnp.where(own_mask2, jnp.exp(scores_own - row_max[:, None]), 0.0), axis=1
                )
                total = total + jnp.sum(
                    jnp.where(prev_mask2, jnp.exp(scores_prev - row_max[:, None]), 0.0), axis=1
                )
                log_total = row_max + jnp.log(total)
                probs_own = jnp.where(own_mask2, jnp.exp(scores_own - log_total[:, None]), 0.0)
                probs_prev = jnp.where(
                    prev_mask2, jnp.exp(scores_prev - log_total[:, None]), 0.0
                )
                dprob_prev = mm(cols(c["soft_dout"], h), cols(values_prev, h))
                row_delta = jnp.sum(probs_own * dprob_own, axis=1) + jnp.sum(
                    probs_prev * dprob_prev, axis=1
                )
                ds_own = (probs_own * (dprob_own - row_delta[:, None])).astype(jnp.bfloat16)
                ds_prev = (probs_prev * (dprob_prev - row_delta[:, None])).astype(jnp.bfloat16)
                c["stat%d" % h] = jnp.stack((log_total, row_delta))
                c["dq%d" % h] = (
                    mm_n(ds_own, cols(c["soft_k"], h)) + mm_n(ds_prev, cols(keys_prev, h))
                ) * factor
                c["dk%d" % h] = mm_t(ds_own, cols(c["soft_q"], h)) * factor
                c["dv%d" % h] = mm_t(probs_own.astype(jnp.bfloat16), cols(c["soft_dout"], h))
            if last:
                stats = jnp.stack([c.pop("stat%d" % h) for h in heads_list], axis=1)
                received["stats"] = shifted(
                    stats.reshape(2 * heads_here, length).T, "ctx", -1
                )
                c["grad_q"] = jnp.concatenate([c.pop("dq%d" % h) for h in heads_list], axis=1)
                c["grad_k"] = [c.pop("dk%d" % h) for h in heads_list]
                c["grad_v"] = [c.pop("dv%d" % h) for h in heads_list]
            return c

        return stage

    split = (heads_here + 1) // 2
    soft_stats = soft_heads(heads_list[:split], False)
    soft_grads = soft_heads(heads_list[split:], True)

    carry = dict(
        soft_q=soft_q, soft_k=soft_k, soft_v=soft_v, soft_dout=soft_dout,
        lin_q=lin_q, lin_k=lin_k, lin_v=lin_v, window_weight=window_weight,
    )
    state_in, carry = exclusive_scan(
        block_decay, summary, "ctx", False, (soft_sends, soft_stats, soft_grads), carry
    )

    lin_output = carry["lin_intra"] + factor * lead_weight.T[:, :, None] * jnp.einsum(
        "thd,hde->the", query_f, state_in, precision=exact_mode
    )
    dy_f = lin_dy.reshape(shape_heads).astype(jnp.float32)
    norm_sums = lax.psum(
        (jnp.sum(lin_output * lin_output, axis=(1, 2)), jnp.sum(lin_output * dy_f, axis=(1, 2))),
        "head",
    )
    width_all = LOCAL_HEADS * HEAD_DIM
    rms_value = jnp.sqrt(norm_sums[0] / width_all + 1e-06)
    lin_grad = (
        dy_f / rms_value[:, None, None]
        - lin_output * (norm_sums[1] / (rms_value**3 * width_all))[:, None, None]
    )
    lin_grad_b = lin_grad.astype(jnp.bfloat16)
    lin_grad_f = lin_grad_b.astype(jnp.float32)
    grad_summary = factor * jnp.einsum(
        "ht,thd,the->hde", lead_weight, query_f, lin_grad_f, precision=exact_mode
    )

    def linear_own(c):
        c = dict(c)
        grad_b = c["lin_grad_b"]
        grad_raw = jnp.einsum(
            "the,she->hts", grad_b, c["lin_v"].reshape(shape_heads),
            preferred_element_type=jnp.float32,
        )
        grad_scores = (grad_raw * factor * c["window_weight"]).astype(jnp.bfloat16)
        lin_grad_q = jnp.einsum(
            "hts,shd->thd", grad_scores, c["lin_k"].reshape(shape_heads),
            preferred_element_type=jnp.float32,
        )
        lin_grad_q = lin_grad_q + factor * c["lead_weight"].T[:, :, None] * jnp.einsum(
            "hde,the->thd", c["state_in"], grad_b.astype(jnp.float32), precision=exact_mode
        )
        c["lin_dq"] = lin_grad_q.astype(jnp.bfloat16).reshape(shape_flat)
        c["lin_dk"] = jnp.einsum(
            "hts,thd->shd", grad_scores, c["lin_q"].reshape(shape_heads),
            preferred_element_type=jnp.float32,
        )
        c["lin_dv"] = jnp.einsum(
            "hts,the->she", c["attended"], grad_b, preferred_element_type=jnp.float32
        )
        for name in ("lin_grad_b", "state_in", "lead_weight", "attended", "window_weight"):
            del c[name]
        return c

    def soft_next_scores(c):
        c = dict(c)
        queries_next, grad_out_next = received["next"][0], received["next"][1]
        stats_next = received["stats"]
        ds_next, p_next = [], []
        for h in heads_list:
            scores_next = mm(cols(queries_next, h), cols(c["soft_k"], h)) * factor
            probs_next = jnp.where(
                next_mask2, jnp.exp(scores_next - stats_next[:, h:h + 1]), 0.0
            )
            dprob_next = mm(cols(grad_out_next, h), cols(c["soft_v"], h))
            ds_next.append(
                (probs_next * (dprob_next - stats_next[:, heads_here + h:heads_here + h + 1])).astype(jnp.bfloat16)
            )
            p_next.append(probs_next.astype(jnp.bfloat16))
        c["dscore_next"], c["probs_next_b"] = ds_next, p_next
        return c

    def soft_next_grads(c):
        c = dict(c)
        queries_next, grad_out_next = received["next"][0], received["next"][1]
        dk, dv = [], []
        for h in heads_list:
            dk.append(
                c["grad_k"][h] + mm_t(c["dscore_next"][h], cols(queries_next, h)) * factor
            )
            dv.append(c["grad_v"][h] + mm_t(c["probs_next_b"][h], cols(grad_out_next, h)))
        c["soft_dk"] = jnp.concatenate(dk, axis=1).astype(jnp.bfloat16)
        c["soft_dv"] = jnp.concatenate(dv, axis=1).astype(jnp.bfloat16)
        return c

    late = dict(
        lin_grad_b=lin_grad_b, state_in=state_in, lead_weight=lead_weight,
        attended=carry["attended"], window_weight=window_weight,
        lin_q=lin_q, lin_k=lin_k, lin_v=lin_v,
        soft_k=soft_k, soft_v=soft_v,
        grad_k=carry["grad_k"], grad_v=carry["grad_v"],
    )
    grad_in, late = exclusive_scan(
        block_decay, grad_summary, "ctx", True, (linear_own, soft_next_scores, soft_next_grads),
        late,
    )
    lin_grad_k = late["lin_dk"] + tail_weight.T[:, :, None] * jnp.einsum(
        "hde,she->shd", grad_in, value_f, precision=exact_mode
    )
    lin_grad_v = late["lin_dv"] + tail_weight.T[:, :, None] * jnp.einsum(
        "hde,shd->she", grad_in, key_f, precision=exact_mode
    )
    return (
        carry["grad_q"].astype(jnp.bfloat16),
        late["soft_dk"],
        late["soft_dv"],
        late["lin_dq"],
        lin_grad_k.astype(jnp.bfloat16).reshape(shape_flat),
        lin_grad_v.astype(jnp.bfloat16).reshape(shape_flat),
    )


def solution(mesh):
    in_specs = (
        P("ctx", "head"),
        P("ctx", "head"),
        P("ctx", "head"),
        P("ctx", "head"),
        P("ctx", "head"),
        P("ctx", "head"),
        P("ctx", "head"),
        P("head", "ctx"),
        P("ctx", "head"),
    )
    out_specs = (
        P("ctx", "head"),
        P("ctx", "head"),
        P("ctx", "head"),
        P("ctx", "head"),
        P("ctx", "head"),
        P("ctx", "head"),
    )
    return jax.shard_map(body, mesh=mesh, in_specs=in_specs, out_specs=out_specs, check_vma=False)
```

```python
import jax
import jax.numpy as jnp
from jax import lax
from jax.sharding import PartitionSpec as P

LOCAL_HEADS = 16
HEAD_DIM = 128


masked_fill = -1e30
exact_mode = lax.Precision.HIGHEST


def shifted(x, axis, by):
    peers = lax.axis_size(axis)
    pairs = [(i, i + by) for i in range(peers) if 0 <= i + by < peers]
    return lax.ppermute(x, axis, pairs)


def exclusive_scan(decay, value, axis, reverse, stages=(), carry=()):
    count = lax.axis_size(axis)
    heads, size, width = value.shape
    win_value, win_decay = value, decay
    res_value, res_decay = jnp.zeros_like(value), jnp.ones_like(decay)
    step = 1
    turn = 0
    while step < count:
        send = jnp.concatenate(
            [win_value, jnp.broadcast_to(win_decay[:, None, None], (heads, 8, width))], axis=1
        ).astype(jnp.bfloat16)
        if turn < len(stages):
            send, carry = lax.optimization_barrier((send, carry))
        got = shifted(send, axis, -step if reverse else step)
        if turn < len(stages):
            carry = stages[turn](carry)
        got_value = got[:, :size].astype(jnp.float32)
        got_decay = got[:, size, 0].astype(jnp.float32)
        win_value = win_value + win_decay[:, None, None] * got_value
        res_value = res_value + res_decay[:, None, None] * got_value
        win_decay = win_decay * got_decay
        res_decay = res_decay * got_decay
        step *= 2
        turn += 1
    for stage in stages[turn:]:
        carry = stage(carry)
    return res_value, carry


def linear_parts(gates):
    running = jnp.cumsum(gates, axis=1)
    block_total = running[:, -1]
    length = gates.shape[1]
    row_ids = lax.broadcasted_iota(jnp.int32, (length, length), 0)
    col_ids = lax.broadcasted_iota(jnp.int32, (length, length), 1)
    lower = (col_ids <= row_ids)[None]
    spread = jnp.where(lower, running[:, :, None] - running[:, None, :], 0.0)
    window_weight = jnp.where(lower, jnp.exp(spread), 0.0)
    tail_weight = jnp.exp(block_total[:, None] - running)
    return (jnp.exp(running), jnp.exp(block_total), tail_weight, window_weight)


def body(soft_q, soft_k, soft_v, soft_dout, lin_q, lin_k, lin_v, lin_gate, lin_dy):
    heads_here = lin_gate.shape[0]
    length = soft_q.shape[0]
    head_size = soft_q.shape[1] // heads_here
    factor = head_size ** (-0.5)
    position = lax.axis_index("ctx")
    has_prev = position > 0
    has_next = position < lax.axis_size("ctx") - 1
    shape_heads = (length, heads_here, head_size)
    shape_flat = (length, heads_here * head_size)
    row_ids = lax.broadcasted_iota(jnp.int32, (length, length), 0)
    col_ids = lax.broadcasted_iota(jnp.int32, (length, length), 1)
    own_mask = (col_ids <= row_ids)[None]
    prev_mask = ((col_ids > row_ids) & has_prev)[None]
    next_mask = ((col_ids > row_ids) & has_next)[None]

    lin_queries = lin_q.reshape(shape_heads)
    lin_keys = lin_k.reshape(shape_heads)
    lin_values = lin_v.reshape(shape_heads)
    query_f = lin_queries.astype(jnp.float32)
    key_f = lin_keys.astype(jnp.float32)
    value_f = lin_values.astype(jnp.float32)
    lead_weight, block_decay, tail_weight, window_weight = linear_parts(lin_gate)
    summary = jnp.einsum("hs,shd,she->hde", tail_weight, key_f, value_f, precision=exact_mode)

    def cols(array, head):
        return array[:, head * head_size:(head + 1) * head_size]

    def mm(a, b):
        return lax.dot_general(a, b, (((1,), (1,)), ((), ())), preferred_element_type=jnp.float32)

    def mm_t(a, b):
        return lax.dot_general(a, b, (((0,), (0,)), ((), ())), preferred_element_type=jnp.float32)

    def mm_n(a, b):
        return lax.dot_general(a, b, (((1,), (0,)), ((), ())), preferred_element_type=jnp.float32)

    own_mask2 = own_mask[0]
    prev_mask2 = prev_mask[0]
    next_mask2 = next_mask[0]
    heads_list = range(heads_here)

    received = {}

    def soft_sends(c):
        c = dict(c)
        received["prev"] = shifted(jnp.stack((c["soft_k"], c["soft_v"])), "ctx", 1)
        received["next"] = shifted(jnp.stack((c["soft_q"], c["soft_dout"])), "ctx", -1)
        lin_scores = jnp.einsum(
            "thd,shd->hts", c["lin_q"].reshape(shape_heads), c["lin_k"].reshape(shape_heads),
            preferred_element_type=jnp.float32,
        )
        c["attended"] = (lin_scores * factor * c["window_weight"]).astype(jnp.bfloat16)
        c["lin_intra"] = jnp.einsum(
            "hts,she->the", c["attended"], c["lin_v"].reshape(shape_heads),
            preferred_element_type=jnp.float32,
        )
        return c

    def soft_heads(part, last):
        def stage(c):
            c = dict(c)
            keys_prev, values_prev = received["prev"][0], received["prev"][1]
            for h in part:
                scores_own = mm(cols(c["soft_q"], h), cols(c["soft_k"], h)) * factor
                dprob_own = mm(cols(c["soft_dout"], h), cols(c["soft_v"], h))
                scores_prev = mm(cols(c["soft_q"], h), cols(keys_prev, h)) * factor
                row_max = jnp.maximum(
                    jnp.max(jnp.where(own_mask2, scores_own, masked_fill), axis=1),
                    jnp.max(jnp.where(prev_mask2, scores_prev, masked_fill), axis=1),
                )
                total = jnp.sum(
                    jnp.where(own_mask2, jnp.exp(scores_own - row_max[:, None]), 0.0), axis=1
                )
                total = total + jnp.sum(
                    jnp.where(prev_mask2, jnp.exp(scores_prev - row_max[:, None]), 0.0), axis=1
                )
                log_total = row_max + jnp.log(total)
                probs_own = jnp.where(own_mask2, jnp.exp(scores_own - log_total[:, None]), 0.0)
                probs_prev = jnp.where(
                    prev_mask2, jnp.exp(scores_prev - log_total[:, None]), 0.0
                )
                dprob_prev = mm(cols(c["soft_dout"], h), cols(values_prev, h))
                row_delta = jnp.sum(probs_own * dprob_own, axis=1) + jnp.sum(
                    probs_prev * dprob_prev, axis=1
                )
                ds_own = (probs_own * (dprob_own - row_delta[:, None])).astype(jnp.bfloat16)
                ds_prev = (probs_prev * (dprob_prev - row_delta[:, None])).astype(jnp.bfloat16)
                c["stat%d" % h] = jnp.stack((log_total, row_delta))
                c["dq%d" % h] = (
                    mm_n(ds_own, cols(c["soft_k"], h)) + mm_n(ds_prev, cols(keys_prev, h))
                ) * factor
                c["dk%d" % h] = mm_t(ds_own, cols(c["soft_q"], h)) * factor
                c["dv%d" % h] = mm_t(probs_own.astype(jnp.bfloat16), cols(c["soft_dout"], h))
            if last:
                received["stats"] = shifted(
                    jnp.stack([c.pop("stat%d" % h) for h in heads_list], axis=1), "ctx", -1
                )
                c["grad_q"] = jnp.concatenate([c.pop("dq%d" % h) for h in heads_list], axis=1)
                c["grad_k"] = jnp.concatenate([c.pop("dk%d" % h) for h in heads_list], axis=1)
                c["grad_v"] = jnp.concatenate([c.pop("dv%d" % h) for h in heads_list], axis=1)
            return c

        return stage

    split = (heads_here + 1) // 2
    soft_stats = soft_heads(heads_list[:split], False)
    soft_grads = soft_heads(heads_list[split:], True)

    carry = dict(
        soft_q=soft_q, soft_k=soft_k, soft_v=soft_v, soft_dout=soft_dout,
        lin_q=lin_q, lin_k=lin_k, lin_v=lin_v, window_weight=window_weight,
    )
    state_in, carry = exclusive_scan(
        block_decay, summary, "ctx", False, (soft_sends, soft_stats, soft_grads), carry
    )

    lin_output = carry["lin_intra"] + factor * lead_weight.T[:, :, None] * jnp.einsum(
        "thd,hde->the", query_f, state_in, precision=exact_mode
    )
    dy_f = lin_dy.reshape(shape_heads).astype(jnp.float32)
    norm_sums = lax.psum(
        (jnp.sum(lin_output * lin_output, axis=(1, 2)), jnp.sum(lin_output * dy_f, axis=(1, 2))),
        "head",
    )
    width_all = LOCAL_HEADS * HEAD_DIM
    rms_value = jnp.sqrt(norm_sums[0] / width_all + 1e-06)
    lin_grad = (
        dy_f / rms_value[:, None, None]
        - lin_output * (norm_sums[1] / (rms_value**3 * width_all))[:, None, None]
    )
    lin_grad_b = lin_grad.astype(jnp.bfloat16)
    lin_grad_f = lin_grad_b.astype(jnp.float32)
    grad_summary = factor * jnp.einsum(
        "ht,thd,the->hde", lead_weight, query_f, lin_grad_f, precision=exact_mode
    )

    def linear_own(c):
        c = dict(c)
        grad_b = c["lin_grad_b"]
        grad_raw = jnp.einsum(
            "the,she->hts", grad_b, c["lin_v"].reshape(shape_heads),
            preferred_element_type=jnp.float32,
        )
        grad_scores = (grad_raw * factor * c["window_weight"]).astype(jnp.bfloat16)
        lin_grad_q = jnp.einsum(
            "hts,shd->thd", grad_scores, c["lin_k"].reshape(shape_heads),
            preferred_element_type=jnp.float32,
        )
        lin_grad_q = lin_grad_q + factor * c["lead_weight"].T[:, :, None] * jnp.einsum(
            "hde,the->thd", c["state_in"], grad_b.astype(jnp.float32), precision=exact_mode
        )
        c["lin_dq"] = lin_grad_q.astype(jnp.bfloat16).reshape(shape_flat)
        c["lin_dk"] = jnp.einsum(
            "hts,thd->shd", grad_scores, c["lin_q"].reshape(shape_heads),
            preferred_element_type=jnp.float32,
        )
        c["lin_dv"] = jnp.einsum(
            "hts,the->she", c["attended"], grad_b, preferred_element_type=jnp.float32
        )
        for name in ("lin_grad_b", "state_in", "lead_weight", "attended", "window_weight"):
            del c[name]
        return c

    def soft_next_scores(c):
        c = dict(c)
        queries_next, grad_out_next = received["next"][0], received["next"][1]
        stats_next = received["stats"]
        ds_next, p_next = [], []
        for h in heads_list:
            scores_next = mm(cols(queries_next, h), cols(c["soft_k"], h)) * factor
            probs_next = jnp.where(
                next_mask2, jnp.exp(scores_next - stats_next[0, h][:, None]), 0.0
            )
            dprob_next = mm(cols(grad_out_next, h), cols(c["soft_v"], h))
            ds_next.append(
                (probs_next * (dprob_next - stats_next[1, h][:, None])).astype(jnp.bfloat16)
            )
            p_next.append(probs_next.astype(jnp.bfloat16))
        c["dscore_next"], c["probs_next_b"] = ds_next, p_next
        return c

    def soft_next_grads(c):
        c = dict(c)
        queries_next, grad_out_next = received["next"][0], received["next"][1]
        dk, dv = [], []
        for h in heads_list:
            dk.append(
                cols(c["grad_k"], h) + mm_t(c["dscore_next"][h], cols(queries_next, h)) * factor
            )
            dv.append(
                cols(c["grad_v"], h) + mm_t(c["probs_next_b"][h], cols(grad_out_next, h))
            )
        c["soft_dk"] = jnp.concatenate(dk, axis=1).astype(jnp.bfloat16)
        c["soft_dv"] = jnp.concatenate(dv, axis=1).astype(jnp.bfloat16)
        return c

    late = dict(
        lin_grad_b=lin_grad_b, state_in=state_in, lead_weight=lead_weight,
        attended=carry["attended"], window_weight=window_weight,
        lin_q=lin_q, lin_k=lin_k, lin_v=lin_v,
        soft_k=soft_k, soft_v=soft_v,
        grad_k=carry["grad_k"], grad_v=carry["grad_v"],
    )
    grad_in, late = exclusive_scan(
        block_decay, grad_summary, "ctx", True, (linear_own, soft_next_scores, soft_next_grads),
        late,
    )
    lin_grad_k = late["lin_dk"] + tail_weight.T[:, :, None] * jnp.einsum(
        "hde,she->shd", grad_in, value_f, precision=exact_mode
    )
    lin_grad_v = late["lin_dv"] + tail_weight.T[:, :, None] * jnp.einsum(
        "hde,shd->she", grad_in, key_f, precision=exact_mode
    )
    return (
        carry["grad_q"].astype(jnp.bfloat16),
        late["soft_dk"],
        late["soft_dv"],
        late["lin_dq"],
        lin_grad_k.astype(jnp.bfloat16).reshape(shape_flat),
        lin_grad_v.astype(jnp.bfloat16).reshape(shape_flat),
    )


def solution(mesh):
    in_specs = (
        P("ctx", "head"),
        P("ctx", "head"),
        P("ctx", "head"),
        P("ctx", "head"),
        P("ctx", "head"),
        P("ctx", "head"),
        P("ctx", "head"),
        P("head", "ctx"),
        P("ctx", "head"),
    )
    out_specs = (
        P("ctx", "head"),
        P("ctx", "head"),
        P("ctx", "head"),
        P("ctx", "head"),
        P("ctx", "head"),
        P("ctx", "head"),
    )
    return jax.shard_map(body, mesh=mesh, in_specs=in_specs, out_specs=out_specs, check_vma=False)
```

```python
import jax
import jax.numpy as jnp
from jax import lax
from jax.sharding import PartitionSpec as P

LOCAL_HEADS = 16
HEAD_DIM = 128


masked_fill = -1e30
exact_mode = lax.Precision.HIGHEST


def shifted(x, axis, by):
    peers = lax.axis_size(axis)
    pairs = [(i, i + by) for i in range(peers) if 0 <= i + by < peers]
    return lax.ppermute(x, axis, pairs)


def exclusive_scan(decay, value, axis, reverse, stages=(), carry=()):
    count = lax.axis_size(axis)
    heads, size, width = value.shape
    win_value, win_decay = value, decay
    res_value, res_decay = jnp.zeros_like(value), jnp.ones_like(decay)
    step = 1
    turn = 0
    while step < count:
        send = jnp.concatenate(
            [win_value, jnp.broadcast_to(win_decay[:, None, None], (heads, 8, width))], axis=1
        ).astype(jnp.bfloat16)
        if turn < len(stages):
            send, carry = lax.optimization_barrier((send, carry))
        got = shifted(send, axis, -step if reverse else step)
        if turn < len(stages):
            carry = stages[turn](carry)
        got_value = got[:, :size].astype(jnp.float32)
        got_decay = got[:, size, 0].astype(jnp.float32)
        win_value = win_value + win_decay[:, None, None] * got_value
        res_value = res_value + res_decay[:, None, None] * got_value
        win_decay = win_decay * got_decay
        res_decay = res_decay * got_decay
        step *= 2
        turn += 1
    for stage in stages[turn:]:
        carry = stage(carry)
    return res_value, carry


def linear_parts(gates):
    running = jnp.cumsum(gates, axis=1)
    block_total = running[:, -1]
    length = gates.shape[1]
    row_ids = lax.broadcasted_iota(jnp.int32, (length, length), 0)
    col_ids = lax.broadcasted_iota(jnp.int32, (length, length), 1)
    lower = (col_ids <= row_ids)[None]
    spread = jnp.where(lower, running[:, :, None] - running[:, None, :], 0.0)
    window_weight = jnp.where(lower, jnp.exp(spread), 0.0)
    tail_weight = jnp.exp(block_total[:, None] - running)
    return (jnp.exp(running), jnp.exp(block_total), tail_weight, window_weight)


def body(soft_q, soft_k, soft_v, soft_dout, lin_q, lin_k, lin_v, lin_gate, lin_dy):
    heads_here = lin_gate.shape[0]
    length = soft_q.shape[0]
    head_size = soft_q.shape[1] // heads_here
    factor = head_size ** (-0.5)
    position = lax.axis_index("ctx")
    has_prev = position > 0
    has_next = position < lax.axis_size("ctx") - 1
    shape_heads = (length, heads_here, head_size)
    shape_flat = (length, heads_here * head_size)
    row_ids = lax.broadcasted_iota(jnp.int32, (length, length), 0)
    col_ids = lax.broadcasted_iota(jnp.int32, (length, length), 1)
    own_mask = (col_ids <= row_ids)[None]
    prev_mask = ((col_ids > row_ids) & has_prev)[None]
    next_mask = ((col_ids > row_ids) & has_next)[None]

    lin_queries = lin_q.reshape(shape_heads)
    lin_keys = lin_k.reshape(shape_heads)
    lin_values = lin_v.reshape(shape_heads)
    query_f = lin_queries.astype(jnp.float32)
    key_f = lin_keys.astype(jnp.float32)
    value_f = lin_values.astype(jnp.float32)
    lead_weight, block_decay, tail_weight, window_weight = linear_parts(lin_gate)
    summary = jnp.einsum("hs,shd,she->hde", tail_weight, key_f, value_f, precision=exact_mode)

    def cols(array, head):
        return array[:, head * head_size:(head + 1) * head_size]

    def mm(a, b):
        return lax.dot_general(a, b, (((1,), (1,)), ((), ())), preferred_element_type=jnp.float32)

    def mm_t(a, b):
        return lax.dot_general(a, b, (((0,), (0,)), ((), ())), preferred_element_type=jnp.float32)

    def mm_n(a, b):
        return lax.dot_general(a, b, (((1,), (0,)), ((), ())), preferred_element_type=jnp.float32)

    own_mask2 = own_mask[0]
    prev_mask2 = prev_mask[0]
    next_mask2 = next_mask[0]
    heads_list = range(heads_here)

    received = {}

    def soft_sends(c):
        c = dict(c)
        received["prev"] = shifted(jnp.stack((c["soft_k"], c["soft_v"])), "ctx", 1)
        received["next"] = shifted(jnp.stack((c["soft_q"], c["soft_dout"])), "ctx", -1)
        lin_scores = jnp.einsum(
            "thd,shd->hts", c["lin_q"].reshape(shape_heads), c["lin_k"].reshape(shape_heads),
            preferred_element_type=jnp.float32,
        )
        c["attended"] = (lin_scores * factor * c["window_weight"]).astype(jnp.bfloat16)
        c["lin_intra"] = jnp.einsum(
            "hts,she->the", c["attended"], c["lin_v"].reshape(shape_heads),
            preferred_element_type=jnp.float32,
        )
        return c

    def soft_heads(part, last):
        def stage(c):
            c = dict(c)
            keys_prev, values_prev = received["prev"][0], received["prev"][1]
            for h in part:
                scores_own = mm(cols(c["soft_q"], h), cols(c["soft_k"], h)) * factor
                dprob_own = mm(cols(c["soft_dout"], h), cols(c["soft_v"], h))
                scores_prev = mm(cols(c["soft_q"], h), cols(keys_prev, h)) * factor
                row_max = jnp.maximum(
                    jnp.max(jnp.where(own_mask2, scores_own, masked_fill), axis=1),
                    jnp.max(jnp.where(prev_mask2, scores_prev, masked_fill), axis=1),
                )
                total = jnp.sum(
                    jnp.where(own_mask2, jnp.exp(scores_own - row_max[:, None]), 0.0), axis=1
                )
                total = total + jnp.sum(
                    jnp.where(prev_mask2, jnp.exp(scores_prev - row_max[:, None]), 0.0), axis=1
                )
                log_total = row_max + jnp.log(total)
                probs_own = jnp.where(own_mask2, jnp.exp(scores_own - log_total[:, None]), 0.0)
                probs_prev = jnp.where(
                    prev_mask2, jnp.exp(scores_prev - log_total[:, None]), 0.0
                )
                dprob_prev = mm(cols(c["soft_dout"], h), cols(values_prev, h))
                row_delta = jnp.sum(probs_own * dprob_own, axis=1) + jnp.sum(
                    probs_prev * dprob_prev, axis=1
                )
                ds_own = (probs_own * (dprob_own - row_delta[:, None])).astype(jnp.bfloat16)
                ds_prev = (probs_prev * (dprob_prev - row_delta[:, None])).astype(jnp.bfloat16)
                c["stat%d" % h] = jnp.stack((log_total, row_delta))
                c["dq%d" % h] = (
                    mm_n(ds_own, cols(c["soft_k"], h)) + mm_n(ds_prev, cols(keys_prev, h))
                ) * factor
                c["dk%d" % h] = mm_t(ds_own, cols(c["soft_q"], h)) * factor
                c["dv%d" % h] = mm_t(probs_own.astype(jnp.bfloat16), cols(c["soft_dout"], h))
            if last:
                received["stats"] = shifted(
                    jnp.stack([c.pop("stat%d" % h) for h in heads_list], axis=1), "ctx", -1
                )
                c["grad_q"] = jnp.concatenate([c.pop("dq%d" % h) for h in heads_list], axis=1)
                c["grad_k"] = jnp.concatenate([c.pop("dk%d" % h) for h in heads_list], axis=1)
                c["grad_v"] = jnp.concatenate([c.pop("dv%d" % h) for h in heads_list], axis=1)
            return c

        return stage

    split = (heads_here + 1) // 2
    soft_stats = soft_heads(heads_list[:split], False)
    soft_grads = soft_heads(heads_list[split:], True)

    carry = dict(
        soft_q=soft_q, soft_k=soft_k, soft_v=soft_v, soft_dout=soft_dout,
        lin_q=lin_q, lin_k=lin_k, lin_v=lin_v, window_weight=window_weight,
    )
    state_in, carry = exclusive_scan(
        block_decay, summary, "ctx", False, (soft_sends, soft_stats, soft_grads), carry
    )

    lin_output = carry["lin_intra"] + factor * lead_weight.T[:, :, None] * jnp.einsum(
        "thd,hde->the", query_f, state_in, precision=exact_mode
    )
    dy_f = lin_dy.reshape(shape_heads).astype(jnp.float32)
    norm_sums = lax.psum(
        (jnp.sum(lin_output * lin_output, axis=(1, 2)), jnp.sum(lin_output * dy_f, axis=(1, 2))),
        "head",
    )
    width_all = LOCAL_HEADS * HEAD_DIM
    rms_value = jnp.sqrt(norm_sums[0] / width_all + 1e-06)
    lin_grad = (
        dy_f / rms_value[:, None, None]
        - lin_output * (norm_sums[1] / (rms_value**3 * width_all))[:, None, None]
    )
    lin_grad_b = lin_grad.astype(jnp.bfloat16)
    lin_grad_f = lin_grad_b.astype(jnp.float32)
    grad_summary = factor * jnp.einsum(
        "ht,thd,the->hde", lead_weight, query_f, lin_grad_f, precision=exact_mode
    )

    def linear_own(c):
        c = dict(c)
        grad_b = c["lin_grad_b"]
        grad_raw = jnp.einsum(
            "the,she->hts", grad_b, c["lin_v"].reshape(shape_heads),
            preferred_element_type=jnp.float32,
        )
        grad_scores = (grad_raw * factor * c["window_weight"]).astype(jnp.bfloat16)
        lin_grad_q = jnp.einsum(
            "hts,shd->thd", grad_scores, c["lin_k"].reshape(shape_heads),
            preferred_element_type=jnp.float32,
        )
        lin_grad_q = lin_grad_q + factor * c["lead_weight"].T[:, :, None] * jnp.einsum(
            "hde,the->thd", c["state_in"], grad_b.astype(jnp.float32), precision=exact_mode
        )
        c["lin_dq"] = lin_grad_q.astype(jnp.bfloat16).reshape(shape_flat)
        c["lin_dk"] = jnp.einsum(
            "hts,thd->shd", grad_scores, c["lin_q"].reshape(shape_heads),
            preferred_element_type=jnp.float32,
        )
        c["lin_dv"] = jnp.einsum(
            "hts,the->she", c["attended"], grad_b, preferred_element_type=jnp.float32
        )
        for name in ("lin_grad_b", "state_in", "lead_weight", "attended", "window_weight"):
            del c[name]
        return c

    def soft_next_scores(c):
        c = dict(c)
        queries_next, grad_out_next = received["next"][0], received["next"][1]
        stats_next = received["stats"]
        ds_next, p_next = [], []
        for h in heads_list:
            scores_next = mm(cols(queries_next, h), cols(c["soft_k"], h)) * factor
            probs_next = jnp.where(
                next_mask2, jnp.exp(scores_next - stats_next[0, h][:, None]), 0.0
            )
            dprob_next = mm(cols(grad_out_next, h), cols(c["soft_v"], h))
            ds_next.append(
                (probs_next * (dprob_next - stats_next[1, h][:, None])).astype(jnp.bfloat16)
            )
            p_next.append(probs_next.astype(jnp.bfloat16))
        c["dscore_next"] = jnp.concatenate(ds_next, axis=1)
        c["probs_next_b"] = jnp.concatenate(p_next, axis=1)
        return c

    def soft_next_grads(c):
        c = dict(c)
        queries_next, grad_out_next = received["next"][0], received["next"][1]
        dk, dv = [], []
        for h in heads_list:
            part = slice(h * length, (h + 1) * length)
            dk.append(
                cols(c["grad_k"], h)
                + mm_t(c["dscore_next"][:, part], cols(queries_next, h)) * factor
            )
            dv.append(
                cols(c["grad_v"], h) + mm_t(c["probs_next_b"][:, part], cols(grad_out_next, h))
            )
        c["soft_dk"] = jnp.concatenate(dk, axis=1).astype(jnp.bfloat16)
        c["soft_dv"] = jnp.concatenate(dv, axis=1).astype(jnp.bfloat16)
        return c

    late = dict(
        lin_grad_b=lin_grad_b, state_in=state_in, lead_weight=lead_weight,
        attended=carry["attended"], window_weight=window_weight,
        lin_q=lin_q, lin_k=lin_k, lin_v=lin_v,
        soft_k=soft_k, soft_v=soft_v,
        grad_k=carry["grad_k"], grad_v=carry["grad_v"],
    )
    grad_in, late = exclusive_scan(
        block_decay, grad_summary, "ctx", True, (linear_own, soft_next_scores, soft_next_grads),
        late,
    )
    lin_grad_k = late["lin_dk"] + tail_weight.T[:, :, None] * jnp.einsum(
        "hde,she->shd", grad_in, value_f, precision=exact_mode
    )
    lin_grad_v = late["lin_dv"] + tail_weight.T[:, :, None] * jnp.einsum(
        "hde,shd->she", grad_in, key_f, precision=exact_mode
    )
    return (
        carry["grad_q"].astype(jnp.bfloat16),
        late["soft_dk"],
        late["soft_dv"],
        late["lin_dq"],
        lin_grad_k.astype(jnp.bfloat16).reshape(shape_flat),
        lin_grad_v.astype(jnp.bfloat16).reshape(shape_flat),
    )


def solution(mesh):
    in_specs = (
        P("ctx", "head"),
        P("ctx", "head"),
        P("ctx", "head"),
        P("ctx", "head"),
        P("ctx", "head"),
        P("ctx", "head"),
        P("ctx", "head"),
        P("head", "ctx"),
        P("ctx", "head"),
    )
    out_specs = (
        P("ctx", "head"),
        P("ctx", "head"),
        P("ctx", "head"),
        P("ctx", "head"),
        P("ctx", "head"),
        P("ctx", "head"),
    )
    return jax.shard_map(body, mesh=mesh, in_specs=in_specs, out_specs=out_specs, check_vma=False)
```

```python
import jax
import jax.numpy as jnp
from jax import lax
from jax.sharding import PartitionSpec as P

LOCAL_HEADS = 16
HEAD_DIM = 128


masked_fill = -1e30
exact_mode = lax.Precision.HIGHEST


def shifted(x, axis, by):
    peers = lax.axis_size(axis)
    pairs = [(i, i + by) for i in range(peers) if 0 <= i + by < peers]
    return lax.ppermute(x, axis, pairs)


def exclusive_scan(decay, value, axis, reverse, stages=(), carry=()):
    count = lax.axis_size(axis)
    heads, size, width = value.shape
    win_value, win_decay = value, decay
    res_value, res_decay = jnp.zeros_like(value), jnp.ones_like(decay)
    step = 1
    turn = 0
    while step < count:
        send = jnp.concatenate(
            [win_value, jnp.broadcast_to(win_decay[:, None, None], (heads, 8, width))], axis=1
        ).astype(jnp.bfloat16)
        if turn < len(stages):
            send, carry = lax.optimization_barrier((send, carry))
        got = shifted(send, axis, -step if reverse else step)
        if turn < len(stages):
            carry = stages[turn](carry)
        got_value = got[:, :size].astype(jnp.float32)
        got_decay = got[:, size, 0].astype(jnp.float32)
        win_value = win_value + win_decay[:, None, None] * got_value
        res_value = res_value + res_decay[:, None, None] * got_value
        win_decay = win_decay * got_decay
        res_decay = res_decay * got_decay
        step *= 2
        turn += 1
    for stage in stages[turn:]:
        carry = stage(carry)
    return res_value, carry


def linear_parts(gates):
    running = jnp.cumsum(gates, axis=1)
    block_total = running[:, -1]
    length = gates.shape[1]
    row_ids = lax.broadcasted_iota(jnp.int32, (length, length), 0)
    col_ids = lax.broadcasted_iota(jnp.int32, (length, length), 1)
    lower = (col_ids <= row_ids)[None]
    spread = jnp.where(lower, running[:, :, None] - running[:, None, :], 0.0)
    window_weight = jnp.where(lower, jnp.exp(spread), 0.0)
    tail_weight = jnp.exp(block_total[:, None] - running)
    return (jnp.exp(running), jnp.exp(block_total), tail_weight, window_weight)


def body(soft_q, soft_k, soft_v, soft_dout, lin_q, lin_k, lin_v, lin_gate, lin_dy):
    heads_here = lin_gate.shape[0]
    length = soft_q.shape[0]
    head_size = soft_q.shape[1] // heads_here
    factor = head_size ** (-0.5)
    position = lax.axis_index("ctx")
    has_prev = position > 0
    has_next = position < lax.axis_size("ctx") - 1
    shape_heads = (length, heads_here, head_size)
    shape_flat = (length, heads_here * head_size)
    row_ids = lax.broadcasted_iota(jnp.int32, (length, length), 0)
    col_ids = lax.broadcasted_iota(jnp.int32, (length, length), 1)
    own_mask = (col_ids <= row_ids)[None]
    prev_mask = ((col_ids > row_ids) & has_prev)[None]
    next_mask = ((col_ids > row_ids) & has_next)[None]

    lin_queries = lin_q.reshape(shape_heads)
    lin_keys = lin_k.reshape(shape_heads)
    lin_values = lin_v.reshape(shape_heads)
    query_f = lin_queries.astype(jnp.float32)
    key_f = lin_keys.astype(jnp.float32)
    value_f = lin_values.astype(jnp.float32)
    lead_weight, block_decay, tail_weight, window_weight = linear_parts(lin_gate)
    summary = jnp.einsum("hs,shd,she->hde", tail_weight, key_f, value_f, precision=exact_mode)

    def cols(array, head):
        return array[:, head * head_size:(head + 1) * head_size]

    def mm(a, b):
        return lax.dot_general(a, b, (((1,), (1,)), ((), ())), preferred_element_type=jnp.float32)

    def mm_t(a, b):
        return lax.dot_general(a, b, (((0,), (0,)), ((), ())), preferred_element_type=jnp.float32)

    def mm_n(a, b):
        return lax.dot_general(a, b, (((1,), (0,)), ((), ())), preferred_element_type=jnp.float32)

    own_mask2 = own_mask[0]
    prev_mask2 = prev_mask[0]
    next_mask2 = next_mask[0]
    heads_list = range(heads_here)

    received = {}

    def soft_sends(c):
        c = dict(c)
        received["prev"] = shifted(jnp.stack((c["soft_k"], c["soft_v"])), "ctx", 1)
        received["next"] = shifted(jnp.stack((c["soft_q"], c["soft_dout"])), "ctx", -1)
        lin_scores = jnp.einsum(
            "thd,shd->hts", c["lin_q"].reshape(shape_heads), c["lin_k"].reshape(shape_heads),
            preferred_element_type=jnp.float32,
        )
        c["attended"] = (lin_scores * factor * c["window_weight"]).astype(jnp.bfloat16)
        c["lin_intra"] = jnp.einsum(
            "hts,she->the", c["attended"], c["lin_v"].reshape(shape_heads),
            preferred_element_type=jnp.float32,
        )
        return c

    def soft_heads(part, last):
        def stage(c):
            c = dict(c)
            keys_prev, values_prev = received["prev"][0], received["prev"][1]
            for h in part:
                scores_own = mm(cols(c["soft_q"], h), cols(c["soft_k"], h)) * factor
                dprob_own = mm(cols(c["soft_dout"], h), cols(c["soft_v"], h))
                scores_prev = mm(cols(c["soft_q"], h), cols(keys_prev, h)) * factor
                row_max = jnp.maximum(
                    jnp.max(jnp.where(own_mask2, scores_own, masked_fill), axis=1),
                    jnp.max(jnp.where(prev_mask2, scores_prev, masked_fill), axis=1),
                )
                total = jnp.sum(
                    jnp.where(own_mask2, jnp.exp(scores_own - row_max[:, None]), 0.0), axis=1
                )
                total = total + jnp.sum(
                    jnp.where(prev_mask2, jnp.exp(scores_prev - row_max[:, None]), 0.0), axis=1
                )
                log_total = row_max + jnp.log(total)
                probs_own = jnp.where(own_mask2, jnp.exp(scores_own - log_total[:, None]), 0.0)
                probs_prev = jnp.where(
                    prev_mask2, jnp.exp(scores_prev - log_total[:, None]), 0.0
                )
                dprob_prev = mm(cols(c["soft_dout"], h), cols(values_prev, h))
                row_delta = jnp.sum(probs_own * dprob_own, axis=1) + jnp.sum(
                    probs_prev * dprob_prev, axis=1
                )
                ds_own = (probs_own * (dprob_own - row_delta[:, None])).astype(jnp.bfloat16)
                ds_prev = (probs_prev * (dprob_prev - row_delta[:, None])).astype(jnp.bfloat16)
                c["stat%d" % h] = jnp.stack((log_total, row_delta))
                c["dq%d" % h] = (
                    mm_n(ds_own, cols(c["soft_k"], h)) + mm_n(ds_prev, cols(keys_prev, h))
                ) * factor
                c["dk%d" % h] = mm_t(ds_own, cols(c["soft_q"], h)) * factor
                c["dv%d" % h] = mm_t(probs_own.astype(jnp.bfloat16), cols(c["soft_dout"], h))
            c["stat_g"] = c.get("stat_g", []) + [
                jnp.stack([c.pop("stat%d" % h) for h in part], axis=1)
            ]
            for kind in ("dq", "dk", "dv"):
                c[kind + "_g"] = c.get(kind + "_g", []) + [
                    jnp.concatenate([c.pop(kind + "%d" % h) for h in part], axis=1)
                ]
            if last:
                received["stats"] = shifted(
                    jnp.concatenate(c.pop("stat_g"), axis=1), "ctx", -1
                )
                c["grad_q"] = jnp.concatenate(c.pop("dq_g"), axis=1)
                c["grad_k"] = jnp.concatenate(c.pop("dk_g"), axis=1)
                c["grad_v"] = jnp.concatenate(c.pop("dv_g"), axis=1)
            return c

        return stage

    split = (heads_here + 1) // 2
    soft_stats = soft_heads(heads_list[:split], False)
    soft_grads = soft_heads(heads_list[split:], True)

    carry = dict(
        soft_q=soft_q, soft_k=soft_k, soft_v=soft_v, soft_dout=soft_dout,
        lin_q=lin_q, lin_k=lin_k, lin_v=lin_v, window_weight=window_weight,
    )
    state_in, carry = exclusive_scan(
        block_decay, summary, "ctx", False, (soft_sends, soft_stats, soft_grads), carry
    )

    lin_output = carry["lin_intra"] + factor * lead_weight.T[:, :, None] * jnp.einsum(
        "thd,hde->the", query_f, state_in, precision=exact_mode
    )
    dy_f = lin_dy.reshape(shape_heads).astype(jnp.float32)
    norm_sums = lax.psum(
        (jnp.sum(lin_output * lin_output, axis=(1, 2)), jnp.sum(lin_output * dy_f, axis=(1, 2))),
        "head",
    )
    width_all = LOCAL_HEADS * HEAD_DIM
    rms_value = jnp.sqrt(norm_sums[0] / width_all + 1e-06)
    lin_grad = (
        dy_f / rms_value[:, None, None]
        - lin_output * (norm_sums[1] / (rms_value**3 * width_all))[:, None, None]
    )
    lin_grad_b = lin_grad.astype(jnp.bfloat16)
    lin_grad_f = lin_grad_b.astype(jnp.float32)
    grad_summary = factor * jnp.einsum(
        "ht,thd,the->hde", lead_weight, query_f, lin_grad_f, precision=exact_mode
    )

    def linear_own(c):
        c = dict(c)
        grad_b = c["lin_grad_b"]
        grad_raw = jnp.einsum(
            "the,she->hts", grad_b, c["lin_v"].reshape(shape_heads),
            preferred_element_type=jnp.float32,
        )
        grad_scores = (grad_raw * factor * c["window_weight"]).astype(jnp.bfloat16)
        lin_grad_q = jnp.einsum(
            "hts,shd->thd", grad_scores, c["lin_k"].reshape(shape_heads),
            preferred_element_type=jnp.float32,
        )
        lin_grad_q = lin_grad_q + factor * c["lead_weight"].T[:, :, None] * jnp.einsum(
            "hde,the->thd", c["state_in"], grad_b.astype(jnp.float32), precision=exact_mode
        )
        c["lin_dq"] = lin_grad_q.astype(jnp.bfloat16).reshape(shape_flat)
        c["lin_dk"] = jnp.einsum(
            "hts,thd->shd", grad_scores, c["lin_q"].reshape(shape_heads),
            preferred_element_type=jnp.float32,
        )
        c["lin_dv"] = jnp.einsum(
            "hts,the->she", c["attended"], grad_b, preferred_element_type=jnp.float32
        )
        for name in ("lin_grad_b", "state_in", "lead_weight", "attended", "window_weight"):
            del c[name]
        return c

    def soft_next_scores(c):
        c = dict(c)
        queries_next, grad_out_next = received["next"][0], received["next"][1]
        stats_next = received["stats"]
        ds_next, p_next = [], []
        for h in heads_list:
            scores_next = mm(cols(queries_next, h), cols(c["soft_k"], h)) * factor
            probs_next = jnp.where(
                next_mask2, jnp.exp(scores_next - stats_next[0, h][:, None]), 0.0
            )
            dprob_next = mm(cols(grad_out_next, h), cols(c["soft_v"], h))
            ds_next.append(
                (probs_next * (dprob_next - stats_next[1, h][:, None])).astype(jnp.bfloat16)
            )
            p_next.append(probs_next.astype(jnp.bfloat16))
        c["dscore_next"], c["probs_next_b"] = ds_next, p_next
        return c

    def soft_next_grads(c):
        c = dict(c)
        queries_next, grad_out_next = received["next"][0], received["next"][1]
        dk, dv = [], []
        for h in heads_list:
            dk.append(
                cols(c["grad_k"], h) + mm_t(c["dscore_next"][h], cols(queries_next, h)) * factor
            )
            dv.append(
                cols(c["grad_v"], h) + mm_t(c["probs_next_b"][h], cols(grad_out_next, h))
            )
        c["soft_dk"] = jnp.concatenate(dk, axis=1).astype(jnp.bfloat16)
        c["soft_dv"] = jnp.concatenate(dv, axis=1).astype(jnp.bfloat16)
        return c

    late = dict(
        lin_grad_b=lin_grad_b, state_in=state_in, lead_weight=lead_weight,
        attended=carry["attended"], window_weight=window_weight,
        lin_q=lin_q, lin_k=lin_k, lin_v=lin_v,
        soft_k=soft_k, soft_v=soft_v,
        grad_k=carry["grad_k"], grad_v=carry["grad_v"],
    )
    grad_in, late = exclusive_scan(
        block_decay, grad_summary, "ctx", True, (linear_own, soft_next_scores, soft_next_grads),
        late,
    )
    lin_grad_k = late["lin_dk"] + tail_weight.T[:, :, None] * jnp.einsum(
        "hde,she->shd", grad_in, value_f, precision=exact_mode
    )
    lin_grad_v = late["lin_dv"] + tail_weight.T[:, :, None] * jnp.einsum(
        "hde,shd->she", grad_in, key_f, precision=exact_mode
    )
    return (
        carry["grad_q"].astype(jnp.bfloat16),
        late["soft_dk"],
        late["soft_dv"],
        late["lin_dq"],
        lin_grad_k.astype(jnp.bfloat16).reshape(shape_flat),
        lin_grad_v.astype(jnp.bfloat16).reshape(shape_flat),
    )


def solution(mesh):
    in_specs = (
        P("ctx", "head"),
        P("ctx", "head"),
        P("ctx", "head"),
        P("ctx", "head"),
        P("ctx", "head"),
        P("ctx", "head"),
        P("ctx", "head"),
        P("head", "ctx"),
        P("ctx", "head"),
    )
    out_specs = (
        P("ctx", "head"),
        P("ctx", "head"),
        P("ctx", "head"),
        P("ctx", "head"),
        P("ctx", "head"),
        P("ctx", "head"),
    )
    return jax.shard_map(body, mesh=mesh, in_specs=in_specs, out_specs=out_specs, check_vma=False)
```
